32 devices in a mesh: wide: 8 (over z, x), narrow: 4 (over y, core).
Axes of the slice: x: 2, y: 2, z: 4, core: 2. Of those that a mesh axis runs over, the one named last changes fastest.
Arguments:
- start_block: float32 [4096, 256], P(('wide', 'narrow'))
- jacobian: float32 [4096, 5, 4096], P(('wide', 'narrow')), may hold values from -0.3125 to 0.3125
- counts: int32 [32], P(('wide', 'narrow')), may hold values from 2 to 128, as said below
- columns: int32 [4096, 5], P(('wide', 'narrow')), may hold values from 0 to 255, as said below
- send_list: int32 [32, 4, 32], P(('wide', 'narrow')), may hold values from 0 to 127, as said below
Outputs:
- correction: float32 [4096, 256], P(('wide', 'narrow'))
- residual: float32 [4096, 256], P(('wide', 'narrow'))
The draws below stay inside these ranges and needn't reach their ends.
Inputs may be any that keep to these rules, and one draw needn't show every extreme that they name: `counts`: one device has exactly 128 live elements in every draw; the loads are uneven. columns[e, 0] is the element's own slot; a value below 128 in columns[e, 1:] is below the device's count, a larger one is a ghost slot of one of the four neighbour directions. `send_list`: every entry is below the count of the device that lends it; lists may repeat elements.
All inputs are finite; a program needn't handle non-finite values.
Results may differ from the reference program's by a relative error of at most 0.0003.
Values sent between devices are 32-bit elements; how exact they have to be, the bound alone decides.
No kernel may reach another device: no remote copies, remote signals or barrier semaphores. Data moves between devices by JAX's collectives and lax.ppermute only.
A program may use at most 128 MiB of HBM per device.

```python
import jax
import jax.numpy as jnp
from jax import lax

BLK = 64
VECS = 4
NB = 5
E_DEV = 128
GHOST = 32
ELEMS = 4096
N_WIDE = 8
N_NARROW = 4
DEVICES = 32


def shared_counts(key):
    base_key = jax.random.fold_in(key, 101)
    key_levels, key_jitter, key_fullest = jax.random.split(base_key, 3)
    levels = jax.random.randint(key_levels, (DEVICES,), 0, 4)
    jitter = jax.random.randint(key_jitter, (DEVICES,), 0, max(E_DEV // 16, 1))
    row_counts = jnp.maximum(jnp.right_shift(jnp.int32(E_DEV), levels.astype(jnp.int32)) - jitter, 2)
    fullest = jax.random.randint(key_fullest, (), 0, DEVICES)
    return jnp.where(jnp.arange(DEVICES) == fullest, E_DEV, row_counts).astype(jnp.int32)


def draw_counts(key, part):
    return shared_counts(key)


def draw_columns(key, part):
    row_counts = shared_counts(key)
    base_key = jax.random.fold_in(key, 202)
    key_local, key_flag = jax.random.split(base_key, 2)
    row_ids = jnp.arange(ELEMS, dtype=jnp.int32)
    owner = row_ids // E_DEV
    own_slot = row_ids % E_DEV
    limit = row_counts[owner]
    local_pick = jax.random.randint(key_local, (ELEMS, NB - 1), 0, limit[:, None])
    remote_flag = jax.random.randint(key_flag, (ELEMS, NB - 1), 0, 4) == 0
    face_ids = jnp.arange(NB - 1, dtype=jnp.int32)
    forced = (own_slot[:, None] == E_DEV - 1) & (face_ids[None, :] == NB - 2)
    remote_flag = remote_flag | forced
    ghost_slot = E_DEV + face_ids[None, :] * GHOST + own_slot[:, None] % GHOST
    faces = jnp.where(remote_flag, ghost_slot, local_pick)
    return jnp.concatenate([own_slot[:, None], faces], 1).astype(jnp.int32)


def draw_send_list(key, part):
    row_counts = shared_counts(key)
    base_key = jax.random.fold_in(key, 303)
    picks = jax.random.randint(base_key, (DEVICES, 4, GHOST), 0, row_counts[:, None, None])
    first_slot = jnp.arange(GHOST, dtype=jnp.int32)[None, None, :] == 0
    full_device = (row_counts == E_DEV)[:, None, None]
    picks = jnp.where(first_slot & full_device, E_DEV - 1, picks)
    return picks.astype(jnp.int32)


def draw_start_block(key, part):
    base_key = jax.random.fold_in(key, 404)
    key_rows, key_vectors, key_main = jax.random.split(base_key, 3)
    row_ids = jnp.arange(ELEMS, dtype=jnp.int32)
    owner = (row_ids // E_DEV).astype(jnp.float32)
    ramp = 1.0 + 2.0 * owner / max(DEVICES - 1, 1)
    row_scale = 10.0 ** jax.random.uniform(key_rows, (ELEMS, 1), jnp.float32)
    vector_scale = jnp.repeat(10.0 ** jax.random.uniform(key_vectors, (VECS,), jnp.float32), BLK)[None, :]
    entries = jnp.clip(jax.random.normal(key_main, (ELEMS, VECS * BLK), jnp.float32), -4.0, 4.0)
    return (entries * row_scale * vector_scale * ramp[:, None] / 6.0).astype(jnp.float32)


def block_levels(own_key, dims, cuts, smallest, top_value):
    loudness = 1.0
    for position, blocks in cuts:
        steps = jax.random.uniform(jax.random.fold_in(jax.random.fold_in(own_key, 6), position), (blocks,), jnp.float32, smallest / len(cuts), top_value / len(cuts))
        loudness = loudness * jnp.repeat(jnp.exp(steps), dims[position] // blocks).reshape((-1,) + (1,) * (len(dims) - 1 - position))
    return loudness


def noise(key, dims, width, most, cuts=(), held_as=jnp.bfloat16):
    values = jax.random.normal(key, dims, jnp.float32) * width
    if len(cuts) > 0:
        values = block_levels(key, dims, cuts, -0.22, 0.18) * values
    return jnp.clip(values, min=-most, max=most).astype(held_as)


def setup_inputs(seed: int = 0) -> dict:
    key_list = jax.random.split(jax.random.key(seed), 6)
    return {
        "start_block": draw_start_block(jax.random.fold_in(key_list[5], 71), 0),
        "jacobian": noise(key_list[1], (ELEMS, NB, BLK * BLK), (BLK * NB) ** -0.5, 0.3125, ((0, 32),), jnp.float32),
        "counts": draw_counts(jax.random.fold_in(key_list[5], 71), 0),
        "columns": draw_columns(jax.random.fold_in(key_list[5], 71), 0),
        "send_list": draw_send_list(jax.random.fold_in(key_list[5], 71), 0),
    }


DIAG_SHIFT = 1.5

def linked_rows(columns, send_list):
    device_ids = jnp.arange(DEVICES, dtype=jnp.int32)
    wide_pos = device_ids // N_NARROW
    narrow_pos = device_ids % N_NARROW
    wide_near = jnp.stack([wide_pos - 1, wide_pos + 1, wide_pos, wide_pos], 1)
    narrow_near = jnp.stack([narrow_pos, narrow_pos, narrow_pos - 1, narrow_pos + 1], 1)
    inside = (wide_near >= 0) & (wide_near < N_WIDE) & (narrow_near >= 0) & (narrow_near < N_NARROW)
    lender = (jnp.clip(wide_near, 0, N_WIDE - 1) * N_NARROW + jnp.clip(narrow_near, 0, N_NARROW - 1)).astype(jnp.int32)
    quarter = jnp.arange(4, dtype=jnp.int32)
    lent = send_list[lender, quarter[None, :], :]
    remote_rows = jnp.where(inside[:, :, None], lender[:, :, None] * E_DEV + lent, ELEMS).astype(jnp.int32)
    remote_flat = remote_rows.reshape(DEVICES, 4 * GHOST)
    row_ids = jnp.arange(ELEMS, dtype=jnp.int32)
    owner = row_ids // E_DEV
    near_rows = owner[:, None] * E_DEV + columns
    offset = jnp.clip(columns - E_DEV, 0, 4 * GHOST - 1).astype(jnp.int32)
    far_rows = remote_flat[owner[:, None], offset]
    return jnp.where(columns < E_DEV, near_rows, far_rows).astype(jnp.int32)

def apply_operator(values, jacobian, linked, living):
    padded = jnp.concatenate([values, jnp.zeros((1, VECS * BLK), jnp.float32)], 0)

    def one_device(pieces):
        matrices, targets = pieces
        picked = padded[targets].reshape(E_DEV, NB, VECS, BLK)
        square = matrices.reshape(E_DEV, NB, BLK, BLK)
        summed = jnp.einsum('ekij,ekcj->eci', square, picked, precision=lax.Precision.HIGHEST)
        return summed.reshape(E_DEV, VECS * BLK)
    coupled = lax.map(one_device, (jacobian.reshape(DEVICES, E_DEV, NB, BLK * BLK), linked.reshape(DEVICES, E_DEV, NB)))
    summed = DIAG_SHIFT * values + coupled.reshape(ELEMS, VECS * BLK)
    return jnp.where(living, summed, jnp.float32(0.0))

def combine(values, mixing):
    shaped = values.reshape(ELEMS, VECS, BLK)
    return jnp.einsum('eci,cd->edi', shaped, mixing, precision=lax.Precision.HIGHEST).reshape(ELEMS, VECS * BLK)

def reference(start_block, jacobian, counts, columns, send_list):
    row_ids = jnp.arange(ELEMS, dtype=jnp.int32)
    living = (row_ids % E_DEV < counts[row_ids // E_DEV])[:, None]
    anchor = jnp.where(living, start_block, jnp.float32(0.0))
    linked = linked_rows(columns, send_list)
    first_image = apply_operator(anchor, jacobian, linked, living)
    second_image = apply_operator(first_image, jacobian, linked, living)
    basis = jnp.concatenate([anchor.reshape(ELEMS, VECS, BLK), first_image.reshape(ELEMS, VECS, BLK), second_image.reshape(ELEMS, VECS, BLK)], 1)
    gram_full = jnp.einsum('eai,ebi->ab', basis, basis, precision=lax.Precision.HIGHEST)
    normal_matrix = gram_full[VECS:, VECS:]
    right_terms = gram_full[VECS:, :VECS]
    factor = jnp.linalg.cholesky(normal_matrix)
    coefficients = jax.scipy.linalg.cho_solve((factor, True), right_terms)
    correction = combine(anchor, coefficients[:VECS]) + combine(first_image, coefficients[VECS:])
    residual = anchor - (combine(first_image, coefficients[:VECS]) + combine(second_image, coefficients[VECS:]))
    return (correction, residual)
```

```python
import jax
import jax.numpy as jnp
from jax import lax
from jax.experimental import pallas as pl
from jax.experimental.pallas import tpu as pltpu
from jax.sharding import PartitionSpec as P

BLK = 64
VECS = 4
NB = 5
E_DEV = 128
LANES = 128
ROWS_PER_STEP = 32


DIAG_SHIFT = 1.5


def padded(cells, sides, width):
    for axis, dim in sides:
        count = lax.axis_size(axis)
        ends = count - 1
        head = lax.slice_in_dim(cells, 0, width, axis=dim)
        tail = lax.slice_in_dim(cells, cells.shape[dim] - width, cells.shape[dim], axis=dim)
        cells = jnp.concatenate(
            [
                lax.ppermute(tail, axis, [(i, (i + 1) % count) for i in range(ends)]),
                cells,
                lax.ppermute(head, axis, [((i + 1) % count, i) for i in range(ends)]),
            ],
            axis=dim,
        )
    return cells


def combine(values, mixing):
    shaped = values.reshape(values.shape[0], VECS, BLK)
    return jnp.einsum("eci,cd->edi", shaped, mixing, precision=lax.Precision.HIGHEST).reshape(
        values.shape[0], VECS * BLK
    )


def inner_block(left_side, right_side):
    left_shaped = left_side.reshape(left_side.shape[0], VECS, BLK)
    right_shaped = right_side.reshape(right_side.shape[0], VECS, BLK)
    return jnp.einsum("eci,edi->cd", left_shaped, right_shaped, precision=lax.Precision.HIGHEST)


def tree_sum(values, axes):
    for axis in axes:
        count = lax.axis_size(axis)
        if count & (count - 1):
            values = lax.psum(values, axis)
            continue
        stride = 1
        while stride < count:
            values = values + lax.ppermute(values, axis, [(i, i ^ stride) for i in range(count)])
            stride *= 2
    return values


def coupling_kernel(jac_ref, picked_ref, seg_ref, out_ref, parts_ref):
    step = pl.program_id(0)
    rows = jac_ref.shape[1]
    tiles = jac_ref.shape[2] // LANES
    row0 = pl.multiple_of(step * rows, rows)

    def one_tile(t, carry):
        off = pl.multiple_of(t * LANES, LANES)
        blocks = [jac_ref[k, :, pl.ds(off, LANES)] for k in range(NB)]
        for c in range(VECS):
            total = blocks[0] * picked_ref[0, :, c * LANES:(c + 1) * LANES]
            for k in range(1, NB):
                total = total + blocks[k] * picked_ref[k, :, c * LANES:(c + 1) * LANES]
            high = total.astype(jnp.bfloat16)
            low = (total - high.astype(jnp.float32)).astype(jnp.bfloat16)
            parts_ref[2 * c, pl.ds(row0, rows), pl.ds(off, LANES)] = high
            parts_ref[2 * c + 1, pl.ds(row0, rows), pl.ds(off, LANES)] = low
        return carry

    lax.fori_loop(0, tiles, one_tile, 0)

    @pl.when(step == pl.num_programs(0) - 1)
    def _():
        count = parts_ref.shape[1]
        flat = parts_ref[...].reshape(2 * VECS * count, tiles * LANES)
        sums = jnp.dot(flat, seg_ref[...], preferred_element_type=jnp.float32)
        for c in range(VECS):
            high = sums[(2 * c) * count:(2 * c + 1) * count]
            low = sums[(2 * c + 1) * count:(2 * c + 2) * count]
            out_ref[:, c * BLK:(c + 1) * BLK] = high + low


def coupled_sum(jac_t, picked, seg):
    blocks, count, width = jac_t.shape
    rows = min(ROWS_PER_STEP, count)
    return pl.pallas_call(
        coupling_kernel,
        out_shape=jax.ShapeDtypeStruct((count, VECS * BLK), jnp.float32),
        grid=(count // rows,),
        in_specs=[
            pl.BlockSpec((blocks, rows, width), lambda b: (0, b, 0)),
            pl.BlockSpec((blocks, rows, VECS * LANES), lambda b: (0, b, 0)),
            pl.BlockSpec((width, BLK), lambda b: (0, 0)),
        ],
        out_specs=pl.BlockSpec((count, VECS * BLK), lambda b: (0, 0)),
        scratch_shapes=[pltpu.VMEM((2 * VECS, count, width), jnp.bfloat16)],
        compiler_params=pltpu.CompilerParams(dimension_semantics=("arbitrary",)),
        cost_estimate=pl.CostEstimate(
            flops=2 * blocks * count * width * VECS + 2 * 2 * VECS * count * width * BLK,
            bytes_accessed=4 * (blocks * count * width + blocks * count * VECS * LANES + count * VECS * BLK),
            transcendentals=0,
        ),
    )(jac_t, picked, seg)


def per_device(start_block, jacobian, counts, columns, send_list):
    living = (lax.iota(jnp.int32, E_DEV) < counts[0])[:, None]
    anchor = jnp.where(living, start_block, jnp.float32(0.0))
    lend_rows = send_list[0]
    jac_t = jnp.transpose(jacobian, (1, 0, 2))
    lane = lax.broadcasted_iota(jnp.int32, (BLK * BLK, BLK), 0)
    col = lax.broadcasted_iota(jnp.int32, (BLK * BLK, BLK), 1)
    seg = (lane // BLK == col).astype(jnp.bfloat16)

    def ghosts(values):
        outgoing = values[lend_rows]
        wide_in = padded(jnp.stack([outgoing[1], outgoing[0]]), (("wide", 0),), 1)
        narrow_in = padded(jnp.stack([outgoing[3], outgoing[2]]), (("narrow", 0),), 1)
        return jnp.concatenate([wide_in[0], wide_in[3], narrow_in[0], narrow_in[3]], 0)

    def operate(values):
        ghost_rows = ghosts(values)
        source = jnp.concatenate([values, ghost_rows], 0)
        picked = source[columns].reshape(E_DEV, NB, VECS, 1, BLK)
        picked = jnp.broadcast_to(picked, (E_DEV, NB, VECS, 2, BLK)).reshape(E_DEV, NB, VECS * LANES)
        picked = jnp.transpose(picked, (1, 0, 2))
        summed = coupled_sum(jac_t, picked, seg)
        return jnp.where(living, DIAG_SHIFT * values + summed, jnp.float32(0.0))

    first_image = operate(anchor)
    second_image = operate(first_image)
    blocks = (
        inner_block(first_image, anchor),
        inner_block(first_image, first_image),
        inner_block(second_image, anchor),
        inner_block(second_image, first_image),
        inner_block(second_image, second_image),
    )
    gram_parts = tree_sum(jnp.stack(blocks), ("narrow", "wide"))
    normal_matrix = jnp.concatenate(
        [
            jnp.concatenate([gram_parts[1], gram_parts[3].T], 1),
            jnp.concatenate([gram_parts[3], gram_parts[4]], 1),
        ],
        0,
    )
    right_terms = jnp.concatenate([gram_parts[0], gram_parts[2]], 0)
    factor = jnp.linalg.cholesky(normal_matrix)
    coefficients = jax.scipy.linalg.cho_solve((factor, True), right_terms)
    correction = combine(anchor, coefficients[:VECS]) + combine(first_image, coefficients[VECS:])
    residual = anchor - (
        combine(first_image, coefficients[:VECS]) + combine(second_image, coefficients[VECS:])
    )
    return (correction, residual)


def solution(mesh):
    placed = (
        P(("wide", "narrow"), None),
        P(("wide", "narrow"), None, None),
        P(("wide", "narrow")),
        P(("wide", "narrow"), None),
        P(("wide", "narrow"), None, None),
    )
    return jax.shard_map(
        per_device,
        mesh=mesh,
        in_specs=placed,
        out_specs=(P(("wide", "narrow"), None), P(("wide", "narrow"), None)),
        check_vma=False,
    )
```

```python
import jax
import jax.numpy as jnp
from jax import lax
from jax.experimental import pallas as pl
from jax.experimental.pallas import tpu as pltpu
from jax.sharding import PartitionSpec as P

BLK = 64
VECS = 4
NB = 5
E_DEV = 128
LANES = 128
ROWS_PER_STEP = 32


DIAG_SHIFT = 1.5


def padded(cells, sides, width):
    for axis, dim in sides:
        count = lax.axis_size(axis)
        ends = count - 1
        head = lax.slice_in_dim(cells, 0, width, axis=dim)
        tail = lax.slice_in_dim(cells, cells.shape[dim] - width, cells.shape[dim], axis=dim)
        cells = jnp.concatenate(
            [
                lax.ppermute(tail, axis, [(i, (i + 1) % count) for i in range(ends)]),
                cells,
                lax.ppermute(head, axis, [((i + 1) % count, i) for i in range(ends)]),
            ],
            axis=dim,
        )
    return cells


def combine(values, mixing):
    shaped = values.reshape(values.shape[0], VECS, BLK)
    return jnp.einsum("eci,cd->edi", shaped, mixing, precision=lax.Precision.HIGHEST).reshape(
        values.shape[0], VECS * BLK
    )


def inner_block(left_side, right_side):
    left_shaped = left_side.reshape(left_side.shape[0], VECS, BLK)
    right_shaped = right_side.reshape(right_side.shape[0], VECS, BLK)
    return jnp.einsum("eci,edi->cd", left_shaped, right_shaped, precision=lax.Precision.HIGHEST)


def tree_sum(values, axes):
    for axis in axes:
        count = lax.axis_size(axis)
        if count & (count - 1):
            values = lax.psum(values, axis)
            continue
        stride = 1
        while stride < count:
            values = values + lax.ppermute(values, axis, [(i, i ^ stride) for i in range(count)])
            stride *= 2
    return values


def coupling_kernel(jac_ref, picked_ref, out_ref, parts_ref, doubled_ref):
    step = pl.program_id(0)
    rows = jac_ref.shape[1]
    tiles = jac_ref.shape[2] // LANES
    row0 = pl.multiple_of(step * rows, rows)
    lane = lax.broadcasted_iota(jnp.int32, (rows, LANES), 1)
    for k in range(NB):
        for pair in range(VECS // 2):
            tile = picked_ref[k, :, pair * LANES:(pair + 1) * LANES]
            swapped = pltpu.roll(tile, BLK, 1)
            doubled_ref[k, :, (2 * pair) * LANES:(2 * pair + 1) * LANES] = jnp.where(lane < BLK, tile, swapped)
            doubled_ref[k, :, (2 * pair + 1) * LANES:(2 * pair + 2) * LANES] = jnp.where(lane >= BLK, tile, swapped)

    def one_tile(t, carry):
        off = pl.multiple_of(t * LANES, LANES)
        blocks = [jac_ref[k, :, pl.ds(off, LANES)] for k in range(NB)]
        for c in range(VECS):
            total = blocks[0] * doubled_ref[0, :, c * LANES:(c + 1) * LANES]
            for k in range(1, NB):
                total = total + blocks[k] * doubled_ref[k, :, c * LANES:(c + 1) * LANES]
            high = total.astype(jnp.bfloat16)
            low = (total - high.astype(jnp.float32)).astype(jnp.bfloat16)
            parts_ref[2 * c, pl.ds(row0, rows), pl.ds(off, LANES)] = high
            parts_ref[2 * c + 1, pl.ds(row0, rows), pl.ds(off, LANES)] = low
        return carry

    lax.fori_loop(0, tiles, one_tile, 0)

    @pl.when(step == pl.num_programs(0) - 1)
    def _():
        count = parts_ref.shape[1]
        flat = parts_ref[...].reshape(2 * VECS * count, tiles * LANES)
        width = tiles * LANES
        seg = (
            lax.broadcasted_iota(jnp.int32, (width, BLK), 0) // BLK
            == lax.broadcasted_iota(jnp.int32, (width, BLK), 1)
        ).astype(jnp.bfloat16)
        sums = jnp.dot(flat, seg, preferred_element_type=jnp.float32)
        for c in range(VECS):
            high = sums[(2 * c) * count:(2 * c + 1) * count]
            low = sums[(2 * c + 1) * count:(2 * c + 2) * count]
            out_ref[:, c * BLK:(c + 1) * BLK] = high + low


def coupled_sum(jac_t, picked):
    blocks, count, width = jac_t.shape
    rows = min(ROWS_PER_STEP, count)
    return pl.pallas_call(
        coupling_kernel,
        out_shape=jax.ShapeDtypeStruct((count, VECS * BLK), jnp.float32),
        grid=(count // rows,),
        in_specs=[
            pl.BlockSpec((blocks, rows, width), lambda b: (0, b, 0)),
            pl.BlockSpec((blocks, rows, VECS * BLK), lambda b: (0, b, 0)),
        ],
        out_specs=pl.BlockSpec((count, VECS * BLK), lambda b: (0, 0)),
        scratch_shapes=[
            pltpu.VMEM((2 * VECS, count, width), jnp.bfloat16),
            pltpu.VMEM((blocks, rows, VECS * LANES), jnp.float32),
        ],
        compiler_params=pltpu.CompilerParams(dimension_semantics=("arbitrary",)),
        cost_estimate=pl.CostEstimate(
            flops=2 * blocks * count * width * VECS + 2 * 2 * VECS * count * width * BLK,
            bytes_accessed=4 * (blocks * count * width + blocks * count * VECS * BLK + count * VECS * BLK),
            transcendentals=0,
        ),
    )(jac_t, picked)


def per_device(start_block, jacobian, counts, columns, send_list):
    living = (lax.iota(jnp.int32, E_DEV) < counts[0])[:, None]
    anchor = jnp.where(living, start_block, jnp.float32(0.0))
    lend_rows = send_list[0]
    jac_t = jnp.transpose(jacobian, (1, 0, 2))
    gather_rows = jnp.transpose(columns, (1, 0))

    def ghosts(values):
        outgoing = values[lend_rows]
        wide_in = padded(jnp.stack([outgoing[1], outgoing[0]]), (("wide", 0),), 1)
        narrow_in = padded(jnp.stack([outgoing[3], outgoing[2]]), (("narrow", 0),), 1)
        return jnp.concatenate([wide_in[0], wide_in[3], narrow_in[0], narrow_in[3]], 0)

    def operate(values):
        ghost_rows = ghosts(values)
        source = jnp.concatenate([values, ghost_rows], 0)
        picked = source[gather_rows]
        summed = coupled_sum(jac_t, picked)
        return jnp.where(living, DIAG_SHIFT * values + summed, jnp.float32(0.0))

    first_image = operate(anchor)
    second_image = operate(first_image)
    blocks = (
        inner_block(first_image, anchor),
        inner_block(first_image, first_image),
        inner_block(second_image, anchor),
        inner_block(second_image, first_image),
        inner_block(second_image, second_image),
    )
    gram_parts = tree_sum(jnp.stack(blocks), ("narrow", "wide"))
    normal_matrix = jnp.concatenate(
        [
            jnp.concatenate([gram_parts[1], gram_parts[3].T], 1),
            jnp.concatenate([gram_parts[3], gram_parts[4]], 1),
        ],
        0,
    )
    right_terms = jnp.concatenate([gram_parts[0], gram_parts[2]], 0)
    factor = jnp.linalg.cholesky(normal_matrix)
    coefficients = jax.scipy.linalg.cho_solve((factor, True), right_terms)
    correction = combine(anchor, coefficients[:VECS]) + combine(first_image, coefficients[VECS:])
    residual = anchor - (
        combine(first_image, coefficients[:VECS]) + combine(second_image, coefficients[VECS:])
    )
    return (correction, residual)


def solution(mesh):
    placed = (
        P(("wide", "narrow"), None),
        P(("wide", "narrow"), None, None),
        P(("wide", "narrow")),
        P(("wide", "narrow"), None),
        P(("wide", "narrow"), None, None),
    )
    return jax.shard_map(
        per_device,
        mesh=mesh,
        in_specs=placed,
        out_specs=(P(("wide", "narrow"), None), P(("wide", "narrow"), None)),
        check_vma=False,
    )
```

```python
import jax
import jax.numpy as jnp
from jax import lax
from jax.experimental import pallas as pl
from jax.experimental.pallas import tpu as pltpu
from jax.sharding import PartitionSpec as P

BLK = 64
VECS = 4
NB = 5
E_DEV = 128
LANES = 128
SUBLANES = 8
ROWS_PER_STEP = 32


DIAG_SHIFT = 1.5


def padded(cells, sides, width):
    for axis, dim in sides:
        count = lax.axis_size(axis)
        ends = count - 1
        head = lax.slice_in_dim(cells, 0, width, axis=dim)
        tail = lax.slice_in_dim(cells, cells.shape[dim] - width, cells.shape[dim], axis=dim)
        cells = jnp.concatenate(
            [
                lax.ppermute(tail, axis, [(i, (i + 1) % count) for i in range(ends)]),
                cells,
                lax.ppermute(head, axis, [((i + 1) % count, i) for i in range(ends)]),
            ],
            axis=dim,
        )
    return cells


def combine(values, mixing):
    shaped = values.reshape(values.shape[0], VECS, BLK)
    return jnp.einsum("eci,cd->edi", shaped, mixing, precision=lax.Precision.HIGHEST).reshape(
        values.shape[0], VECS * BLK
    )


def inner_block(left_side, right_side):
    left_shaped = left_side.reshape(left_side.shape[0], VECS, BLK)
    right_shaped = right_side.reshape(right_side.shape[0], VECS, BLK)
    return jnp.einsum("eci,edi->cd", left_shaped, right_shaped, precision=lax.Precision.HIGHEST)


def tree_sum(values, axes):
    for axis in axes:
        count = lax.axis_size(axis)
        if count & (count - 1):
            values = lax.psum(values, axis)
            continue
        stride = 1
        while stride < count:
            values = values + lax.ppermute(values, axis, [(i, i ^ stride) for i in range(count)])
            stride *= 2
    return values


def split_three(values):
    high = values.astype(jnp.bfloat16)
    rest = values - high.astype(jnp.float32)
    middle = rest.astype(jnp.bfloat16)
    low = (rest - middle.astype(jnp.float32)).astype(jnp.bfloat16)
    return jnp.concatenate([high, middle, low], axis=1)


def exchange_sum(values, axes):
    count = 1
    for axis in axes:
        count *= lax.axis_size(axis)
    flat = values.reshape(1, -1)
    everyone = lax.all_to_all(jnp.broadcast_to(flat, (count, flat.shape[1])), axes, 0, 0, tiled=True)
    return jnp.sum(everyone, axis=0).reshape(values.shape)


def coupling_kernel(jac_ref, own_ref, ghost_ref, cols_ref, mask_ref, out_ref, source_ref, picked_ref, z_ref, parts_ref):
    step = pl.program_id(0)
    rows = jac_ref.shape[1]
    tiles = jac_ref.shape[2] // LANES
    count = own_ref.shape[0]
    width = own_ref.shape[1]
    row0 = pl.multiple_of(step * rows, rows)

    @pl.when(step == 0)
    def _():
        source_ref[0:count] = split_three(own_ref[...])
        source_ref[count:2 * count] = split_three(ghost_ref[...])

    slots = lax.broadcasted_iota(jnp.int32, (rows, 2 * count), 1)
    for k in range(NB):
        chosen = (cols_ref[k] == slots).astype(jnp.bfloat16)
        spread = jnp.dot(chosen, source_ref[...], preferred_element_type=jnp.float32)
        picked_ref[k] = spread[:, 0:width] + spread[:, width:2 * width] + spread[:, 2 * width:3 * width]

    lane = lax.broadcasted_iota(jnp.int32, (SUBLANES, LANES), 1)
    for group in range(rows // SUBLANES):
        top = group * SUBLANES
        doubled = []
        for k in range(NB):
            per_vector = []
            for pair in range(VECS // 2):
                tile = picked_ref[k, top:top + SUBLANES, pair * LANES:(pair + 1) * LANES]
                swapped = pltpu.roll(tile, BLK, 1)
                per_vector.append(jnp.where(lane < BLK, tile, swapped))
                per_vector.append(jnp.where(lane >= BLK, tile, swapped))
            doubled.append(per_vector)

        def one_tile(t, carry):
            off = pl.multiple_of(t * LANES, LANES)
            blocks = [jac_ref[k, top:top + SUBLANES, pl.ds(off, LANES)] for k in range(NB)]
            for c in range(VECS):
                total = blocks[0] * doubled[0][c]
                for k in range(1, NB):
                    total = total + blocks[k] * doubled[k][c]
                z_ref[c, pl.ds(row0 + top, SUBLANES), pl.ds(off, LANES)] = total
            return carry

        lax.fori_loop(0, tiles, one_tile, 0)

    @pl.when(step == pl.num_programs(0) - 1)
    def _():
        full = tiles * LANES
        for c in range(VECS):
            total = z_ref[c]
            high = total.astype(jnp.bfloat16)
            parts_ref[2 * c] = high
            parts_ref[2 * c + 1] = (total - high.astype(jnp.float32)).astype(jnp.bfloat16)
        flat = parts_ref[...].reshape(2 * VECS * count, full)
        seg = (
            lax.broadcasted_iota(jnp.int32, (full, BLK), 0) // BLK
            == lax.broadcasted_iota(jnp.int32, (full, BLK), 1)
        ).astype(jnp.bfloat16)
        sums = jnp.dot(flat, seg, preferred_element_type=jnp.float32)
        coupled = jnp.concatenate(
            [sums[(2 * c) * count:(2 * c + 1) * count] + sums[(2 * c + 1) * count:(2 * c + 2) * count] for c in range(VECS)],
            axis=1,
        )
        summed = DIAG_SHIFT * own_ref[...] + coupled
        out_ref[...] = jnp.where(mask_ref[...] > 0.0, summed, jnp.float32(0.0))


def apply_operator(jac_t, own, ghost_rows, cols, mask):
    blocks, count, full = jac_t.shape
    width = own.shape[1]
    rows = min(ROWS_PER_STEP, count)
    return pl.pallas_call(
        coupling_kernel,
        out_shape=jax.ShapeDtypeStruct((count, width), jnp.float32),
        grid=(count // rows,),
        in_specs=[
            pl.BlockSpec((blocks, rows, full), lambda b: (0, b, 0)),
            pl.BlockSpec((count, width), lambda b: (0, 0)),
            pl.BlockSpec((count, width), lambda b: (0, 0)),
            pl.BlockSpec((blocks, rows, 1), lambda b: (0, b, 0)),
            pl.BlockSpec((count, 1), lambda b: (0, 0)),
        ],
        out_specs=pl.BlockSpec((count, width), lambda b: (0, 0)),
        scratch_shapes=[
            pltpu.VMEM((2 * count, 3 * width), jnp.bfloat16),
            pltpu.VMEM((blocks, rows, width), jnp.float32),
            pltpu.VMEM((VECS, count, full), jnp.float32),
            pltpu.VMEM((2 * VECS, count, full), jnp.bfloat16),
        ],
        compiler_params=pltpu.CompilerParams(dimension_semantics=("arbitrary",)),
        cost_estimate=pl.CostEstimate(
            flops=2 * blocks * count * full * VECS + 2 * 2 * VECS * count * full * BLK,
            bytes_accessed=4 * (blocks * count * full + 4 * count * width),
            transcendentals=0,
        ),
    )(jac_t, own, ghost_rows, cols, mask)


def per_device(start_block, jacobian, counts, columns, send_list):
    living = (lax.iota(jnp.int32, E_DEV) < counts[0])[:, None]
    anchor = jnp.where(living, start_block, jnp.float32(0.0))
    lend_rows = send_list[0]
    jac_t = jnp.transpose(jacobian, (1, 0, 2))
    cols = jnp.transpose(columns, (1, 0))[:, :, None]
    mask = living.astype(jnp.float32)

    def ghosts(values):
        outgoing = values[lend_rows]
        wide_in = padded(jnp.stack([outgoing[1], outgoing[0]]), (("wide", 0),), 1)
        narrow_in = padded(jnp.stack([outgoing[3], outgoing[2]]), (("narrow", 0),), 1)
        return jnp.concatenate([wide_in[0], wide_in[3], narrow_in[0], narrow_in[3]], 0)

    def operate(values):
        return apply_operator(jac_t, values, ghosts(values), cols, mask)

    first_image = operate(anchor)
    second_image = operate(first_image)
    blocks = (
        inner_block(first_image, anchor),
        inner_block(first_image, first_image),
        inner_block(second_image, anchor),
        inner_block(second_image, first_image),
        inner_block(second_image, second_image),
    )
    gram_parts = exchange_sum(jnp.stack(blocks), ("wide", "narrow"))
    normal_matrix = jnp.concatenate(
        [
            jnp.concatenate([gram_parts[1], gram_parts[3].T], 1),
            jnp.concatenate([gram_parts[3], gram_parts[4]], 1),
        ],
        0,
    )
    right_terms = jnp.concatenate([gram_parts[0], gram_parts[2]], 0)
    factor = jnp.linalg.cholesky(normal_matrix)
    coefficients = jax.scipy.linalg.cho_solve((factor, True), right_terms)
    correction = combine(anchor, coefficients[:VECS]) + combine(first_image, coefficients[VECS:])
    residual = anchor - (
        combine(first_image, coefficients[:VECS]) + combine(second_image, coefficients[VECS:])
    )
    return (correction, residual)


def solution(mesh):
    placed = (
        P(("wide", "narrow"), None),
        P(("wide", "narrow"), None, None),
        P(("wide", "narrow")),
        P(("wide", "narrow"), None),
        P(("wide", "narrow"), None, None),
    )
    return jax.shard_map(
        per_device,
        mesh=mesh,
        in_specs=placed,
        out_specs=(P(("wide", "narrow"), None), P(("wide", "narrow"), None)),
        check_vma=False,
    )
```

```python
import jax
import jax.numpy as jnp
from jax import lax
from jax.experimental import pallas as pl
from jax.experimental.pallas import tpu as pltpu
from jax.sharding import PartitionSpec as P

BLK = 64
VECS = 4
NB = 5
E_DEV = 128
LANES = 128
SUBLANES = 8
UNROLL = 4
ROWS_PER_STEP = 32


DIAG_SHIFT = 1.5


def padded(cells, sides, width):
    for axis, dim in sides:
        count = lax.axis_size(axis)
        ends = count - 1
        head = lax.slice_in_dim(cells, 0, width, axis=dim)
        tail = lax.slice_in_dim(cells, cells.shape[dim] - width, cells.shape[dim], axis=dim)
        cells = jnp.concatenate(
            [
                lax.ppermute(tail, axis, [(i, (i + 1) % count) for i in range(ends)]),
                cells,
                lax.ppermute(head, axis, [((i + 1) % count, i) for i in range(ends)]),
            ],
            axis=dim,
        )
    return cells


def combine(values, mixing):
    shaped = values.reshape(values.shape[0], VECS, BLK)
    return jnp.einsum("eci,cd->edi", shaped, mixing, precision=lax.Precision.HIGHEST).reshape(
        values.shape[0], VECS * BLK
    )


def inner_block(left_side, right_side):
    left_shaped = left_side.reshape(left_side.shape[0], VECS, BLK)
    right_shaped = right_side.reshape(right_side.shape[0], VECS, BLK)
    return jnp.einsum("eci,edi->cd", left_shaped, right_shaped, precision=lax.Precision.HIGHEST)


def tree_sum(values, axes):
    for axis in axes:
        count = lax.axis_size(axis)
        if count & (count - 1):
            values = lax.psum(values, axis)
            continue
        stride = 1
        while stride < count:
            values = values + lax.ppermute(values, axis, [(i, i ^ stride) for i in range(count)])
            stride *= 2
    return values


def split_three(values):
    high = values.astype(jnp.bfloat16)
    rest = values - high.astype(jnp.float32)
    middle = rest.astype(jnp.bfloat16)
    low = (rest - middle.astype(jnp.float32)).astype(jnp.bfloat16)
    return jnp.concatenate([high, middle, low], axis=1)


def exchange_sum(values, axes):
    count = 1
    for axis in axes:
        count *= lax.axis_size(axis)
    flat = values.reshape(1, -1)
    everyone = lax.all_to_all(jnp.broadcast_to(flat, (count, flat.shape[1])), axes, 0, 0, tiled=True)
    return jnp.sum(everyone, axis=0).reshape(values.shape)


def coupling_kernel(jac_ref, own_ref, ghost_ref, cols_ref, mask_ref, out_ref, source_ref, picked_ref, z_ref, parts_ref):
    step = pl.program_id(0)
    rows = jac_ref.shape[1]
    tiles = jac_ref.shape[2] // LANES
    count = own_ref.shape[0]
    width = own_ref.shape[1]
    row0 = pl.multiple_of(step * rows, rows)

    @pl.when(step == 0)
    def _():
        source_ref[0:count] = split_three(own_ref[...])
        source_ref[count:2 * count] = split_three(ghost_ref[...])

    slots = lax.broadcasted_iota(jnp.int32, (rows, 2 * count), 1)
    for k in range(NB):
        chosen = (cols_ref[k] == slots).astype(jnp.bfloat16)
        spread = jnp.dot(chosen, source_ref[...], preferred_element_type=jnp.float32)
        picked_ref[k] = spread[:, 0:width] + spread[:, width:2 * width] + spread[:, 2 * width:3 * width]

    lane = lax.broadcasted_iota(jnp.int32, (SUBLANES, LANES), 1)
    for group in range(rows // SUBLANES):
        top = group * SUBLANES
        doubled = []
        for k in range(NB):
            per_vector = []
            for pair in range(VECS // 2):
                tile = picked_ref[k, top:top + SUBLANES, pair * LANES:(pair + 1) * LANES]
                swapped = pltpu.roll(tile, BLK, 1)
                per_vector.append(jnp.where(lane < BLK, tile, swapped))
                per_vector.append(jnp.where(lane >= BLK, tile, swapped))
            doubled.append(per_vector)

        def one_tile(t, carry):
            off = pl.multiple_of(t * LANES, LANES)
            blocks = [jac_ref[k, top:top + SUBLANES, pl.ds(off, LANES)] for k in range(NB)]
            for c in range(VECS):
                terms = [blocks[k] * doubled[k][c] for k in range(NB)]
                while len(terms) > 1:
                    terms = [terms[i] + terms[i + 1] for i in range(0, len(terms) - 1, 2)] + (
                        [terms[-1]] if len(terms) % 2 else []
                    )
                z_ref[c, pl.ds(row0 + top, SUBLANES), pl.ds(off, LANES)] = terms[0]
            return carry

        lax.fori_loop(0, tiles, one_tile, 0, unroll=UNROLL)

    @pl.when(step == pl.num_programs(0) - 1)
    def _():
        full = tiles * LANES
        for c in range(VECS):
            total = z_ref[c]
            high = total.astype(jnp.bfloat16)
            parts_ref[2 * c] = high
            parts_ref[2 * c + 1] = (total - high.astype(jnp.float32)).astype(jnp.bfloat16)
        flat = parts_ref[...].reshape(2 * VECS * count, full)
        seg = (
            lax.broadcasted_iota(jnp.int32, (full, BLK), 0) // BLK
            == lax.broadcasted_iota(jnp.int32, (full, BLK), 1)
        ).astype(jnp.bfloat16)
        sums = jnp.dot(flat, seg, preferred_element_type=jnp.float32)
        coupled = jnp.concatenate(
            [sums[(2 * c) * count:(2 * c + 1) * count] + sums[(2 * c + 1) * count:(2 * c + 2) * count] for c in range(VECS)],
            axis=1,
        )
        summed = DIAG_SHIFT * own_ref[...] + coupled
        out_ref[...] = jnp.where(mask_ref[...] > 0.0, summed, jnp.float32(0.0))


def apply_operator(jac_t, own, ghost_rows, cols, mask):
    blocks, count, full = jac_t.shape
    width = own.shape[1]
    rows = min(ROWS_PER_STEP, count)
    return pl.pallas_call(
        coupling_kernel,
        out_shape=jax.ShapeDtypeStruct((count, width), jnp.float32),
        grid=(count // rows,),
        in_specs=[
            pl.BlockSpec((blocks, rows, full), lambda b: (0, b, 0)),
            pl.BlockSpec((count, width), lambda b: (0, 0)),
            pl.BlockSpec((count, width), lambda b: (0, 0)),
            pl.BlockSpec((blocks, rows, 1), lambda b: (0, b, 0)),
            pl.BlockSpec((count, 1), lambda b: (0, 0)),
        ],
        out_specs=pl.BlockSpec((count, width), lambda b: (0, 0)),
        scratch_shapes=[
            pltpu.VMEM((2 * count, 3 * width), jnp.bfloat16),
            pltpu.VMEM((blocks, rows, width), jnp.float32),
            pltpu.VMEM((VECS, count, full), jnp.float32),
            pltpu.VMEM((2 * VECS, count, full), jnp.bfloat16),
        ],
        compiler_params=pltpu.CompilerParams(dimension_semantics=("arbitrary",)),
        cost_estimate=pl.CostEstimate(
            flops=2 * blocks * count * full * VECS + 2 * 2 * VECS * count * full * BLK,
            bytes_accessed=4 * (blocks * count * full + 4 * count * width),
            transcendentals=0,
        ),
    )(jac_t, own, ghost_rows, cols, mask)


def per_device(start_block, jacobian, counts, columns, send_list):
    living = (lax.iota(jnp.int32, E_DEV) < counts[0])[:, None]
    anchor = jnp.where(living, start_block, jnp.float32(0.0))
    lend_rows = send_list[0]
    jac_t = jnp.transpose(jacobian, (1, 0, 2))
    cols = jnp.transpose(columns, (1, 0))[:, :, None]
    mask = living.astype(jnp.float32)

    def ghosts(values):
        outgoing = values[lend_rows]
        wide_in = padded(jnp.stack([outgoing[1], outgoing[0]]), (("wide", 0),), 1)
        narrow_in = padded(jnp.stack([outgoing[3], outgoing[2]]), (("narrow", 0),), 1)
        return jnp.concatenate([wide_in[0], wide_in[3], narrow_in[0], narrow_in[3]], 0)

    def operate(values):
        return apply_operator(jac_t, values, ghosts(values), cols, mask)

    first_image = operate(anchor)
    second_image = operate(first_image)
    blocks = (
        inner_block(first_image, anchor),
        inner_block(first_image, first_image),
        inner_block(second_image, anchor),
        inner_block(second_image, first_image),
        inner_block(second_image, second_image),
    )
    gram_parts = exchange_sum(jnp.stack(blocks), ("wide", "narrow"))
    normal_matrix = jnp.concatenate(
        [
            jnp.concatenate([gram_parts[1], gram_parts[3].T], 1),
            jnp.concatenate([gram_parts[3], gram_parts[4]], 1),
        ],
        0,
    )
    right_terms = jnp.concatenate([gram_parts[0], gram_parts[2]], 0)
    factor = jnp.linalg.cholesky(normal_matrix)
    coefficients = jax.scipy.linalg.cho_solve((factor, True), right_terms)
    correction = combine(anchor, coefficients[:VECS]) + combine(first_image, coefficients[VECS:])
    residual = anchor - (
        combine(first_image, coefficients[:VECS]) + combine(second_image, coefficients[VECS:])
    )
    return (correction, residual)


def solution(mesh):
    placed = (
        P(("wide", "narrow"), None),
        P(("wide", "narrow"), None, None),
        P(("wide", "narrow")),
        P(("wide", "narrow"), None),
        P(("wide", "narrow"), None, None),
    )
    return jax.shard_map(
        per_device,
        mesh=mesh,
        in_specs=placed,
        out_specs=(P(("wide", "narrow"), None), P(("wide", "narrow"), None)),
        check_vma=False,
    )
```

```python
import jax
import jax.numpy as jnp
from jax import lax
from jax.experimental import pallas as pl
from jax.experimental.pallas import tpu as pltpu
from jax.sharding import PartitionSpec as P

BLK = 64
VECS = 4
NB = 5
E_DEV = 128
LANES = 128
SUBLANES = 8
UNROLL = 4
ROWS_PER_STEP = 32


DIAG_SHIFT = 1.5


def padded(cells, sides, width):
    for axis, dim in sides:
        count = lax.axis_size(axis)
        ends = count - 1
        head = lax.slice_in_dim(cells, 0, width, axis=dim)
        tail = lax.slice_in_dim(cells, cells.shape[dim] - width, cells.shape[dim], axis=dim)
        cells = jnp.concatenate(
            [
                lax.ppermute(tail, axis, [(i, (i + 1) % count) for i in range(ends)]),
                cells,
                lax.ppermute(head, axis, [((i + 1) % count, i) for i in range(ends)]),
            ],
            axis=dim,
        )
    return cells


def combine(values, mixing):
    shaped = values.reshape(values.shape[0], VECS, BLK)
    return jnp.einsum("eci,cd->edi", shaped, mixing, precision=lax.Precision.HIGHEST).reshape(
        values.shape[0], VECS * BLK
    )


def inner_block(left_side, right_side):
    left_shaped = left_side.reshape(left_side.shape[0], VECS, BLK)
    right_shaped = right_side.reshape(right_side.shape[0], VECS, BLK)
    return jnp.einsum("eci,edi->cd", left_shaped, right_shaped, precision=lax.Precision.HIGHEST)


def tree_sum(values, axes):
    for axis in axes:
        count = lax.axis_size(axis)
        if count & (count - 1):
            values = lax.psum(values, axis)
            continue
        stride = 1
        while stride < count:
            values = values + lax.ppermute(values, axis, [(i, i ^ stride) for i in range(count)])
            stride *= 2
    return values


def split_three(values):
    high = values.astype(jnp.bfloat16)
    rest = values - high.astype(jnp.float32)
    middle = rest.astype(jnp.bfloat16)
    low = (rest - middle.astype(jnp.float32)).astype(jnp.bfloat16)
    return jnp.concatenate([high, middle, low], axis=1)


def exchange_sum(values, axes):
    count = 1
    for axis in axes:
        count *= lax.axis_size(axis)
    flat = values.reshape(1, -1)
    everyone = lax.all_to_all(jnp.broadcast_to(flat, (count, flat.shape[1])), axes, 0, 0, tiled=True)
    return jnp.sum(everyone, axis=0).reshape(values.shape)


def coupling_kernel(
    count_ref, lend_ref, jac_ref, own_ref, g0_ref, g1_ref, g2_ref, g3_ref, cols_ref,
    out_ref, lent_ref, kept_ref, source_ref, picked_ref, z_ref, parts_ref,
):
    step = pl.program_id(0)
    rows = jac_ref.shape[1]
    tiles = jac_ref.shape[2] // LANES
    count = own_ref.shape[0]
    width = own_ref.shape[1]
    ghost = g0_ref.shape[0]
    row0 = pl.multiple_of(step * rows, rows)

    @pl.when(step == 0)
    def _():
        living = lax.broadcasted_iota(jnp.int32, (count, 1), 0) < count_ref[0]
        source_ref[0:count] = split_three(jnp.where(living, own_ref[...], jnp.float32(0.0)))
        for q, piece in enumerate((g0_ref, g1_ref, g2_ref, g3_ref)):
            source_ref[count + q * ghost:count + (q + 1) * ghost] = split_three(piece[...])

    slots = lax.broadcasted_iota(jnp.int32, (rows, source_ref.shape[0]), 1)
    for k in range(NB):
        chosen = (cols_ref[:, k:k + 1] == slots).astype(jnp.bfloat16)
        spread = jnp.dot(chosen, source_ref[...], preferred_element_type=jnp.float32)
        picked_ref[k] = spread[:, 0:width] + spread[:, width:2 * width] + spread[:, 2 * width:3 * width]

    lane = lax.broadcasted_iota(jnp.int32, (SUBLANES, LANES), 1)
    for group in range(rows // SUBLANES):
        top = group * SUBLANES
        doubled = []
        for k in range(NB):
            per_vector = []
            for pair in range(VECS // 2):
                tile = picked_ref[k, top:top + SUBLANES, pair * LANES:(pair + 1) * LANES]
                swapped = pltpu.roll(tile, BLK, 1)
                per_vector.append(jnp.where(lane < BLK, tile, swapped))
                per_vector.append(jnp.where(lane >= BLK, tile, swapped))
            doubled.append(per_vector)

        def one_tile(t, carry):
            off = pl.multiple_of(t * LANES, LANES)
            blocks = [jac_ref[k, top:top + SUBLANES, pl.ds(off, LANES)] for k in range(NB)]
            for c in range(VECS):
                terms = [blocks[k] * doubled[k][c] for k in range(NB)]
                while len(terms) > 1:
                    terms = [terms[i] + terms[i + 1] for i in range(0, len(terms) - 1, 2)] + (
                        [terms[-1]] if len(terms) % 2 else []
                    )
                z_ref[c, pl.ds(row0 + top, SUBLANES), pl.ds(off, LANES)] = terms[0]
            return carry

        lax.fori_loop(0, tiles, one_tile, 0, unroll=UNROLL)

    @pl.when(step == pl.num_programs(0) - 1)
    def _():
        full = tiles * LANES
        for c in range(VECS):
            total = z_ref[c]
            high = total.astype(jnp.bfloat16)
            parts_ref[2 * c] = high
            parts_ref[2 * c + 1] = (total - high.astype(jnp.float32)).astype(jnp.bfloat16)
        flat = parts_ref[...].reshape(2 * VECS * count, full)
        seg = (
            lax.broadcasted_iota(jnp.int32, (full, BLK), 0) // BLK
            == lax.broadcasted_iota(jnp.int32, (full, BLK), 1)
        ).astype(jnp.bfloat16)
        sums = jnp.dot(flat, seg, preferred_element_type=jnp.float32)
        coupled = jnp.concatenate(
            [sums[(2 * c) * count:(2 * c + 1) * count] + sums[(2 * c + 1) * count:(2 * c + 2) * count] for c in range(VECS)],
            axis=1,
        )
        own = own_ref[...]
        living = lax.broadcasted_iota(jnp.int32, (count, 1), 0) < count_ref[0]
        out_ref[...] = jnp.where(living, DIAG_SHIFT * own + coupled, jnp.float32(0.0))
        kept_ref[...] = jnp.where(living, own, jnp.float32(0.0))
        for q in range(lend_ref.shape[0]):
            for j in range(lend_ref.shape[1]):
                row = q * lend_ref.shape[1] + j
                lent_ref[row:row + 1, :] = out_ref[pl.ds(lend_ref[q, j], 1), :]


def apply_operator(jac_t, own, ghost_rows, columns, counts, lend_rows):
    blocks, count, full = jac_t.shape
    width = own.shape[1]
    ghost = ghost_rows[0].shape[0]
    rows = min(ROWS_PER_STEP, count)
    smem = pl.BlockSpec(memory_space=pltpu.SMEM)
    whole = pl.BlockSpec((count, width), lambda b: (0, 0))
    piece = pl.BlockSpec((ghost, width), lambda b: (0, 0))
    lent = lend_rows.shape[0] * lend_rows.shape[1]
    return pl.pallas_call(
        coupling_kernel,
        out_shape=(
            jax.ShapeDtypeStruct((count, width), jnp.float32),
            jax.ShapeDtypeStruct((lent, width), jnp.float32),
            jax.ShapeDtypeStruct((count, width), jnp.float32),
        ),
        grid=(count // rows,),
        in_specs=[
            smem,
            smem,
            pl.BlockSpec((blocks, rows, full), lambda b: (0, b, 0)),
            whole,
            piece,
            piece,
            piece,
            piece,
            pl.BlockSpec((rows, blocks), lambda b: (b, 0)),
        ],
        out_specs=(whole, pl.BlockSpec((lent, width), lambda b: (0, 0)), whole),
        scratch_shapes=[
            pltpu.VMEM((count + 4 * ghost, 3 * width), jnp.bfloat16),
            pltpu.VMEM((blocks, rows, width), jnp.float32),
            pltpu.VMEM((VECS, count, full), jnp.float32),
            pltpu.VMEM((2 * VECS, count, full), jnp.bfloat16),
        ],
        compiler_params=pltpu.CompilerParams(dimension_semantics=("arbitrary",)),
        cost_estimate=pl.CostEstimate(
            flops=2 * blocks * count * full * VECS + 2 * 2 * VECS * count * full * BLK,
            bytes_accessed=4 * (blocks * count * full + 6 * count * width),
            transcendentals=0,
        ),
    )(counts, lend_rows, jac_t, own, *ghost_rows, columns)


def per_device(start_block, jacobian, counts, columns, send_list):
    lend_rows = send_list[0]
    jac_t = jnp.transpose(jacobian, (1, 0, 2))

    def ghosts(outgoing):
        wide, narrow = lax.axis_size("wide"), lax.axis_size("narrow")
        return (
            lax.ppermute(outgoing[0], "wide", [(i, i + 1) for i in range(wide - 1)]),
            lax.ppermute(outgoing[1], "wide", [(i + 1, i) for i in range(wide - 1)]),
            lax.ppermute(outgoing[2], "narrow", [(i, i + 1) for i in range(narrow - 1)]),
            lax.ppermute(outgoing[3], "narrow", [(i + 1, i) for i in range(narrow - 1)]),
        )

    def operate(values, outgoing):
        image, lent, kept = apply_operator(jac_t, values, ghosts(outgoing), columns, counts, lend_rows)
        return image, lent.reshape(outgoing.shape), kept

    first_image, first_lent, anchor = operate(start_block, start_block[lend_rows])
    second_image, _, _ = operate(first_image, first_lent)
    blocks = (
        inner_block(first_image, anchor),
        inner_block(first_image, first_image),
        inner_block(second_image, anchor),
        inner_block(second_image, first_image),
        inner_block(second_image, second_image),
    )
    gram_parts = exchange_sum(jnp.stack(blocks), ("wide", "narrow"))
    normal_matrix = jnp.concatenate(
        [
            jnp.concatenate([gram_parts[1], gram_parts[3].T], 1),
            jnp.concatenate([gram_parts[3], gram_parts[4]], 1),
        ],
        0,
    )
    right_terms = jnp.concatenate([gram_parts[0], gram_parts[2]], 0)
    factor = jnp.linalg.cholesky(normal_matrix)
    coefficients = jax.scipy.linalg.cho_solve((factor, True), right_terms)
    correction = combine(anchor, coefficients[:VECS]) + combine(first_image, coefficients[VECS:])
    residual = anchor - (
        combine(first_image, coefficients[:VECS]) + combine(second_image, coefficients[VECS:])
    )
    return (correction, residual)


def solution(mesh):
    placed = (
        P(("wide", "narrow"), None),
        P(("wide", "narrow"), None, None),
        P(("wide", "narrow")),
        P(("wide", "narrow"), None),
        P(("wide", "narrow"), None, None),
    )
    return jax.shard_map(
        per_device,
        mesh=mesh,
        in_specs=placed,
        out_specs=(P(("wide", "narrow"), None), P(("wide", "narrow"), None)),
        check_vma=False,
    )
```

```python
import functools

import jax
import jax.numpy as jnp
import numpy as np
from jax import lax
from jax.experimental import pallas as pl
from jax.experimental.pallas import tpu as pltpu
from jax.sharding import PartitionSpec as P

BLK = 64
VECS = 4
NB = 5
E_DEV = 128
LANES = 128
SUBLANES = 8
UNROLL = 4
ROWS_PER_STEP = 32


DIAG_SHIFT = 1.5


def padded(cells, sides, width):
    for axis, dim in sides:
        count = lax.axis_size(axis)
        ends = count - 1
        head = lax.slice_in_dim(cells, 0, width, axis=dim)
        tail = lax.slice_in_dim(cells, cells.shape[dim] - width, cells.shape[dim], axis=dim)
        cells = jnp.concatenate(
            [
                lax.ppermute(tail, axis, [(i, (i + 1) % count) for i in range(ends)]),
                cells,
                lax.ppermute(head, axis, [((i + 1) % count, i) for i in range(ends)]),
            ],
            axis=dim,
        )
    return cells


def combine(values, mixing):
    shaped = values.reshape(values.shape[0], VECS, BLK)
    return jnp.einsum("eci,cd->edi", shaped, mixing, precision=lax.Precision.HIGHEST).reshape(
        values.shape[0], VECS * BLK
    )


def inner_block(left_side, right_side):
    left_shaped = left_side.reshape(left_side.shape[0], VECS, BLK)
    right_shaped = right_side.reshape(right_side.shape[0], VECS, BLK)
    return jnp.einsum("eci,edi->cd", left_shaped, right_shaped, precision=lax.Precision.HIGHEST)


def tree_sum(values, axes):
    for axis in axes:
        count = lax.axis_size(axis)
        if count & (count - 1):
            values = lax.psum(values, axis)
            continue
        stride = 1
        while stride < count:
            values = values + lax.ppermute(values, axis, [(i, i ^ stride) for i in range(count)])
            stride *= 2
    return values


def split_three(values):
    high = values.astype(jnp.bfloat16)
    rest = values - high.astype(jnp.float32)
    middle = rest.astype(jnp.bfloat16)
    low = (rest - middle.astype(jnp.float32)).astype(jnp.bfloat16)
    return jnp.concatenate([high, middle, low], axis=1)


def exchange_sum(values, axes):
    count = 1
    for axis in axes:
        count *= lax.axis_size(axis)
    flat = values.reshape(1, -1)
    everyone = lax.all_to_all(jnp.broadcast_to(flat, (count, flat.shape[1])), axes, 0, 0, tiled=True)
    return jnp.sum(everyone, axis=0).reshape(values.shape)


def segment_sums(values, segments):
    width = values.shape[1]
    seg = (
        lax.broadcasted_iota(jnp.int32, (width, segments), 0) // (width // segments)
        == lax.broadcasted_iota(jnp.int32, (width, segments), 1)
    ).astype(jnp.bfloat16)
    parts = split_three(values)
    return (
        jnp.dot(parts[:, 0:width], seg, preferred_element_type=jnp.float32)
        + jnp.dot(parts[:, width:2 * width], seg, preferred_element_type=jnp.float32)
        + jnp.dot(parts[:, 2 * width:3 * width], seg, preferred_element_type=jnp.float32)
    )


def gram_rows(pairs):
    rows = []
    for left, right in pairs:
        for shift in range(VECS):
            moved = right if shift == 0 else pltpu.roll(right, shift * BLK, 1)
            rows.append(jnp.sum(left * moved, axis=0, keepdims=True))
    return segment_sums(jnp.concatenate(rows, axis=0), VECS)


def coupling_kernel(with_gram, count_ref, lend_ref, jac_ref, own_ref, g0_ref, g1_ref, g2_ref, g3_ref, cols_ref, *rest):
    if with_gram:
        anchor_ref, rest = rest[0], rest[1:]
    out_ref, l0_ref, l1_ref, l2_ref, l3_ref, kept_ref = rest[:6]
    rest = rest[6:]
    if with_gram:
        gram_ref, rest = rest[0], rest[1:]
    source_ref, picked_ref, z_ref, parts_ref = rest
    step = pl.program_id(0)
    rows = jac_ref.shape[1]
    tiles = jac_ref.shape[2] // LANES
    count = own_ref.shape[0]
    width = own_ref.shape[1]
    ghost = g0_ref.shape[0]
    row0 = pl.multiple_of(step * rows, rows)

    @pl.when(step == 0)
    def _():
        living = lax.broadcasted_iota(jnp.int32, (count, 1), 0) < count_ref[0]
        source_ref[0:count] = split_three(jnp.where(living, own_ref[...], jnp.float32(0.0)))
        for q, piece in enumerate((g0_ref, g1_ref, g2_ref, g3_ref)):
            source_ref[count + q * ghost:count + (q + 1) * ghost] = split_three(piece[...])
        slots = lax.broadcasted_iota(jnp.int32, (source_ref.shape[0], count), 0)
        for k in range(NB):
            chosen = (cols_ref[k:k + 1, :] == slots).astype(jnp.bfloat16)
            spread = lax.dot_general(
                chosen, source_ref[...], (((0,), (0,)), ((), ())), preferred_element_type=jnp.float32
            )
            picked_ref[k] = spread[:, 0:width] + spread[:, width:2 * width] + spread[:, 2 * width:3 * width]

    lane = lax.broadcasted_iota(jnp.int32, (SUBLANES, LANES), 1)
    for group in range(rows // SUBLANES):
        top = group * SUBLANES
        first_row = pl.multiple_of(row0 + top, SUBLANES)
        doubled = []
        for k in range(NB):
            per_vector = []
            for pair in range(VECS // 2):
                tile = picked_ref[k, pl.ds(first_row, SUBLANES), pair * LANES:(pair + 1) * LANES]
                swapped = pltpu.roll(tile, BLK, 1)
                per_vector.append(jnp.where(lane < BLK, tile, swapped))
                per_vector.append(jnp.where(lane >= BLK, tile, swapped))
            doubled.append(per_vector)

        def one_tile(t, carry):
            off = pl.multiple_of(t * LANES, LANES)
            blocks = [jac_ref[k, top:top + SUBLANES, pl.ds(off, LANES)] for k in range(NB)]
            for c in range(VECS):
                terms = [blocks[k] * doubled[k][c] for k in range(NB)]
                while len(terms) > 1:
                    terms = [terms[i] + terms[i + 1] for i in range(0, len(terms) - 1, 2)] + (
                        [terms[-1]] if len(terms) % 2 else []
                    )
                z_ref[c, pl.ds(first_row, SUBLANES), pl.ds(off, LANES)] = terms[0]
            return carry

        lax.fori_loop(0, tiles, one_tile, 0, unroll=UNROLL)

    @pl.when(step == pl.num_programs(0) - 1)
    def _():
        full = tiles * LANES
        for c in range(VECS):
            total = z_ref[c]
            high = total.astype(jnp.bfloat16)
            parts_ref[2 * c] = high
            parts_ref[2 * c + 1] = (total - high.astype(jnp.float32)).astype(jnp.bfloat16)
        flat = parts_ref[...].reshape(2 * VECS * count, full)
        seg = (
            lax.broadcasted_iota(jnp.int32, (full, BLK), 0) // BLK
            == lax.broadcasted_iota(jnp.int32, (full, BLK), 1)
        ).astype(jnp.bfloat16)
        sums = jnp.dot(flat, seg, preferred_element_type=jnp.float32)
        coupled = jnp.concatenate(
            [sums[(2 * c) * count:(2 * c + 1) * count] + sums[(2 * c + 1) * count:(2 * c + 2) * count] for c in range(VECS)],
            axis=1,
        )
        own = own_ref[...]
        living = lax.broadcasted_iota(jnp.int32, (count, 1), 0) < count_ref[0]
        image = jnp.where(living, DIAG_SHIFT * own + coupled, jnp.float32(0.0))
        out_ref[...] = image
        kept = jnp.where(living, own, jnp.float32(0.0))
        kept_ref[...] = kept
        for q, lent_ref in enumerate((l0_ref, l1_ref, l2_ref, l3_ref)):
            for j in range(lend_ref.shape[1]):
                lent_ref[j:j + 1, :] = out_ref[pl.ds(lend_ref[q, j], 1), :]
        if with_gram:
            anchor = anchor_ref[...]
            gram_ref[...] = gram_rows(
                ((kept, anchor), (kept, kept), (image, anchor), (image, kept), (image, image))
            )


def apply_operator(jac_t, own, ghost_rows, cols_t, counts, lend_rows, anchor=None):
    blocks, count, full = jac_t.shape
    width = own.shape[1]
    ghost = ghost_rows[0].shape[0]
    rows = min(ROWS_PER_STEP, count)
    with_gram = anchor is not None
    smem = pl.BlockSpec(memory_space=pltpu.SMEM)
    whole = pl.BlockSpec((count, width), lambda b: (0, 0))
    piece = pl.BlockSpec((ghost, width), lambda b: (0, 0))
    lent = lend_rows.shape[1]
    lent_spec = pl.BlockSpec((lent, width), lambda b: (0, 0))
    in_specs = [smem, smem, pl.BlockSpec((blocks, rows, full), lambda b: (0, b, 0)), whole, piece, piece, piece, piece,
                pl.BlockSpec((blocks, count), lambda b: (0, 0))]
    out_shape = [jax.ShapeDtypeStruct((count, width), jnp.float32)]
    out_shape += [jax.ShapeDtypeStruct((lent, width), jnp.float32)] * lend_rows.shape[0]
    out_shape += [jax.ShapeDtypeStruct((count, width), jnp.float32)]
    out_specs = [whole] + [lent_spec] * lend_rows.shape[0] + [whole]
    args = [counts, lend_rows, jac_t, own, *ghost_rows, cols_t]
    if with_gram:
        in_specs.append(whole)
        args.append(anchor)
        gram_count = 5 * VECS
        out_shape.append(jax.ShapeDtypeStruct((gram_count, VECS), jnp.float32))
        out_specs.append(pl.BlockSpec((gram_count, VECS), lambda b: (0, 0)))
    return pl.pallas_call(
        functools.partial(coupling_kernel, with_gram),
        out_shape=tuple(out_shape),
        grid=(count // rows,),
        in_specs=in_specs,
        out_specs=tuple(out_specs),
        scratch_shapes=[
            pltpu.VMEM((count + 4 * ghost, 3 * width), jnp.bfloat16),
            pltpu.VMEM((blocks, count, width), jnp.float32),
            pltpu.VMEM((VECS, count, full), jnp.float32),
            pltpu.VMEM((2 * VECS, count, full), jnp.bfloat16),
        ],
        compiler_params=pltpu.CompilerParams(dimension_semantics=("arbitrary",)),
        cost_estimate=pl.CostEstimate(
            flops=2 * blocks * count * full * VECS + 2 * 2 * VECS * count * full * BLK,
            bytes_accessed=4 * (blocks * count * full + 6 * count * width),
            transcendentals=0,
        ),
    )(*args)


def per_device(start_block, jacobian, counts, columns, send_list):
    lend_rows = send_list[0]
    jac_t = jnp.transpose(jacobian, (1, 0, 2))

    def ghosts(outgoing):
        wide, narrow = lax.axis_size("wide"), lax.axis_size("narrow")
        return (
            lax.ppermute(outgoing[0], "wide", [(i, i + 1) for i in range(wide - 1)]),
            lax.ppermute(outgoing[1], "wide", [(i + 1, i) for i in range(wide - 1)]),
            lax.ppermute(outgoing[2], "narrow", [(i, i + 1) for i in range(narrow - 1)]),
            lax.ppermute(outgoing[3], "narrow", [(i + 1, i) for i in range(narrow - 1)]),
        )

    cols_t = jnp.transpose(columns, (1, 0))
    first = apply_operator(jac_t, start_block, ghosts(start_block[lend_rows]), cols_t, counts, lend_rows)
    first_image, first_lent, anchor = first[0], jnp.stack(first[1:5]), first[5]
    second = apply_operator(jac_t, first_image, ghosts(first_lent), cols_t, counts, lend_rows, anchor)
    second_image, raw_gram = second[0], second[6]
    raw_gram = exchange_sum(raw_gram, ("wide", "narrow"))
    pair = np.arange(5)[:, None, None]
    row_c = np.arange(VECS)[None, :, None]
    col_d = np.arange(VECS)[None, None, :]
    gram_parts = raw_gram[pair * VECS + (row_c - col_d) % VECS, np.broadcast_to(row_c, (5, VECS, VECS))]
    normal_matrix = jnp.concatenate(
        [
            jnp.concatenate([gram_parts[1], gram_parts[3].T], 1),
            jnp.concatenate([gram_parts[3], gram_parts[4]], 1),
        ],
        0,
    )
    right_terms = jnp.concatenate([gram_parts[0], gram_parts[2]], 0)
    factor = jnp.linalg.cholesky(normal_matrix)
    coefficients = jax.scipy.linalg.cho_solve((factor, True), right_terms)
    correction = combine(anchor, coefficients[:VECS]) + combine(first_image, coefficients[VECS:])
    residual = anchor - (
        combine(first_image, coefficients[:VECS]) + combine(second_image, coefficients[VECS:])
    )
    return (correction, residual)


def solution(mesh):
    placed = (
        P(("wide", "narrow"), None),
        P(("wide", "narrow"), None, None),
        P(("wide", "narrow")),
        P(("wide", "narrow"), None),
        P(("wide", "narrow"), None, None),
    )
    return jax.shard_map(
        per_device,
        mesh=mesh,
        in_specs=placed,
        out_specs=(P(("wide", "narrow"), None), P(("wide", "narrow"), None)),
        check_vma=False,
    )
```

```python
import functools

import jax
import jax.numpy as jnp
import numpy as np
from jax import lax
from jax.experimental import pallas as pl
from jax.experimental.pallas import tpu as pltpu
from jax.sharding import PartitionSpec as P

BLK = 64
VECS = 4
NB = 5
E_DEV = 128
LANES = 128
SUBLANES = 8
UNROLL = 4
ROWS_PER_STEP = 32


DIAG_SHIFT = 1.5


def padded(cells, sides, width):
    for axis, dim in sides:
        count = lax.axis_size(axis)
        ends = count - 1
        head = lax.slice_in_dim(cells, 0, width, axis=dim)
        tail = lax.slice_in_dim(cells, cells.shape[dim] - width, cells.shape[dim], axis=dim)
        cells = jnp.concatenate(
            [
                lax.ppermute(tail, axis, [(i, (i + 1) % count) for i in range(ends)]),
                cells,
                lax.ppermute(head, axis, [((i + 1) % count, i) for i in range(ends)]),
            ],
            axis=dim,
        )
    return cells


def combine(values, mixing):
    shaped = values.reshape(values.shape[0], VECS, BLK)
    return jnp.einsum("eci,cd->edi", shaped, mixing, precision=lax.Precision.HIGHEST).reshape(
        values.shape[0], VECS * BLK
    )


def inner_block(left_side, right_side):
    left_shaped = left_side.reshape(left_side.shape[0], VECS, BLK)
    right_shaped = right_side.reshape(right_side.shape[0], VECS, BLK)
    return jnp.einsum("eci,edi->cd", left_shaped, right_shaped, precision=lax.Precision.HIGHEST)


def tree_sum(values, axes):
    for axis in axes:
        count = lax.axis_size(axis)
        if count & (count - 1):
            values = lax.psum(values, axis)
            continue
        stride = 1
        while stride < count:
            values = values + lax.ppermute(values, axis, [(i, i ^ stride) for i in range(count)])
            stride *= 2
    return values


def split_three(values):
    high = values.astype(jnp.bfloat16)
    rest = values - high.astype(jnp.float32)
    middle = rest.astype(jnp.bfloat16)
    low = (rest - middle.astype(jnp.float32)).astype(jnp.bfloat16)
    return jnp.concatenate([high, middle, low], axis=1)


def exchange_sum(values, axes):
    count = 1
    for axis in axes:
        count *= lax.axis_size(axis)
    flat = values.reshape(1, -1)
    everyone = lax.all_to_all(jnp.broadcast_to(flat, (count, flat.shape[1])), axes, 0, 0, tiled=True)
    return jnp.sum(everyone, axis=0).reshape(values.shape)


def segment_sums(values, segments):
    width = values.shape[1]
    seg = (
        lax.broadcasted_iota(jnp.int32, (width, segments), 0) // (width // segments)
        == lax.broadcasted_iota(jnp.int32, (width, segments), 1)
    ).astype(jnp.bfloat16)
    parts = split_three(values)
    return (
        jnp.dot(parts[:, 0:width], seg, preferred_element_type=jnp.float32)
        + jnp.dot(parts[:, width:2 * width], seg, preferred_element_type=jnp.float32)
        + jnp.dot(parts[:, 2 * width:3 * width], seg, preferred_element_type=jnp.float32)
    )


def gram_rows(pairs):
    rows = []
    for left, right in pairs:
        for shift in range(VECS):
            moved = right if shift == 0 else pltpu.roll(right, shift * BLK, 1)
            rows.append(jnp.sum(left * moved, axis=0, keepdims=True))
    return segment_sums(jnp.concatenate(rows, axis=0), VECS)


def coupling_kernel(with_gram, count_ref, lend_ref, jac_ref, own_ref, g0_ref, g1_ref, g2_ref, g3_ref, cols_ref, *rest):
    if with_gram:
        anchor_ref, rest = rest[0], rest[1:]
    out_ref, l0_ref, l1_ref, l2_ref, l3_ref, kept_ref = rest[:6]
    rest = rest[6:]
    if with_gram:
        gram_ref, rest = rest[0], rest[1:]
    source_ref, picked_ref, z_ref, parts_ref = rest
    step = pl.program_id(0)
    rows = jac_ref.shape[1]
    tiles = jac_ref.shape[2] // LANES
    count = own_ref.shape[0]
    width = own_ref.shape[1]
    ghost = g0_ref.shape[0]
    row0 = pl.multiple_of(step * rows, rows)

    @pl.when(step == 0)
    def _():
        living = lax.broadcasted_iota(jnp.int32, (count, 1), 0) < count_ref[0]
        source_ref[0:count] = split_three(jnp.where(living, own_ref[...], jnp.float32(0.0)))
        for q, piece in enumerate((g0_ref, g1_ref, g2_ref, g3_ref)):
            source_ref[count + q * ghost:count + (q + 1) * ghost] = split_three(piece[...])
        slots = lax.broadcasted_iota(jnp.int32, (source_ref.shape[0], count), 0)
        for k in range(NB):
            chosen = (cols_ref[k:k + 1, :] == slots).astype(jnp.bfloat16)
            spread = lax.dot_general(
                chosen, source_ref[...], (((0,), (0,)), ((), ())), preferred_element_type=jnp.float32
            )
            picked_ref[k] = spread[:, 0:width] + spread[:, width:2 * width] + spread[:, 2 * width:3 * width]

    lane = lax.broadcasted_iota(jnp.int32, (SUBLANES, LANES), 1)
    for group in range(rows // SUBLANES):
        top = group * SUBLANES
        first_row = pl.multiple_of(row0 + top, SUBLANES)
        doubled = []
        for k in range(NB):
            per_vector = []
            for pair in range(VECS // 2):
                tile = picked_ref[k, pl.ds(first_row, SUBLANES), pair * LANES:(pair + 1) * LANES]
                swapped = pltpu.roll(tile, BLK, 1)
                per_vector.append(jnp.where(lane < BLK, tile, swapped))
                per_vector.append(jnp.where(lane >= BLK, tile, swapped))
            doubled.append(per_vector)

        def one_tile(t, carry):
            off = pl.multiple_of(t * LANES, LANES)
            blocks = [jac_ref[k, top:top + SUBLANES, pl.ds(off, LANES)] for k in range(NB)]
            for c in range(VECS):
                terms = [blocks[k] * doubled[k][c] for k in range(NB)]
                while len(terms) > 1:
                    terms = [terms[i] + terms[i + 1] for i in range(0, len(terms) - 1, 2)] + (
                        [terms[-1]] if len(terms) % 2 else []
                    )
                z_ref[c, pl.ds(first_row, SUBLANES), pl.ds(off, LANES)] = terms[0]
            return carry

        lax.fori_loop(0, tiles, one_tile, 0, unroll=UNROLL)

    @pl.when(step == pl.num_programs(0) - 1)
    def _():
        full = tiles * LANES
        for c in range(VECS):
            total = z_ref[c]
            high = total.astype(jnp.bfloat16)
            parts_ref[2 * c] = high
            parts_ref[2 * c + 1] = (total - high.astype(jnp.float32)).astype(jnp.bfloat16)
        flat = parts_ref[...].reshape(2 * VECS * count, full)
        seg = (
            lax.broadcasted_iota(jnp.int32, (full, BLK), 0) // BLK
            == lax.broadcasted_iota(jnp.int32, (full, BLK), 1)
        ).astype(jnp.bfloat16)
        sums = jnp.dot(flat, seg, preferred_element_type=jnp.float32)
        coupled = jnp.concatenate(
            [sums[(2 * c) * count:(2 * c + 1) * count] + sums[(2 * c + 1) * count:(2 * c + 2) * count] for c in range(VECS)],
            axis=1,
        )
        own = own_ref[...]
        living = lax.broadcasted_iota(jnp.int32, (count, 1), 0) < count_ref[0]
        image = jnp.where(living, DIAG_SHIFT * own + coupled, jnp.float32(0.0))
        out_ref[...] = image
        kept = jnp.where(living, own, jnp.float32(0.0))
        kept_ref[...] = kept
        for q, lent_ref in enumerate((l0_ref, l1_ref, l2_ref, l3_ref)):
            for j in range(lend_ref.shape[1]):
                lent_ref[j:j + 1, :] = out_ref[pl.ds(lend_ref[q, j], 1), :]
        if with_gram:
            anchor = anchor_ref[...]
            partial = gram_rows(((kept, anchor), (kept, kept), (image, anchor), (image, kept), (image, image)))
            for target in range(gram_ref.shape[0]):
                gram_ref[target] = partial


def apply_operator(jac_t, own, ghost_rows, cols_t, counts, lend_rows, anchor=None, peers=1):
    blocks, count, full = jac_t.shape
    width = own.shape[1]
    ghost = ghost_rows[0].shape[0]
    rows = min(ROWS_PER_STEP, count)
    with_gram = anchor is not None
    smem = pl.BlockSpec(memory_space=pltpu.SMEM)
    whole = pl.BlockSpec((count, width), lambda b: (0, 0))
    piece = pl.BlockSpec((ghost, width), lambda b: (0, 0))
    lent = lend_rows.shape[1]
    lent_spec = pl.BlockSpec((lent, width), lambda b: (0, 0))
    in_specs = [smem, smem, pl.BlockSpec((blocks, rows, full), lambda b: (0, b, 0)), whole, piece, piece, piece, piece,
                pl.BlockSpec((blocks, count), lambda b: (0, 0))]
    out_shape = [jax.ShapeDtypeStruct((count, width), jnp.float32)]
    out_shape += [jax.ShapeDtypeStruct((lent, width), jnp.float32)] * lend_rows.shape[0]
    out_shape += [jax.ShapeDtypeStruct((count, width), jnp.float32)]
    out_specs = [whole] + [lent_spec] * lend_rows.shape[0] + [whole]
    args = [counts, lend_rows, jac_t, own, *ghost_rows, cols_t]
    if with_gram:
        in_specs.append(whole)
        args.append(anchor)
        gram_count = 5 * VECS
        out_shape.append(jax.ShapeDtypeStruct((peers, gram_count, VECS), jnp.float32))
        out_specs.append(pl.BlockSpec((peers, gram_count, VECS), lambda b: (0, 0, 0)))
    return pl.pallas_call(
        functools.partial(coupling_kernel, with_gram),
        out_shape=tuple(out_shape),
        grid=(count // rows,),
        in_specs=in_specs,
        out_specs=tuple(out_specs),
        scratch_shapes=[
            pltpu.VMEM((count + 4 * ghost, 3 * width), jnp.bfloat16),
            pltpu.VMEM((blocks, count, width), jnp.float32),
            pltpu.VMEM((VECS, count, full), jnp.float32),
            pltpu.VMEM((2 * VECS, count, full), jnp.bfloat16),
        ],
        compiler_params=pltpu.CompilerParams(dimension_semantics=("arbitrary",)),
        cost_estimate=pl.CostEstimate(
            flops=2 * blocks * count * full * VECS + 2 * 2 * VECS * count * full * BLK,
            bytes_accessed=4 * (blocks * count * full + 6 * count * width),
            transcendentals=0,
        ),
    )(*args)


def per_device(start_block, jacobian, counts, columns, send_list):
    lend_rows = send_list[0]
    jac_t = jnp.transpose(jacobian, (1, 0, 2))

    def ghosts(outgoing):
        wide, narrow = lax.axis_size("wide"), lax.axis_size("narrow")
        return (
            lax.ppermute(outgoing[0], "wide", [(i, i + 1) for i in range(wide - 1)]),
            lax.ppermute(outgoing[1], "wide", [(i + 1, i) for i in range(wide - 1)]),
            lax.ppermute(outgoing[2], "narrow", [(i, i + 1) for i in range(narrow - 1)]),
            lax.ppermute(outgoing[3], "narrow", [(i + 1, i) for i in range(narrow - 1)]),
        )

    cols_t = jnp.transpose(columns, (1, 0))
    first = apply_operator(jac_t, start_block, ghosts(start_block[lend_rows]), cols_t, counts, lend_rows)
    first_image, first_lent, anchor = first[0], jnp.stack(first[1:5]), first[5]
    peers = lax.axis_size("wide") * lax.axis_size("narrow")
    second = apply_operator(jac_t, first_image, ghosts(first_lent), cols_t, counts, lend_rows, anchor, peers)
    second_image, raw_gram = second[0], second[6]
    everyone = lax.all_to_all(raw_gram, ("wide", "narrow"), 0, 0, tiled=True)
    raw_gram = jnp.sum(everyone, axis=0).reshape(5, VECS, VECS)
    shift = np.arange(VECS)[:, None, None]
    row_c = np.arange(VECS)[None, :, None]
    col_d = np.arange(VECS)[None, None, :]
    pick = jnp.asarray(((row_c - col_d) % VECS == shift).astype(np.float32))
    gram_parts = jnp.sum(raw_gram[:, :, :, None] * pick[None], axis=1)
    normal_matrix = jnp.concatenate(
        [
            jnp.concatenate([gram_parts[1], gram_parts[3].T], 1),
            jnp.concatenate([gram_parts[3], gram_parts[4]], 1),
        ],
        0,
    )
    right_terms = jnp.concatenate([gram_parts[0], gram_parts[2]], 0)
    factor = jnp.linalg.cholesky(normal_matrix)
    coefficients = jax.scipy.linalg.cho_solve((factor, True), right_terms)
    correction = combine(anchor, coefficients[:VECS]) + combine(first_image, coefficients[VECS:])
    residual = anchor - (
        combine(first_image, coefficients[:VECS]) + combine(second_image, coefficients[VECS:])
    )
    return (correction, residual)


def solution(mesh):
    placed = (
        P(("wide", "narrow"), None),
        P(("wide", "narrow"), None, None),
        P(("wide", "narrow")),
        P(("wide", "narrow"), None),
        P(("wide", "narrow"), None, None),
    )
    return jax.shard_map(
        per_device,
        mesh=mesh,
        in_specs=placed,
        out_specs=(P(("wide", "narrow"), None), P(("wide", "narrow"), None)),
        check_vma=False,
    )
```

```python
import functools

import jax
import jax.numpy as jnp
import numpy as np
from jax import lax
from jax.experimental import pallas as pl
from jax.experimental.pallas import tpu as pltpu
from jax.sharding import PartitionSpec as P

BLK = 64
VECS = 4
NB = 5
E_DEV = 128
LANES = 128
SUBLANES = 8
UNROLL = 4
ROWS_PER_STEP = 32


DIAG_SHIFT = 1.5


def padded(cells, sides, width):
    for axis, dim in sides:
        count = lax.axis_size(axis)
        ends = count - 1
        head = lax.slice_in_dim(cells, 0, width, axis=dim)
        tail = lax.slice_in_dim(cells, cells.shape[dim] - width, cells.shape[dim], axis=dim)
        cells = jnp.concatenate(
            [
                lax.ppermute(tail, axis, [(i, (i + 1) % count) for i in range(ends)]),
                cells,
                lax.ppermute(head, axis, [((i + 1) % count, i) for i in range(ends)]),
            ],
            axis=dim,
        )
    return cells


def combine(values, mixing):
    shaped = values.reshape(values.shape[0], VECS, BLK)
    return jnp.einsum("eci,cd->edi", shaped, mixing, precision=lax.Precision.HIGHEST).reshape(
        values.shape[0], VECS * BLK
    )


def inner_block(left_side, right_side):
    left_shaped = left_side.reshape(left_side.shape[0], VECS, BLK)
    right_shaped = right_side.reshape(right_side.shape[0], VECS, BLK)
    return jnp.einsum("eci,edi->cd", left_shaped, right_shaped, precision=lax.Precision.HIGHEST)


def tree_sum(values, axes):
    for axis in axes:
        count = lax.axis_size(axis)
        if count & (count - 1):
            values = lax.psum(values, axis)
            continue
        stride = 1
        while stride < count:
            values = values + lax.ppermute(values, axis, [(i, i ^ stride) for i in range(count)])
            stride *= 2
    return values


def split_three(values):
    high = values.astype(jnp.bfloat16)
    rest = values - high.astype(jnp.float32)
    middle = rest.astype(jnp.bfloat16)
    low = (rest - middle.astype(jnp.float32)).astype(jnp.bfloat16)
    return jnp.concatenate([high, middle, low], axis=1)


def exchange_sum(values, axes):
    count = 1
    for axis in axes:
        count *= lax.axis_size(axis)
    flat = values.reshape(1, -1)
    everyone = lax.all_to_all(jnp.broadcast_to(flat, (count, flat.shape[1])), axes, 0, 0, tiled=True)
    return jnp.sum(everyone, axis=0).reshape(values.shape)


def segment_sums(values, segments):
    width = values.shape[1]
    seg = (
        lax.broadcasted_iota(jnp.int32, (width, segments), 0) // (width // segments)
        == lax.broadcasted_iota(jnp.int32, (width, segments), 1)
    ).astype(jnp.bfloat16)
    parts = split_three(values)
    return (
        jnp.dot(parts[:, 0:width], seg, preferred_element_type=jnp.float32)
        + jnp.dot(parts[:, width:2 * width], seg, preferred_element_type=jnp.float32)
        + jnp.dot(parts[:, 2 * width:3 * width], seg, preferred_element_type=jnp.float32)
    )


def gram_columns(pairs):
    rows = []
    for left, right in pairs:
        for shift in range(VECS):
            moved = right if shift == 0 else pltpu.roll(right, shift * BLK, 1)
            rows.append(jnp.sum(left * moved, axis=0, keepdims=True))
    stacked = jnp.concatenate(rows, axis=0)
    width = stacked.shape[1]
    seg = (
        lax.broadcasted_iota(jnp.int32, (VECS, width), 1) // BLK
        == lax.broadcasted_iota(jnp.int32, (VECS, width), 0)
    ).astype(jnp.bfloat16)
    parts = split_three(stacked)
    dims = (((1,), (1,)), ((), ()))
    return sum(
        lax.dot_general(seg, parts[:, p * width:(p + 1) * width], dims, preferred_element_type=jnp.float32)
        for p in range(3)
    )


def coupling_kernel(with_gram, count_ref, lend_ref, jac_ref, own_ref, g0_ref, g1_ref, g2_ref, g3_ref, cols_ref, *rest):
    if with_gram:
        anchor_ref, rest = rest[0], rest[1:]
    out_ref, l0_ref, l1_ref, l2_ref, l3_ref, kept_ref = rest[:6]
    rest = rest[6:]
    if with_gram:
        gram_ref, rest = rest[0], rest[1:]
    source_ref, picked_ref, z_ref, parts_ref = rest
    step = pl.program_id(0)
    rows = jac_ref.shape[1]
    tiles = jac_ref.shape[2] // LANES
    count = own_ref.shape[0]
    width = own_ref.shape[1]
    ghost = g0_ref.shape[0]
    row0 = pl.multiple_of(step * rows, rows)

    @pl.when(step == 0)
    def _():
        living = lax.broadcasted_iota(jnp.int32, (count, 1), 0) < count_ref[0]
        source_ref[0:count] = split_three(jnp.where(living, own_ref[...], jnp.float32(0.0)))
        for q, piece in enumerate((g0_ref, g1_ref, g2_ref, g3_ref)):
            source_ref[count + q * ghost:count + (q + 1) * ghost] = split_three(piece[...])
        slots = lax.broadcasted_iota(jnp.int32, (source_ref.shape[0], count), 0)
        for k in range(NB):
            chosen = (cols_ref[k:k + 1, :] == slots).astype(jnp.bfloat16)
            spread = lax.dot_general(
                chosen, source_ref[...], (((0,), (0,)), ((), ())), preferred_element_type=jnp.float32
            )
            picked_ref[k] = spread[:, 0:width] + spread[:, width:2 * width] + spread[:, 2 * width:3 * width]

    lane = lax.broadcasted_iota(jnp.int32, (SUBLANES, LANES), 1)
    for group in range(rows // SUBLANES):
        top = group * SUBLANES
        first_row = pl.multiple_of(row0 + top, SUBLANES)
        doubled = []
        for k in range(NB):
            per_vector = []
            for pair in range(VECS // 2):
                tile = picked_ref[k, pl.ds(first_row, SUBLANES), pair * LANES:(pair + 1) * LANES]
                swapped = pltpu.roll(tile, BLK, 1)
                per_vector.append(jnp.where(lane < BLK, tile, swapped))
                per_vector.append(jnp.where(lane >= BLK, tile, swapped))
            doubled.append(per_vector)

        def one_tile(t, carry):
            off = pl.multiple_of(t * LANES, LANES)
            blocks = [jac_ref[k, top:top + SUBLANES, pl.ds(off, LANES)] for k in range(NB)]
            for c in range(VECS):
                terms = [blocks[k] * doubled[k][c] for k in range(NB)]
                while len(terms) > 1:
                    terms = [terms[i] + terms[i + 1] for i in range(0, len(terms) - 1, 2)] + (
                        [terms[-1]] if len(terms) % 2 else []
                    )
                z_ref[c, pl.ds(first_row, SUBLANES), pl.ds(off, LANES)] = terms[0]
            return carry

        lax.fori_loop(0, tiles, one_tile, 0, unroll=UNROLL)

    @pl.when(step == pl.num_programs(0) - 1)
    def _():
        full = tiles * LANES
        for c in range(VECS):
            total = z_ref[c]
            high = total.astype(jnp.bfloat16)
            parts_ref[2 * c] = high
            parts_ref[2 * c + 1] = (total - high.astype(jnp.float32)).astype(jnp.bfloat16)
        flat = parts_ref[...].reshape(2 * VECS * count, full)
        seg = (
            lax.broadcasted_iota(jnp.int32, (full, BLK), 0) // BLK
            == lax.broadcasted_iota(jnp.int32, (full, BLK), 1)
        ).astype(jnp.bfloat16)
        sums = jnp.dot(flat, seg, preferred_element_type=jnp.float32)
        coupled = jnp.concatenate(
            [sums[(2 * c) * count:(2 * c + 1) * count] + sums[(2 * c + 1) * count:(2 * c + 2) * count] for c in range(VECS)],
            axis=1,
        )
        own = own_ref[...]
        living = lax.broadcasted_iota(jnp.int32, (count, 1), 0) < count_ref[0]
        image = jnp.where(living, DIAG_SHIFT * own + coupled, jnp.float32(0.0))
        out_ref[...] = image
        kept = jnp.where(living, own, jnp.float32(0.0))
        kept_ref[...] = kept
        for q, lent_ref in enumerate((l0_ref, l1_ref, l2_ref, l3_ref)):
            for j in range(lend_ref.shape[1]):
                lent_ref[j:j + 1, :] = out_ref[pl.ds(lend_ref[q, j], 1), :]
        if with_gram:
            anchor = anchor_ref[...]
            partial = gram_columns(((kept, anchor), (kept, kept), (image, anchor), (image, kept), (image, image)))
            for target in range(gram_ref.shape[0]):
                gram_ref[target] = partial


def apply_operator(jac_t, own, ghost_rows, cols_t, counts, lend_rows, anchor=None, peers=1):
    blocks, count, full = jac_t.shape
    width = own.shape[1]
    ghost = ghost_rows[0].shape[0]
    rows = min(ROWS_PER_STEP, count)
    with_gram = anchor is not None
    smem = pl.BlockSpec(memory_space=pltpu.SMEM)
    whole = pl.BlockSpec((count, width), lambda b: (0, 0))
    piece = pl.BlockSpec((ghost, width), lambda b: (0, 0))
    lent = lend_rows.shape[1]
    lent_spec = pl.BlockSpec((lent, width), lambda b: (0, 0))
    in_specs = [smem, smem, pl.BlockSpec((blocks, rows, full), lambda b: (0, b, 0)), whole, piece, piece, piece, piece,
                pl.BlockSpec((blocks, count), lambda b: (0, 0))]
    out_shape = [jax.ShapeDtypeStruct((count, width), jnp.float32)]
    out_shape += [jax.ShapeDtypeStruct((lent, width), jnp.float32)] * lend_rows.shape[0]
    out_shape += [jax.ShapeDtypeStruct((count, width), jnp.float32)]
    out_specs = [whole] + [lent_spec] * lend_rows.shape[0] + [whole]
    args = [counts, lend_rows, jac_t, own, *ghost_rows, cols_t]
    if with_gram:
        in_specs.append(whole)
        args.append(anchor)
        gram_count = 5 * VECS
        out_shape.append(jax.ShapeDtypeStruct((peers, VECS, gram_count), jnp.float32))
        out_specs.append(pl.BlockSpec((peers, VECS, gram_count), lambda b: (0, 0, 0)))
    return pl.pallas_call(
        functools.partial(coupling_kernel, with_gram),
        out_shape=tuple(out_shape),
        grid=(count // rows,),
        in_specs=in_specs,
        out_specs=tuple(out_specs),
        scratch_shapes=[
            pltpu.VMEM((count + 4 * ghost, 3 * width), jnp.bfloat16),
            pltpu.VMEM((blocks, count, width), jnp.float32),
            pltpu.VMEM((VECS, count, full), jnp.float32),
            pltpu.VMEM((2 * VECS, count, full), jnp.bfloat16),
        ],
        compiler_params=pltpu.CompilerParams(dimension_semantics=("arbitrary",)),
        cost_estimate=pl.CostEstimate(
            flops=2 * blocks * count * full * VECS + 2 * 2 * VECS * count * full * BLK,
            bytes_accessed=4 * (blocks * count * full + 6 * count * width),
            transcendentals=0,
        ),
    )(*args)


def mixing_kernel(mix_ref, anchor_ref, first_ref, second_ref, correction_ref, residual_ref):
    width = anchor_ref.shape[1]
    segment = lax.broadcasted_iota(jnp.int32, (1, width), 1) // BLK

    def weights(row_offset, shift):
        out = jnp.zeros((1, width), jnp.float32)
        for d in range(VECS):
            out = jnp.where(segment == d, mix_ref[row_offset + (d - shift) % VECS, d], out)
        return out

    def mixed(values, row_offset):
        total = None
        for shift in range(VECS):
            moved = values if shift == 0 else pltpu.roll(values, shift * BLK, 1)
            term = moved * weights(row_offset, shift)
            total = term if total is None else total + term
        return total

    anchor = anchor_ref[...]
    first = first_ref[...]
    second = second_ref[...]
    correction_ref[...] = mixed(anchor, 0) + mixed(first, VECS)
    residual_ref[...] = anchor - (mixed(first, 0) + mixed(second, VECS))


def mix_outputs(coefficients, anchor, first, second):
    whole = pl.BlockSpec(memory_space=pltpu.VMEM)
    return pl.pallas_call(
        mixing_kernel,
        out_shape=(jax.ShapeDtypeStruct(anchor.shape, jnp.float32),) * 2,
        in_specs=[pl.BlockSpec(memory_space=pltpu.SMEM), whole, whole, whole],
        out_specs=(whole, whole),
    )(coefficients, anchor, first, second)


def per_device(start_block, jacobian, counts, columns, send_list):
    lend_rows = send_list[0]
    jac_t = jnp.transpose(jacobian, (1, 0, 2))

    def ghosts(outgoing):
        wide, narrow = lax.axis_size("wide"), lax.axis_size("narrow")
        return (
            lax.ppermute(outgoing[0], "wide", [(i, i + 1) for i in range(wide - 1)]),
            lax.ppermute(outgoing[1], "wide", [(i + 1, i) for i in range(wide - 1)]),
            lax.ppermute(outgoing[2], "narrow", [(i, i + 1) for i in range(narrow - 1)]),
            lax.ppermute(outgoing[3], "narrow", [(i + 1, i) for i in range(narrow - 1)]),
        )

    cols_t = jnp.transpose(columns, (1, 0))
    first = apply_operator(jac_t, start_block, ghosts(start_block[lend_rows]), cols_t, counts, lend_rows)
    first_image, first_lent, anchor = first[0], jnp.stack(first[1:5]), first[5]
    peers = lax.axis_size("wide") * lax.axis_size("narrow")
    second = apply_operator(jac_t, first_image, ghosts(first_lent), cols_t, counts, lend_rows, anchor, peers)
    second_image, raw_gram = second[0], second[6]
    everyone = lax.all_to_all(raw_gram, ("wide", "narrow"), 0, 0, tiled=True)
    raw_gram = jnp.transpose(jnp.sum(everyone, axis=0), (1, 0)).reshape(5, VECS, VECS)
    shift = np.arange(VECS)[:, None, None]
    row_c = np.arange(VECS)[None, :, None]
    col_d = np.arange(VECS)[None, None, :]
    pick = jnp.asarray(((row_c - col_d) % VECS == shift).astype(np.float32))
    gram_parts = jnp.sum(raw_gram[:, :, :, None] * pick[None], axis=1)
    normal_matrix = jnp.concatenate(
        [
            jnp.concatenate([gram_parts[1], gram_parts[3].T], 1),
            jnp.concatenate([gram_parts[3], gram_parts[4]], 1),
        ],
        0,
    )
    right_terms = jnp.concatenate([gram_parts[0], gram_parts[2]], 0)
    factor = jnp.linalg.cholesky(normal_matrix)
    coefficients = jax.scipy.linalg.cho_solve((factor, True), right_terms)
    return mix_outputs(coefficients, anchor, first_image, second_image)


def solution(mesh):
    placed = (
        P(("wide", "narrow"), None),
        P(("wide", "narrow"), None, None),
        P(("wide", "narrow")),
        P(("wide", "narrow"), None),
        P(("wide", "narrow"), None, None),
    )
    return jax.shard_map(
        per_device,
        mesh=mesh,
        in_specs=placed,
        out_specs=(P(("wide", "narrow"), None), P(("wide", "narrow"), None)),
        check_vma=False,
    )
```

```python
import functools

import jax
import jax.numpy as jnp
import numpy as np
from jax import lax
from jax.experimental import pallas as pl
from jax.experimental.pallas import tpu as pltpu
from jax.sharding import PartitionSpec as P

BLK = 64
VECS = 4
NB = 5
E_DEV = 128
LANES = 128
SUBLANES = 8
UNROLL = 4
ROWS_PER_STEP = 32


DIAG_SHIFT = 1.5


def padded(cells, sides, width):
    for axis, dim in sides:
        count = lax.axis_size(axis)
        ends = count - 1
        head = lax.slice_in_dim(cells, 0, width, axis=dim)
        tail = lax.slice_in_dim(cells, cells.shape[dim] - width, cells.shape[dim], axis=dim)
        cells = jnp.concatenate(
            [
                lax.ppermute(tail, axis, [(i, (i + 1) % count) for i in range(ends)]),
                cells,
                lax.ppermute(head, axis, [((i + 1) % count, i) for i in range(ends)]),
            ],
            axis=dim,
        )
    return cells


def combine(values, mixing):
    shaped = values.reshape(values.shape[0], VECS, BLK)
    return jnp.einsum("eci,cd->edi", shaped, mixing, precision=lax.Precision.HIGHEST).reshape(
        values.shape[0], VECS * BLK
    )


def inner_block(left_side, right_side):
    left_shaped = left_side.reshape(left_side.shape[0], VECS, BLK)
    right_shaped = right_side.reshape(right_side.shape[0], VECS, BLK)
    return jnp.einsum("eci,edi->cd", left_shaped, right_shaped, precision=lax.Precision.HIGHEST)


def tree_sum(values, axes):
    for axis in axes:
        count = lax.axis_size(axis)
        if count & (count - 1):
            values = lax.psum(values, axis)
            continue
        stride = 1
        while stride < count:
            values = values + lax.ppermute(values, axis, [(i, i ^ stride) for i in range(count)])
            stride *= 2
    return values


def split_three(values):
    high = values.astype(jnp.bfloat16)
    rest = values - high.astype(jnp.float32)
    middle = rest.astype(jnp.bfloat16)
    low = (rest - middle.astype(jnp.float32)).astype(jnp.bfloat16)
    return jnp.concatenate([high, middle, low], axis=1)


def exchange_sum(values, axes):
    count = 1
    for axis in axes:
        count *= lax.axis_size(axis)
    flat = values.reshape(1, -1)
    everyone = lax.all_to_all(jnp.broadcast_to(flat, (count, flat.shape[1])), axes, 0, 0, tiled=True)
    return jnp.sum(everyone, axis=0).reshape(values.shape)


def segment_sums(values, segments):
    width = values.shape[1]
    seg = (
        lax.broadcasted_iota(jnp.int32, (width, segments), 0) // (width // segments)
        == lax.broadcasted_iota(jnp.int32, (width, segments), 1)
    ).astype(jnp.bfloat16)
    parts = split_three(values)
    return (
        jnp.dot(parts[:, 0:width], seg, preferred_element_type=jnp.float32)
        + jnp.dot(parts[:, width:2 * width], seg, preferred_element_type=jnp.float32)
        + jnp.dot(parts[:, 2 * width:3 * width], seg, preferred_element_type=jnp.float32)
    )


def gram_columns(pairs):
    rows = []
    for left, right in pairs:
        for shift in range(VECS):
            moved = right if shift == 0 else pltpu.roll(right, shift * BLK, 1)
            rows.append(jnp.sum(left * moved, axis=0, keepdims=True))
    stacked = jnp.concatenate(rows, axis=0)
    width = stacked.shape[1]
    seg = (
        lax.broadcasted_iota(jnp.int32, (VECS, width), 1) // BLK
        == lax.broadcasted_iota(jnp.int32, (VECS, width), 0)
    ).astype(jnp.bfloat16)
    parts = split_three(stacked)
    dims = (((1,), (1,)), ((), ()))
    return sum(
        lax.dot_general(seg, parts[:, p * width:(p + 1) * width], dims, preferred_element_type=jnp.float32)
        for p in range(3)
    )


def coupling_kernel(with_gram, count_ref, lend_ref, jac_ref, own_ref, g0_ref, g1_ref, g2_ref, g3_ref, cols_ref, *rest):
    if with_gram:
        anchor_ref, rest = rest[0], rest[1:]
    out_ref, l0_ref, l1_ref, l2_ref, l3_ref, kept_ref = rest[:6]
    rest = rest[6:]
    if with_gram:
        gram_ref, rest = rest[0], rest[1:]
    source_ref, picked_ref, z_ref, parts_ref = rest
    step = pl.program_id(0)
    rows = jac_ref.shape[1]
    tiles = jac_ref.shape[2] // LANES
    count = own_ref.shape[0]
    width = own_ref.shape[1]
    ghost = g0_ref.shape[0]
    row0 = pl.multiple_of(step * rows, rows)

    @pl.when(step == 0)
    def _():
        living = lax.broadcasted_iota(jnp.int32, (count, 1), 0) < count_ref[0]
        source_ref[0:count] = split_three(jnp.where(living, own_ref[...], jnp.float32(0.0)))
        for q, piece in enumerate((g0_ref, g1_ref, g2_ref, g3_ref)):
            source_ref[count + q * ghost:count + (q + 1) * ghost] = split_three(piece[...])
        slots = lax.broadcasted_iota(jnp.int32, (source_ref.shape[0], count), 0)
        for k in range(NB):
            chosen = (cols_ref[k:k + 1, :] == slots).astype(jnp.bfloat16)
            spread = lax.dot_general(
                chosen, source_ref[...], (((0,), (0,)), ((), ())), preferred_element_type=jnp.float32
            )
            picked_ref[k] = spread[:, 0:width] + spread[:, width:2 * width] + spread[:, 2 * width:3 * width]

    lane = lax.broadcasted_iota(jnp.int32, (SUBLANES, LANES), 1)
    for group in range(rows // SUBLANES):
        top = group * SUBLANES
        first_row = pl.multiple_of(row0 + top, SUBLANES)
        doubled = []
        for k in range(NB):
            per_vector = []
            for pair in range(VECS // 2):
                tile = picked_ref[k, pl.ds(first_row, SUBLANES), pair * LANES:(pair + 1) * LANES]
                swapped = pltpu.roll(tile, BLK, 1)
                per_vector.append(jnp.where(lane < BLK, tile, swapped))
                per_vector.append(jnp.where(lane >= BLK, tile, swapped))
            doubled.append(per_vector)

        def one_tile(t, carry):
            off = pl.multiple_of(t * LANES, LANES)
            blocks = [jac_ref[k, top:top + SUBLANES, pl.ds(off, LANES)] for k in range(NB)]
            for c in range(VECS):
                terms = [blocks[k] * doubled[k][c] for k in range(NB)]
                while len(terms) > 1:
                    terms = [terms[i] + terms[i + 1] for i in range(0, len(terms) - 1, 2)] + (
                        [terms[-1]] if len(terms) % 2 else []
                    )
                z_ref[c, pl.ds(first_row, SUBLANES), pl.ds(off, LANES)] = terms[0]
            return carry

        lax.fori_loop(0, tiles, one_tile, 0, unroll=UNROLL)

    @pl.when(step == pl.num_programs(0) - 1)
    def _():
        full = tiles * LANES
        for c in range(VECS):
            total = z_ref[c]
            high = total.astype(jnp.bfloat16)
            parts_ref[2 * c] = high
            parts_ref[2 * c + 1] = (total - high.astype(jnp.float32)).astype(jnp.bfloat16)
        flat = parts_ref[...].reshape(2 * VECS * count, full)
        seg = (
            lax.broadcasted_iota(jnp.int32, (full, BLK), 0) // BLK
            == lax.broadcasted_iota(jnp.int32, (full, BLK), 1)
        ).astype(jnp.bfloat16)
        sums = jnp.dot(flat, seg, preferred_element_type=jnp.float32)
        coupled = jnp.concatenate(
            [sums[(2 * c) * count:(2 * c + 1) * count] + sums[(2 * c + 1) * count:(2 * c + 2) * count] for c in range(VECS)],
            axis=1,
        )
        own = own_ref[...]
        living = lax.broadcasted_iota(jnp.int32, (count, 1), 0) < count_ref[0]
        image = jnp.where(living, DIAG_SHIFT * own + coupled, jnp.float32(0.0))
        out_ref[...] = image
        kept = jnp.where(living, own, jnp.float32(0.0))
        kept_ref[...] = kept
        for q, lent_ref in enumerate((l0_ref, l1_ref, l2_ref, l3_ref)):
            for j in range(lend_ref.shape[1]):
                lent_ref[j:j + 1, :] = out_ref[pl.ds(lend_ref[q, j], 1), :]
        if with_gram:
            anchor = anchor_ref[...]
            partial = gram_columns(((kept, anchor), (kept, kept), (image, anchor), (image, kept), (image, image)))
            for target in range(gram_ref.shape[0]):
                gram_ref[target] = partial


def apply_operator(jac_t, own, ghost_rows, cols_t, counts, lend_rows, anchor=None, peers=1):
    blocks, count, full = jac_t.shape
    width = own.shape[1]
    ghost = ghost_rows[0].shape[0]
    rows = min(ROWS_PER_STEP, count)
    with_gram = anchor is not None
    smem = pl.BlockSpec(memory_space=pltpu.SMEM)
    whole = pl.BlockSpec((count, width), lambda b: (0, 0))
    piece = pl.BlockSpec((ghost, width), lambda b: (0, 0))
    lent = lend_rows.shape[1]
    lent_spec = pl.BlockSpec((lent, width), lambda b: (0, 0))
    in_specs = [smem, smem, pl.BlockSpec((blocks, rows, full), lambda b: (0, b, 0)), whole, piece, piece, piece, piece,
                pl.BlockSpec((blocks, count), lambda b: (0, 0))]
    out_shape = [jax.ShapeDtypeStruct((count, width), jnp.float32)]
    out_shape += [jax.ShapeDtypeStruct((lent, width), jnp.float32)] * lend_rows.shape[0]
    out_shape += [jax.ShapeDtypeStruct((count, width), jnp.float32)]
    out_specs = [whole] + [lent_spec] * lend_rows.shape[0] + [whole]
    args = [counts, lend_rows, jac_t, own, *ghost_rows, cols_t]
    if with_gram:
        in_specs.append(whole)
        args.append(anchor)
        gram_count = 5 * VECS
        out_shape.append(jax.ShapeDtypeStruct((peers, VECS, gram_count), jnp.float32))
        out_specs.append(pl.BlockSpec((peers, VECS, gram_count), lambda b: (0, 0, 0)))
    return pl.pallas_call(
        functools.partial(coupling_kernel, with_gram),
        out_shape=tuple(out_shape),
        grid=(count // rows,),
        in_specs=in_specs,
        out_specs=tuple(out_specs),
        scratch_shapes=[
            pltpu.VMEM((count + 4 * ghost, 3 * width), jnp.bfloat16),
            pltpu.VMEM((blocks, count, width), jnp.float32),
            pltpu.VMEM((VECS, count, full), jnp.float32),
            pltpu.VMEM((2 * VECS, count, full), jnp.bfloat16),
        ],
        compiler_params=pltpu.CompilerParams(dimension_semantics=("arbitrary",)),
        cost_estimate=pl.CostEstimate(
            flops=2 * blocks * count * full * VECS + 2 * 2 * VECS * count * full * BLK,
            bytes_accessed=4 * (blocks * count * full + 6 * count * width),
            transcendentals=0,
        ),
    )(*args)


def lending_kernel(lend_ref, values_ref, *lent_refs):
    for q, lent_ref in enumerate(lent_refs):
        for j in range(lend_ref.shape[1]):
            lent_ref[j:j + 1, :] = values_ref[pl.ds(lend_ref[q, j], 1), :]


def lent_rows_of(values, lend_rows):
    shape = jax.ShapeDtypeStruct((lend_rows.shape[1], values.shape[1]), values.dtype)
    whole = pl.BlockSpec(memory_space=pltpu.VMEM)
    return pl.pallas_call(
        lending_kernel,
        out_shape=(shape,) * lend_rows.shape[0],
        in_specs=[pl.BlockSpec(memory_space=pltpu.SMEM), whole],
        out_specs=(whole,) * lend_rows.shape[0],
    )(lend_rows, values)


def mixing_kernel(mix_ref, anchor_ref, first_ref, second_ref, correction_ref, residual_ref):
    width = anchor_ref.shape[1]
    segment = lax.broadcasted_iota(jnp.int32, (1, width), 1) // BLK

    def weights(row_offset, shift):
        out = jnp.zeros((1, width), jnp.float32)
        for d in range(VECS):
            out = jnp.where(segment == d, mix_ref[row_offset + (d - shift) % VECS, d], out)
        return out

    def mixed(values, row_offset):
        total = None
        for shift in range(VECS):
            moved = values if shift == 0 else pltpu.roll(values, shift * BLK, 1)
            term = moved * weights(row_offset, shift)
            total = term if total is None else total + term
        return total

    anchor = anchor_ref[...]
    first = first_ref[...]
    second = second_ref[...]
    correction_ref[...] = mixed(anchor, 0) + mixed(first, VECS)
    residual_ref[...] = anchor - (mixed(first, 0) + mixed(second, VECS))


def mix_outputs(coefficients, anchor, first, second):
    whole = pl.BlockSpec(memory_space=pltpu.VMEM)
    return pl.pallas_call(
        mixing_kernel,
        out_shape=(jax.ShapeDtypeStruct(anchor.shape, jnp.float32),) * 2,
        in_specs=[pl.BlockSpec(memory_space=pltpu.SMEM), whole, whole, whole],
        out_specs=(whole, whole),
    )(coefficients, anchor, first, second)


def per_device(start_block, jacobian, counts, columns, send_list):
    lend_rows = send_list[0]
    jac_t = jnp.transpose(jacobian, (1, 0, 2))

    def ghosts(outgoing):
        wide, narrow = lax.axis_size("wide"), lax.axis_size("narrow")
        return (
            lax.ppermute(outgoing[0], "wide", [(i, i + 1) for i in range(wide - 1)]),
            lax.ppermute(outgoing[1], "wide", [(i + 1, i) for i in range(wide - 1)]),
            lax.ppermute(outgoing[2], "narrow", [(i, i + 1) for i in range(narrow - 1)]),
            lax.ppermute(outgoing[3], "narrow", [(i + 1, i) for i in range(narrow - 1)]),
        )

    cols_t = jnp.transpose(columns, (1, 0))
    first = apply_operator(jac_t, start_block, ghosts(lent_rows_of(start_block, lend_rows)), cols_t, counts, lend_rows)
    first_image, first_lent, anchor = first[0], jnp.stack(first[1:5]), first[5]
    peers = lax.axis_size("wide") * lax.axis_size("narrow")
    second = apply_operator(jac_t, first_image, ghosts(first_lent), cols_t, counts, lend_rows, anchor, peers)
    second_image, raw_gram = second[0], second[6]
    everyone = lax.all_to_all(raw_gram, ("wide", "narrow"), 0, 0, tiled=True)
    raw_gram = jnp.transpose(jnp.sum(everyone, axis=0), (1, 0)).reshape(5, VECS, VECS)
    shift = np.arange(VECS)[:, None, None]
    row_c = np.arange(VECS)[None, :, None]
    col_d = np.arange(VECS)[None, None, :]
    pick = jnp.asarray(((row_c - col_d) % VECS == shift).astype(np.float32))
    gram_parts = jnp.sum(raw_gram[:, :, :, None] * pick[None], axis=1)
    normal_matrix = jnp.concatenate(
        [
            jnp.concatenate([gram_parts[1], gram_parts[3].T], 1),
            jnp.concatenate([gram_parts[3], gram_parts[4]], 1),
        ],
        0,
    )
    right_terms = jnp.concatenate([gram_parts[0], gram_parts[2]], 0)
    factor = jnp.linalg.cholesky(normal_matrix)
    coefficients = jax.scipy.linalg.cho_solve((factor, True), right_terms)
    return mix_outputs(coefficients, anchor, first_image, second_image)


def solution(mesh):
    placed = (
        P(("wide", "narrow"), None),
        P(("wide", "narrow"), None, None),
        P(("wide", "narrow")),
        P(("wide", "narrow"), None),
        P(("wide", "narrow"), None, None),
    )
    return jax.shard_map(
        per_device,
        mesh=mesh,
        in_specs=placed,
        out_specs=(P(("wide", "narrow"), None), P(("wide", "narrow"), None)),
        check_vma=False,
    )
```

```python
import functools

import jax
import jax.numpy as jnp
import numpy as np
from jax import lax
from jax.experimental import pallas as pl
from jax.experimental.pallas import tpu as pltpu
from jax.sharding import PartitionSpec as P

BLK = 64
VECS = 4
NB = 5
E_DEV = 128
LANES = 128
SUBLANES = 8
UNROLL = 4
CHUNK_ROWS = 16
ROWS_PER_STEP = 32


DIAG_SHIFT = 1.5


def padded(cells, sides, width):
    for axis, dim in sides:
        count = lax.axis_size(axis)
        ends = count - 1
        head = lax.slice_in_dim(cells, 0, width, axis=dim)
        tail = lax.slice_in_dim(cells, cells.shape[dim] - width, cells.shape[dim], axis=dim)
        cells = jnp.concatenate(
            [
                lax.ppermute(tail, axis, [(i, (i + 1) % count) for i in range(ends)]),
                cells,
                lax.ppermute(head, axis, [((i + 1) % count, i) for i in range(ends)]),
            ],
            axis=dim,
        )
    return cells


def combine(values, mixing):
    shaped = values.reshape(values.shape[0], VECS, BLK)
    return jnp.einsum("eci,cd->edi", shaped, mixing, precision=lax.Precision.HIGHEST).reshape(
        values.shape[0], VECS * BLK
    )


def inner_block(left_side, right_side):
    left_shaped = left_side.reshape(left_side.shape[0], VECS, BLK)
    right_shaped = right_side.reshape(right_side.shape[0], VECS, BLK)
    return jnp.einsum("eci,edi->cd", left_shaped, right_shaped, precision=lax.Precision.HIGHEST)


def tree_sum(values, axes):
    for axis in axes:
        count = lax.axis_size(axis)
        if count & (count - 1):
            values = lax.psum(values, axis)
            continue
        stride = 1
        while stride < count:
            values = values + lax.ppermute(values, axis, [(i, i ^ stride) for i in range(count)])
            stride *= 2
    return values


def split_three(values):
    high = values.astype(jnp.bfloat16)
    rest = values - high.astype(jnp.float32)
    middle = rest.astype(jnp.bfloat16)
    low = (rest - middle.astype(jnp.float32)).astype(jnp.bfloat16)
    return jnp.concatenate([high, middle, low], axis=1)


def exchange_sum(values, axes):
    count = 1
    for axis in axes:
        count *= lax.axis_size(axis)
    flat = values.reshape(1, -1)
    everyone = lax.all_to_all(jnp.broadcast_to(flat, (count, flat.shape[1])), axes, 0, 0, tiled=True)
    return jnp.sum(everyone, axis=0).reshape(values.shape)


def segment_sums(values, segments):
    width = values.shape[1]
    seg = (
        lax.broadcasted_iota(jnp.int32, (width, segments), 0) // (width // segments)
        == lax.broadcasted_iota(jnp.int32, (width, segments), 1)
    ).astype(jnp.bfloat16)
    parts = split_three(values)
    return (
        jnp.dot(parts[:, 0:width], seg, preferred_element_type=jnp.float32)
        + jnp.dot(parts[:, width:2 * width], seg, preferred_element_type=jnp.float32)
        + jnp.dot(parts[:, 2 * width:3 * width], seg, preferred_element_type=jnp.float32)
    )


def gram_columns(pairs):
    rows = []
    for left, right in pairs:
        for shift in range(VECS):
            moved = right if shift == 0 else pltpu.roll(right, shift * BLK, 1)
            rows.append(jnp.sum(left * moved, axis=0, keepdims=True))
    stacked = jnp.concatenate(rows, axis=0)
    width = stacked.shape[1]
    seg = (
        lax.broadcasted_iota(jnp.int32, (VECS, width), 1) // BLK
        == lax.broadcasted_iota(jnp.int32, (VECS, width), 0)
    ).astype(jnp.bfloat16)
    parts = split_three(stacked)
    dims = (((1,), (1,)), ((), ()))
    return sum(
        lax.dot_general(seg, parts[:, p * width:(p + 1) * width], dims, preferred_element_type=jnp.float32)
        for p in range(3)
    )


def coupling_kernel(with_gram, count_ref, lend_ref, jac_hbm, own_ref, g0_ref, g1_ref, g2_ref, g3_ref, cols_ref, *rest):
    if with_gram:
        anchor_ref, rest = rest[0], rest[1:]
    out_ref, l0_ref, l1_ref, l2_ref, l3_ref, kept_ref = rest[:6]
    rest = rest[6:]
    if with_gram:
        gram_ref, rest = rest[0], rest[1:]
    jac_ref, sems, source_ref, picked_ref, z_ref, parts_ref = rest
    tiles = jac_ref.shape[2] // LANES
    count = own_ref.shape[0]
    width = own_ref.shape[1]
    ghost = g0_ref.shape[0]
    chunks = sems.shape[0]
    chunk_rows = count // chunks

    def chunk_copy(b):
        rows = pl.ds(pl.multiple_of(b * chunk_rows, chunk_rows), chunk_rows)
        return pltpu.make_async_copy(jac_hbm.at[:, rows, :], jac_ref.at[:, rows, :], sems.at[b])

    for b in range(chunks):
        chunk_copy(b).start()

    living = lax.broadcasted_iota(jnp.int32, (count, 1), 0) < count_ref[0]
    source_ref[0:count] = split_three(jnp.where(living, own_ref[...], jnp.float32(0.0)))
    for q, piece in enumerate((g0_ref, g1_ref, g2_ref, g3_ref)):
        source_ref[count + q * ghost:count + (q + 1) * ghost] = split_three(piece[...])
    slots = lax.broadcasted_iota(jnp.int32, (source_ref.shape[0], count), 0)
    for k in range(NB):
        chosen = (cols_ref[k:k + 1, :] == slots).astype(jnp.bfloat16)
        spread = lax.dot_general(
            chosen, source_ref[...], (((0,), (0,)), ((), ())), preferred_element_type=jnp.float32
        )
        picked_ref[k] = spread[:, 0:width] + spread[:, width:2 * width] + spread[:, 2 * width:3 * width]

    lane = lax.broadcasted_iota(jnp.int32, (SUBLANES, LANES), 1)

    def one_chunk(b, carry):
        chunk_copy(b).wait()
        for group in range(chunk_rows // SUBLANES):
            first_row = pl.multiple_of(b * chunk_rows + group * SUBLANES, SUBLANES)
            doubled = []
            for k in range(NB):
                per_vector = []
                for pair in range(VECS // 2):
                    tile = picked_ref[k, pl.ds(first_row, SUBLANES), pair * LANES:(pair + 1) * LANES]
                    swapped = pltpu.roll(tile, BLK, 1)
                    per_vector.append(jnp.where(lane < BLK, tile, swapped))
                    per_vector.append(jnp.where(lane >= BLK, tile, swapped))
                doubled.append(per_vector)

            def one_tile(t, inner):
                off = pl.multiple_of(t * LANES, LANES)
                blocks = [jac_ref[k, pl.ds(first_row, SUBLANES), pl.ds(off, LANES)] for k in range(NB)]
                for c in range(VECS):
                    terms = [blocks[k] * doubled[k][c] for k in range(NB)]
                    while len(terms) > 1:
                        terms = [terms[i] + terms[i + 1] for i in range(0, len(terms) - 1, 2)] + (
                            [terms[-1]] if len(terms) % 2 else []
                        )
                    z_ref[c, pl.ds(first_row, SUBLANES), pl.ds(off, LANES)] = terms[0]
                return inner

            lax.fori_loop(0, tiles, one_tile, 0, unroll=UNROLL)
        return carry

    lax.fori_loop(0, chunks, one_chunk, 0)

    full = tiles * LANES
    for c in range(VECS):
        total = z_ref[c]
        high = total.astype(jnp.bfloat16)
        parts_ref[2 * c] = high
        parts_ref[2 * c + 1] = (total - high.astype(jnp.float32)).astype(jnp.bfloat16)
    flat = parts_ref[...].reshape(2 * VECS * count, full)
    seg = (
        lax.broadcasted_iota(jnp.int32, (full, BLK), 0) // BLK
        == lax.broadcasted_iota(jnp.int32, (full, BLK), 1)
    ).astype(jnp.bfloat16)
    sums = jnp.dot(flat, seg, preferred_element_type=jnp.float32)
    coupled = jnp.concatenate(
        [sums[(2 * c) * count:(2 * c + 1) * count] + sums[(2 * c + 1) * count:(2 * c + 2) * count] for c in range(VECS)],
        axis=1,
    )
    own = own_ref[...]
    image = jnp.where(living, DIAG_SHIFT * own + coupled, jnp.float32(0.0))
    out_ref[...] = image
    kept = jnp.where(living, own, jnp.float32(0.0))
    kept_ref[...] = kept
    for q, lent_ref in enumerate((l0_ref, l1_ref, l2_ref, l3_ref)):
        for j in range(lend_ref.shape[1]):
            lent_ref[j:j + 1, :] = out_ref[pl.ds(lend_ref[q, j], 1), :]
    if with_gram:
        anchor = anchor_ref[...]
        partial = gram_columns(((kept, anchor), (kept, kept), (image, anchor), (image, kept), (image, image)))
        for target in range(gram_ref.shape[0]):
            gram_ref[target] = partial


def apply_operator(jac_t, own, ghost_rows, cols_t, counts, lend_rows, anchor=None, peers=1):
    blocks, count, full = jac_t.shape
    width = own.shape[1]
    ghost = ghost_rows[0].shape[0]
    chunks = max(count // CHUNK_ROWS, 1)
    with_gram = anchor is not None
    smem = pl.BlockSpec(memory_space=pltpu.SMEM)
    vmem = pl.BlockSpec(memory_space=pltpu.VMEM)
    lent = lend_rows.shape[1]
    in_specs = [smem, smem, pl.BlockSpec(memory_space=pl.ANY), vmem, vmem, vmem, vmem, vmem, vmem]
    out_shape = [jax.ShapeDtypeStruct((count, width), jnp.float32)]
    out_shape += [jax.ShapeDtypeStruct((lent, width), jnp.float32)] * lend_rows.shape[0]
    out_shape += [jax.ShapeDtypeStruct((count, width), jnp.float32)]
    args = [counts, lend_rows, jac_t, own, *ghost_rows, cols_t]
    if with_gram:
        in_specs.append(vmem)
        args.append(anchor)
        out_shape.append(jax.ShapeDtypeStruct((peers, VECS, 5 * VECS), jnp.float32))
    return pl.pallas_call(
        functools.partial(coupling_kernel, with_gram),
        out_shape=tuple(out_shape),
        in_specs=in_specs,
        out_specs=tuple(vmem for _ in out_shape),
        scratch_shapes=[
            pltpu.VMEM((blocks, count, full), jnp.float32),
            pltpu.SemaphoreType.DMA((chunks,)),
            pltpu.VMEM((count + 4 * ghost, 3 * width), jnp.bfloat16),
            pltpu.VMEM((blocks, count, width), jnp.float32),
            pltpu.VMEM((VECS, count, full), jnp.float32),
            pltpu.VMEM((2 * VECS, count, full), jnp.bfloat16),
        ],
        cost_estimate=pl.CostEstimate(
            flops=2 * blocks * count * full * VECS + 2 * 2 * VECS * count * full * BLK,
            bytes_accessed=4 * (blocks * count * full + 6 * count * width),
            transcendentals=0,
        ),
    )(*args)


def lending_kernel(lend_ref, values_ref, *lent_refs):
    for q, lent_ref in enumerate(lent_refs):
        for j in range(lend_ref.shape[1]):
            lent_ref[j:j + 1, :] = values_ref[pl.ds(lend_ref[q, j], 1), :]


def lent_rows_of(values, lend_rows):
    shape = jax.ShapeDtypeStruct((lend_rows.shape[1], values.shape[1]), values.dtype)
    whole = pl.BlockSpec(memory_space=pltpu.VMEM)
    return pl.pallas_call(
        lending_kernel,
        out_shape=(shape,) * lend_rows.shape[0],
        in_specs=[pl.BlockSpec(memory_space=pltpu.SMEM), whole],
        out_specs=(whole,) * lend_rows.shape[0],
    )(lend_rows, values)


def mixing_kernel(mix_ref, anchor_ref, first_ref, second_ref, correction_ref, residual_ref):
    width = anchor_ref.shape[1]
    segment = lax.broadcasted_iota(jnp.int32, (1, width), 1) // BLK

    def weights(row_offset, shift):
        out = jnp.zeros((1, width), jnp.float32)
        for d in range(VECS):
            out = jnp.where(segment == d, mix_ref[row_offset + (d - shift) % VECS, d], out)
        return out

    def mixed(values, row_offset):
        total = None
        for shift in range(VECS):
            moved = values if shift == 0 else pltpu.roll(values, shift * BLK, 1)
            term = moved * weights(row_offset, shift)
            total = term if total is None else total + term
        return total

    anchor = anchor_ref[...]
    first = first_ref[...]
    second = second_ref[...]
    correction_ref[...] = mixed(anchor, 0) + mixed(first, VECS)
    residual_ref[...] = anchor - (mixed(first, 0) + mixed(second, VECS))


def mix_outputs(coefficients, anchor, first, second):
    whole = pl.BlockSpec(memory_space=pltpu.VMEM)
    return pl.pallas_call(
        mixing_kernel,
        out_shape=(jax.ShapeDtypeStruct(anchor.shape, jnp.float32),) * 2,
        in_specs=[pl.BlockSpec(memory_space=pltpu.SMEM), whole, whole, whole],
        out_specs=(whole, whole),
    )(coefficients, anchor, first, second)


def per_device(start_block, jacobian, counts, columns, send_list):
    lend_rows = send_list[0]
    jac_t = jnp.transpose(jacobian, (1, 0, 2))

    def ghosts(outgoing):
        wide, narrow = lax.axis_size("wide"), lax.axis_size("narrow")
        return (
            lax.ppermute(outgoing[0], "wide", [(i, i + 1) for i in range(wide - 1)]),
            lax.ppermute(outgoing[1], "wide", [(i + 1, i) for i in range(wide - 1)]),
            lax.ppermute(outgoing[2], "narrow", [(i, i + 1) for i in range(narrow - 1)]),
            lax.ppermute(outgoing[3], "narrow", [(i + 1, i) for i in range(narrow - 1)]),
        )

    cols_t = jnp.transpose(columns, (1, 0))
    first = apply_operator(jac_t, start_block, ghosts(lent_rows_of(start_block, lend_rows)), cols_t, counts, lend_rows)
    first_image, first_lent, anchor = first[0], jnp.stack(first[1:5]), first[5]
    peers = lax.axis_size("wide") * lax.axis_size("narrow")
    second = apply_operator(jac_t, first_image, ghosts(first_lent), cols_t, counts, lend_rows, anchor, peers)
    second_image, raw_gram = second[0], second[6]
    everyone = lax.all_to_all(raw_gram, ("wide", "narrow"), 0, 0, tiled=True)
    raw_gram = jnp.transpose(jnp.sum(everyone, axis=0), (1, 0)).reshape(5, VECS, VECS)
    shift = np.arange(VECS)[:, None, None]
    row_c = np.arange(VECS)[None, :, None]
    col_d = np.arange(VECS)[None, None, :]
    pick = jnp.asarray(((row_c - col_d) % VECS == shift).astype(np.float32))
    gram_parts = jnp.sum(raw_gram[:, :, :, None] * pick[None], axis=1)
    normal_matrix = jnp.concatenate(
        [
            jnp.concatenate([gram_parts[1], gram_parts[3].T], 1),
            jnp.concatenate([gram_parts[3], gram_parts[4]], 1),
        ],
        0,
    )
    right_terms = jnp.concatenate([gram_parts[0], gram_parts[2]], 0)
    factor = jnp.linalg.cholesky(normal_matrix)
    coefficients = jax.scipy.linalg.cho_solve((factor, True), right_terms)
    return mix_outputs(coefficients, anchor, first_image, second_image)


def solution(mesh):
    placed = (
        P(("wide", "narrow"), None),
        P(("wide", "narrow"), None, None),
        P(("wide", "narrow")),
        P(("wide", "narrow"), None),
        P(("wide", "narrow"), None, None),
    )
    return jax.shard_map(
        per_device,
        mesh=mesh,
        in_specs=placed,
        out_specs=(P(("wide", "narrow"), None), P(("wide", "narrow"), None)),
        check_vma=False,
    )
```

```python
import functools

import jax
import jax.numpy as jnp
import numpy as np
from jax import lax
from jax.experimental import pallas as pl
from jax.experimental.pallas import tpu as pltpu
from jax.sharding import PartitionSpec as P

BLK = 64
VECS = 4
NB = 5
E_DEV = 128
LANES = 128
SUBLANES = 8
UNROLL = 4
CHUNK_ROWS = 16
ROWS_PER_STEP = 32


DIAG_SHIFT = 1.5


def padded(cells, sides, width):
    for axis, dim in sides:
        count = lax.axis_size(axis)
        ends = count - 1
        head = lax.slice_in_dim(cells, 0, width, axis=dim)
        tail = lax.slice_in_dim(cells, cells.shape[dim] - width, cells.shape[dim], axis=dim)
        cells = jnp.concatenate(
            [
                lax.ppermute(tail, axis, [(i, (i + 1) % count) for i in range(ends)]),
                cells,
                lax.ppermute(head, axis, [((i + 1) % count, i) for i in range(ends)]),
            ],
            axis=dim,
        )
    return cells


def combine(values, mixing):
    shaped = values.reshape(values.shape[0], VECS, BLK)
    return jnp.einsum("eci,cd->edi", shaped, mixing, precision=lax.Precision.HIGHEST).reshape(
        values.shape[0], VECS * BLK
    )


def inner_block(left_side, right_side):
    left_shaped = left_side.reshape(left_side.shape[0], VECS, BLK)
    right_shaped = right_side.reshape(right_side.shape[0], VECS, BLK)
    return jnp.einsum("eci,edi->cd", left_shaped, right_shaped, precision=lax.Precision.HIGHEST)


def tree_sum(values, axes):
    for axis in axes:
        count = lax.axis_size(axis)
        if count & (count - 1):
            values = lax.psum(values, axis)
            continue
        stride = 1
        while stride < count:
            values = values + lax.ppermute(values, axis, [(i, i ^ stride) for i in range(count)])
            stride *= 2
    return values


def split_three(values):
    high = values.astype(jnp.bfloat16)
    rest = values - high.astype(jnp.float32)
    middle = rest.astype(jnp.bfloat16)
    low = (rest - middle.astype(jnp.float32)).astype(jnp.bfloat16)
    return jnp.concatenate([high, middle, low], axis=1)


def exchange_sum(values, axes):
    count = 1
    for axis in axes:
        count *= lax.axis_size(axis)
    flat = values.reshape(1, -1)
    everyone = lax.all_to_all(jnp.broadcast_to(flat, (count, flat.shape[1])), axes, 0, 0, tiled=True)
    return jnp.sum(everyone, axis=0).reshape(values.shape)


def segment_sums(values, segments):
    width = values.shape[1]
    seg = (
        lax.broadcasted_iota(jnp.int32, (width, segments), 0) // (width // segments)
        == lax.broadcasted_iota(jnp.int32, (width, segments), 1)
    ).astype(jnp.bfloat16)
    parts = split_three(values)
    return (
        jnp.dot(parts[:, 0:width], seg, preferred_element_type=jnp.float32)
        + jnp.dot(parts[:, width:2 * width], seg, preferred_element_type=jnp.float32)
        + jnp.dot(parts[:, 2 * width:3 * width], seg, preferred_element_type=jnp.float32)
    )


def gram_columns(pairs):
    rows = []
    for left, right in pairs:
        for shift in range(VECS):
            moved = right if shift == 0 else pltpu.roll(right, shift * BLK, 1)
            rows.append(jnp.sum(left * moved, axis=0, keepdims=True))
    stacked = jnp.concatenate(rows, axis=0)
    width = stacked.shape[1]
    seg = (
        lax.broadcasted_iota(jnp.int32, (VECS, width), 1) // BLK
        == lax.broadcasted_iota(jnp.int32, (VECS, width), 0)
    ).astype(jnp.bfloat16)
    parts = split_three(stacked)
    dims = (((1,), (1,)), ((), ()))
    return sum(
        lax.dot_general(seg, parts[:, p * width:(p + 1) * width], dims, preferred_element_type=jnp.float32)
        for p in range(3)
    )


def gather_rows(values, index_row):
    width = values.shape[1]
    chosen = (index_row == lax.broadcasted_iota(jnp.int32, (values.shape[0], index_row.shape[1]), 0)).astype(jnp.bfloat16)
    spread = lax.dot_general(
        chosen, split_three(values), (((0,), (0,)), ((), ())), preferred_element_type=jnp.float32
    )
    return spread[:, 0:width] + spread[:, width:2 * width] + spread[:, 2 * width:3 * width]


def coupling_kernel(with_gram, count_ref, lend_ref, jac_hbm, own_ref, g0_ref, g1_ref, g2_ref, g3_ref, cols_ref, *rest):
    if with_gram:
        anchor_ref, rest = rest[0], rest[1:]
    out_ref, l0_ref, l1_ref, l2_ref, l3_ref, kept_ref = rest[:6]
    rest = rest[6:]
    if with_gram:
        gram_ref, rest = rest[0], rest[1:]
    jac_ref, sems, source_ref, picked_ref, z_ref, parts_ref = rest
    tiles = jac_ref.shape[2] // LANES
    count = own_ref.shape[0]
    width = own_ref.shape[1]
    ghost = g0_ref.shape[0]
    chunks = sems.shape[0]
    chunk_rows = count // chunks

    def chunk_copy(b):
        rows = pl.ds(pl.multiple_of(b * chunk_rows, chunk_rows), chunk_rows)
        return pltpu.make_async_copy(jac_hbm.at[:, rows, :], jac_ref.at[:, rows, :], sems.at[b])

    for b in range(chunks):
        chunk_copy(b).start()

    living = lax.broadcasted_iota(jnp.int32, (count, 1), 0) < count_ref[0]
    source_ref[0:count] = split_three(jnp.where(living, own_ref[...], jnp.float32(0.0)))
    for q, piece in enumerate((g0_ref, g1_ref, g2_ref, g3_ref)):
        source_ref[count + q * ghost:count + (q + 1) * ghost] = split_three(piece[...])
    slots = lax.broadcasted_iota(jnp.int32, (source_ref.shape[0], count), 0)
    for k in range(NB):
        chosen = (cols_ref[k:k + 1, :] == slots).astype(jnp.bfloat16)
        spread = lax.dot_general(
            chosen, source_ref[...], (((0,), (0,)), ((), ())), preferred_element_type=jnp.float32
        )
        picked_ref[k] = spread[:, 0:width] + spread[:, width:2 * width] + spread[:, 2 * width:3 * width]

    lane = lax.broadcasted_iota(jnp.int32, (SUBLANES, LANES), 1)

    def one_chunk(b, carry):
        chunk_copy(b).wait()
        for group in range(chunk_rows // SUBLANES):
            first_row = pl.multiple_of(b * chunk_rows + group * SUBLANES, SUBLANES)
            doubled = []
            for k in range(NB):
                per_vector = []
                for pair in range(VECS // 2):
                    tile = picked_ref[k, pl.ds(first_row, SUBLANES), pair * LANES:(pair + 1) * LANES]
                    swapped = pltpu.roll(tile, BLK, 1)
                    per_vector.append(jnp.where(lane < BLK, tile, swapped))
                    per_vector.append(jnp.where(lane >= BLK, tile, swapped))
                doubled.append(per_vector)

            def one_tile(t, inner):
                off = pl.multiple_of(t * LANES, LANES)
                blocks = [jac_ref[k, pl.ds(first_row, SUBLANES), pl.ds(off, LANES)] for k in range(NB)]
                for c in range(VECS):
                    terms = [blocks[k] * doubled[k][c] for k in range(NB)]
                    while len(terms) > 1:
                        terms = [terms[i] + terms[i + 1] for i in range(0, len(terms) - 1, 2)] + (
                            [terms[-1]] if len(terms) % 2 else []
                        )
                    z_ref[c, pl.ds(first_row, SUBLANES), pl.ds(off, LANES)] = terms[0]
                return inner

            lax.fori_loop(0, tiles, one_tile, 0, unroll=UNROLL)
        return carry

    lax.fori_loop(0, chunks, one_chunk, 0)

    full = tiles * LANES
    for c in range(VECS):
        total = z_ref[c]
        high = total.astype(jnp.bfloat16)
        parts_ref[2 * c] = high
        parts_ref[2 * c + 1] = (total - high.astype(jnp.float32)).astype(jnp.bfloat16)
    flat = parts_ref[...].reshape(2 * VECS * count, full)
    seg = (
        lax.broadcasted_iota(jnp.int32, (full, BLK), 0) // BLK
        == lax.broadcasted_iota(jnp.int32, (full, BLK), 1)
    ).astype(jnp.bfloat16)
    sums = jnp.dot(flat, seg, preferred_element_type=jnp.float32)
    coupled = jnp.concatenate(
        [sums[(2 * c) * count:(2 * c + 1) * count] + sums[(2 * c + 1) * count:(2 * c + 2) * count] for c in range(VECS)],
        axis=1,
    )
    own = own_ref[...]
    image = jnp.where(living, DIAG_SHIFT * own + coupled, jnp.float32(0.0))
    out_ref[...] = image
    kept = jnp.where(living, own, jnp.float32(0.0))
    kept_ref[...] = kept
    lent = gather_rows(image, lend_ref[...])
    for q, lent_ref in enumerate((l0_ref, l1_ref, l2_ref, l3_ref)):
        lent_ref[...] = lent[q * ghost:(q + 1) * ghost]
    if with_gram:
        anchor = anchor_ref[...]
        partial = gram_columns(((kept, anchor), (kept, kept), (image, anchor), (image, kept), (image, image)))
        for target in range(gram_ref.shape[0]):
            gram_ref[target] = partial


def apply_operator(jac_t, own, ghost_rows, cols_t, counts, lend_rows, anchor=None, peers=1):
    blocks, count, full = jac_t.shape
    width = own.shape[1]
    ghost = ghost_rows[0].shape[0]
    chunks = max(count // CHUNK_ROWS, 1)
    with_gram = anchor is not None
    smem = pl.BlockSpec(memory_space=pltpu.SMEM)
    vmem = pl.BlockSpec(memory_space=pltpu.VMEM)
    in_specs = [smem, vmem, pl.BlockSpec(memory_space=pl.ANY), vmem, vmem, vmem, vmem, vmem, vmem]
    out_shape = [jax.ShapeDtypeStruct((count, width), jnp.float32)]
    out_shape += [jax.ShapeDtypeStruct((ghost, width), jnp.float32)] * len(ghost_rows)
    out_shape += [jax.ShapeDtypeStruct((count, width), jnp.float32)]
    args = [counts, lend_rows, jac_t, own, *ghost_rows, cols_t]
    if with_gram:
        in_specs.append(vmem)
        args.append(anchor)
        out_shape.append(jax.ShapeDtypeStruct((peers, VECS, 5 * VECS), jnp.float32))
    return pl.pallas_call(
        functools.partial(coupling_kernel, with_gram),
        out_shape=tuple(out_shape),
        in_specs=in_specs,
        out_specs=tuple(vmem for _ in out_shape),
        scratch_shapes=[
            pltpu.VMEM((blocks, count, full), jnp.float32),
            pltpu.SemaphoreType.DMA((chunks,)),
            pltpu.VMEM((count + 4 * ghost, 3 * width), jnp.bfloat16),
            pltpu.VMEM((blocks, count, width), jnp.float32),
            pltpu.VMEM((VECS, count, full), jnp.float32),
            pltpu.VMEM((2 * VECS, count, full), jnp.bfloat16),
        ],
        cost_estimate=pl.CostEstimate(
            flops=2 * blocks * count * full * VECS + 2 * 2 * VECS * count * full * BLK,
            bytes_accessed=4 * (blocks * count * full + 6 * count * width),
            transcendentals=0,
        ),
    )(*args)


def lending_kernel(count_ref, lend_ref, values_ref, *lent_refs):
    living = lax.broadcasted_iota(jnp.int32, (values_ref.shape[0], 1), 0) < count_ref[0]
    lent = gather_rows(jnp.where(living, values_ref[...], jnp.float32(0.0)), lend_ref[...])
    ghost = lent_refs[0].shape[0]
    for q, lent_ref in enumerate(lent_refs):
        lent_ref[...] = lent[q * ghost:(q + 1) * ghost]


def lent_rows_of(values, counts, lend_flat, ghost, directions):
    shape = jax.ShapeDtypeStruct((ghost, values.shape[1]), values.dtype)
    whole = pl.BlockSpec(memory_space=pltpu.VMEM)
    return pl.pallas_call(
        lending_kernel,
        out_shape=(shape,) * directions,
        in_specs=[pl.BlockSpec(memory_space=pltpu.SMEM), whole, whole],
        out_specs=(whole,) * directions,
    )(counts, lend_flat, values)


def mixing_kernel(mix_ref, anchor_ref, first_ref, second_ref, correction_ref, residual_ref):
    width = anchor_ref.shape[1]
    segment = lax.broadcasted_iota(jnp.int32, (1, width), 1) // BLK

    def weights(row_offset, shift):
        out = jnp.zeros((1, width), jnp.float32)
        for d in range(VECS):
            out = jnp.where(segment == d, mix_ref[row_offset + (d - shift) % VECS, d], out)
        return out

    def mixed(values, row_offset):
        total = None
        for shift in range(VECS):
            moved = values if shift == 0 else pltpu.roll(values, shift * BLK, 1)
            term = moved * weights(row_offset, shift)
            total = term if total is None else total + term
        return total

    anchor = anchor_ref[...]
    first = first_ref[...]
    second = second_ref[...]
    correction_ref[...] = mixed(anchor, 0) + mixed(first, VECS)
    residual_ref[...] = anchor - (mixed(first, 0) + mixed(second, VECS))


def mix_outputs(coefficients, anchor, first, second):
    whole = pl.BlockSpec(memory_space=pltpu.VMEM)
    return pl.pallas_call(
        mixing_kernel,
        out_shape=(jax.ShapeDtypeStruct(anchor.shape, jnp.float32),) * 2,
        in_specs=[pl.BlockSpec(memory_space=pltpu.SMEM), whole, whole, whole],
        out_specs=(whole, whole),
    )(coefficients, anchor, first, second)


def per_device(start_block, jacobian, counts, columns, send_list):
    jac_t = jnp.transpose(jacobian, (1, 0, 2))

    def ghosts(outgoing):
        wide, narrow = lax.axis_size("wide"), lax.axis_size("narrow")
        return (
            lax.ppermute(outgoing[0], "wide", [(i, i + 1) for i in range(wide - 1)]),
            lax.ppermute(outgoing[1], "wide", [(i + 1, i) for i in range(wide - 1)]),
            lax.ppermute(outgoing[2], "narrow", [(i, i + 1) for i in range(narrow - 1)]),
            lax.ppermute(outgoing[3], "narrow", [(i + 1, i) for i in range(narrow - 1)]),
        )

    cols_t = jnp.transpose(columns, (1, 0))
    directions, ghost = send_list.shape[1], send_list.shape[2]
    lend_flat = send_list.reshape(1, directions * ghost)
    first_lent = lent_rows_of(start_block, counts, lend_flat, ghost, directions)
    first = apply_operator(jac_t, start_block, ghosts(first_lent), cols_t, counts, lend_flat)
    first_image, first_lent, anchor = first[0], first[1:5], first[5]
    peers = lax.axis_size("wide") * lax.axis_size("narrow")
    second = apply_operator(jac_t, first_image, ghosts(first_lent), cols_t, counts, lend_flat, anchor, peers)
    second_image, raw_gram = second[0], second[6]
    everyone = lax.all_to_all(raw_gram, ("wide", "narrow"), 0, 0, tiled=True)
    raw_gram = jnp.transpose(jnp.sum(everyone, axis=0), (1, 0)).reshape(5, VECS, VECS)
    shift = np.arange(VECS)[:, None, None]
    row_c = np.arange(VECS)[None, :, None]
    col_d = np.arange(VECS)[None, None, :]
    pick = jnp.asarray(((row_c - col_d) % VECS == shift).astype(np.float32))
    gram_parts = jnp.sum(raw_gram[:, :, :, None] * pick[None], axis=1)
    normal_matrix = jnp.concatenate(
        [
            jnp.concatenate([gram_parts[1], gram_parts[3].T], 1),
            jnp.concatenate([gram_parts[3], gram_parts[4]], 1),
        ],
        0,
    )
    right_terms = jnp.concatenate([gram_parts[0], gram_parts[2]], 0)
    factor = jnp.linalg.cholesky(normal_matrix)
    coefficients = jax.scipy.linalg.cho_solve((factor, True), right_terms)
    return mix_outputs(coefficients, anchor, first_image, second_image)


def solution(mesh):
    placed = (
        P(("wide", "narrow"), None),
        P(("wide", "narrow"), None, None),
        P(("wide", "narrow")),
        P(("wide", "narrow"), None),
        P(("wide", "narrow"), None, None),
    )
    return jax.shard_map(
        per_device,
        mesh=mesh,
        in_specs=placed,
        out_specs=(P(("wide", "narrow"), None), P(("wide", "narrow"), None)),
        check_vma=False,
    )
```

```python
import functools

import jax
import jax.numpy as jnp
import numpy as np
from jax import lax
from jax.experimental import pallas as pl
from jax.experimental.pallas import tpu as pltpu
from jax.sharding import PartitionSpec as P

BLK = 64
VECS = 4
NB = 5
E_DEV = 128
LANES = 128
SUBLANES = 8
UNROLL = 4
CHUNK_ROWS = 16
ROWS_PER_STEP = 32


DIAG_SHIFT = 1.5


def padded(cells, sides, width):
    for axis, dim in sides:
        count = lax.axis_size(axis)
        ends = count - 1
        head = lax.slice_in_dim(cells, 0, width, axis=dim)
        tail = lax.slice_in_dim(cells, cells.shape[dim] - width, cells.shape[dim], axis=dim)
        cells = jnp.concatenate(
            [
                lax.ppermute(tail, axis, [(i, (i + 1) % count) for i in range(ends)]),
                cells,
                lax.ppermute(head, axis, [((i + 1) % count, i) for i in range(ends)]),
            ],
            axis=dim,
        )
    return cells


def combine(values, mixing):
    shaped = values.reshape(values.shape[0], VECS, BLK)
    return jnp.einsum("eci,cd->edi", shaped, mixing, precision=lax.Precision.HIGHEST).reshape(
        values.shape[0], VECS * BLK
    )


def inner_block(left_side, right_side):
    left_shaped = left_side.reshape(left_side.shape[0], VECS, BLK)
    right_shaped = right_side.reshape(right_side.shape[0], VECS, BLK)
    return jnp.einsum("eci,edi->cd", left_shaped, right_shaped, precision=lax.Precision.HIGHEST)


def tree_sum(values, axes):
    for axis in axes:
        count = lax.axis_size(axis)
        if count & (count - 1):
            values = lax.psum(values, axis)
            continue
        stride = 1
        while stride < count:
            values = values + lax.ppermute(values, axis, [(i, i ^ stride) for i in range(count)])
            stride *= 2
    return values


def split_three(values):
    high = values.astype(jnp.bfloat16)
    rest = values - high.astype(jnp.float32)
    middle = rest.astype(jnp.bfloat16)
    low = (rest - middle.astype(jnp.float32)).astype(jnp.bfloat16)
    return jnp.concatenate([high, middle, low], axis=1)


def exchange_sum(values, axes):
    count = 1
    for axis in axes:
        count *= lax.axis_size(axis)
    flat = values.reshape(1, -1)
    everyone = lax.all_to_all(jnp.broadcast_to(flat, (count, flat.shape[1])), axes, 0, 0, tiled=True)
    return jnp.sum(everyone, axis=0).reshape(values.shape)


def segment_sums(values, segments):
    width = values.shape[1]
    seg = (
        lax.broadcasted_iota(jnp.int32, (width, segments), 0) // (width // segments)
        == lax.broadcasted_iota(jnp.int32, (width, segments), 1)
    ).astype(jnp.bfloat16)
    parts = split_three(values)
    return (
        jnp.dot(parts[:, 0:width], seg, preferred_element_type=jnp.float32)
        + jnp.dot(parts[:, width:2 * width], seg, preferred_element_type=jnp.float32)
        + jnp.dot(parts[:, 2 * width:3 * width], seg, preferred_element_type=jnp.float32)
    )


def gram_columns(pairs):
    rows = []
    for left, right in pairs:
        for shift in range(VECS):
            moved = right if shift == 0 else pltpu.roll(right, shift * BLK, 1)
            rows.append(jnp.sum(left * moved, axis=0, keepdims=True))
    stacked = jnp.concatenate(rows, axis=0)
    width = stacked.shape[1]
    seg = (
        lax.broadcasted_iota(jnp.int32, (VECS, width), 1) // BLK
        == lax.broadcasted_iota(jnp.int32, (VECS, width), 0)
    ).astype(jnp.bfloat16)
    parts = split_three(stacked)
    dims = (((1,), (1,)), ((), ()))
    return sum(
        lax.dot_general(seg, parts[:, p * width:(p + 1) * width], dims, preferred_element_type=jnp.float32)
        for p in range(3)
    )


def coupling_kernel(with_gram, count_ref, lend_ref, jac_hbm, own_ref, g0_ref, g1_ref, g2_ref, g3_ref, cols_ref, *rest):
    if with_gram:
        anchor_ref, rest = rest[0], rest[1:]
    out_ref, l0_ref, l1_ref, l2_ref, l3_ref, kept_ref = rest[:6]
    rest = rest[6:]
    if with_gram:
        gram_ref, rest = rest[0], rest[1:]
    jac_ref, sems, source_ref, picked_ref, z_ref, parts_ref = rest
    tiles = jac_ref.shape[2] // LANES
    count = own_ref.shape[0]
    width = own_ref.shape[1]
    ghost = g0_ref.shape[0]
    chunks = sems.shape[0]
    chunk_rows = count // chunks

    def chunk_copy(b):
        rows = pl.ds(pl.multiple_of(b * chunk_rows, chunk_rows), chunk_rows)
        return pltpu.make_async_copy(jac_hbm.at[:, rows, :], jac_ref.at[:, rows, :], sems.at[b])

    for b in range(chunks):
        chunk_copy(b).start()

    living = lax.broadcasted_iota(jnp.int32, (count, 1), 0) < count_ref[0]
    source_ref[0:count] = split_three(jnp.where(living, own_ref[...], jnp.float32(0.0)))
    for q, piece in enumerate((g0_ref, g1_ref, g2_ref, g3_ref)):
        source_ref[count + q * ghost:count + (q + 1) * ghost] = split_three(piece[...])
    slots = lax.broadcasted_iota(jnp.int32, (source_ref.shape[0], count), 0)
    for k in range(NB):
        chosen = (cols_ref[k:k + 1, :] == slots).astype(jnp.bfloat16)
        spread = lax.dot_general(
            chosen, source_ref[...], (((0,), (0,)), ((), ())), preferred_element_type=jnp.float32
        )
        picked_ref[k] = spread[:, 0:width] + spread[:, width:2 * width] + spread[:, 2 * width:3 * width]

    lane = lax.broadcasted_iota(jnp.int32, (SUBLANES, LANES), 1)

    def one_chunk(b, carry):
        chunk_copy(b).wait()
        for group in range(chunk_rows // SUBLANES):
            first_row = pl.multiple_of(b * chunk_rows + group * SUBLANES, SUBLANES)
            doubled = []
            for k in range(NB):
                per_vector = []
                for pair in range(VECS // 2):
                    tile = picked_ref[k, pl.ds(first_row, SUBLANES), pair * LANES:(pair + 1) * LANES]
                    swapped = pltpu.roll(tile, BLK, 1)
                    per_vector.append(jnp.where(lane < BLK, tile, swapped))
                    per_vector.append(jnp.where(lane >= BLK, tile, swapped))
                doubled.append(per_vector)

            def one_tile(t, inner):
                off = pl.multiple_of(t * LANES, LANES)
                blocks = [jac_ref[k, pl.ds(first_row, SUBLANES), pl.ds(off, LANES)] for k in range(NB)]
                for c in range(VECS):
                    terms = [blocks[k] * doubled[k][c] for k in range(NB)]
                    while len(terms) > 1:
                        terms = [terms[i] + terms[i + 1] for i in range(0, len(terms) - 1, 2)] + (
                            [terms[-1]] if len(terms) % 2 else []
                        )
                    z_ref[c, pl.ds(first_row, SUBLANES), pl.ds(off, LANES)] = terms[0]
                return inner

            lax.fori_loop(0, tiles, one_tile, 0, unroll=UNROLL)
        return carry

    lax.fori_loop(0, chunks, one_chunk, 0)

    full = tiles * LANES
    for c in range(VECS):
        total = z_ref[c]
        high = total.astype(jnp.bfloat16)
        parts_ref[2 * c] = high
        parts_ref[2 * c + 1] = (total - high.astype(jnp.float32)).astype(jnp.bfloat16)
    flat = parts_ref[...].reshape(2 * VECS * count, full)
    seg = (
        lax.broadcasted_iota(jnp.int32, (full, BLK), 0) // BLK
        == lax.broadcasted_iota(jnp.int32, (full, BLK), 1)
    ).astype(jnp.bfloat16)
    sums = jnp.dot(flat, seg, preferred_element_type=jnp.float32)
    coupled = jnp.concatenate(
        [sums[(2 * c) * count:(2 * c + 1) * count] + sums[(2 * c + 1) * count:(2 * c + 2) * count] for c in range(VECS)],
        axis=1,
    )
    own = own_ref[...]
    image = jnp.where(living, DIAG_SHIFT * own + coupled, jnp.float32(0.0))
    out_ref[...] = image
    kept = jnp.where(living, own, jnp.float32(0.0))
    kept_ref[...] = kept
    for q, lent_ref in enumerate((l0_ref, l1_ref, l2_ref, l3_ref)):
        for j in range(lend_ref.shape[1]):
            lent_ref[j:j + 1, :] = out_ref[pl.ds(lend_ref[q, j], 1), :]
    if with_gram:
        anchor = anchor_ref[...]
        partial = gram_columns(((kept, anchor), (kept, kept), (image, anchor), (image, kept), (image, image)))
        for target in range(gram_ref.shape[0]):
            gram_ref[target] = partial


def apply_operator(jac_t, own, ghost_rows, cols_t, counts, lend_rows, anchor=None, peers=1):
    blocks, count, full = jac_t.shape
    width = own.shape[1]
    ghost = ghost_rows[0].shape[0]
    chunks = max(count // CHUNK_ROWS, 1)
    with_gram = anchor is not None
    smem = pl.BlockSpec(memory_space=pltpu.SMEM)
    vmem = pl.BlockSpec(memory_space=pltpu.VMEM)
    lent = lend_rows.shape[1]
    in_specs = [smem, smem, pl.BlockSpec(memory_space=pl.ANY), vmem, vmem, vmem, vmem, vmem, vmem]
    out_shape = [jax.ShapeDtypeStruct((count, width), jnp.float32)]
    out_shape += [jax.ShapeDtypeStruct((lent, width), jnp.float32)] * lend_rows.shape[0]
    out_shape += [jax.ShapeDtypeStruct((count, width), jnp.float32)]
    args = [counts, lend_rows, jac_t, own, *ghost_rows, cols_t]
    if with_gram:
        in_specs.append(vmem)
        args.append(anchor)
        out_shape.append(jax.ShapeDtypeStruct((peers, VECS, 5 * VECS), jnp.float32))
    return pl.pallas_call(
        functools.partial(coupling_kernel, with_gram),
        out_shape=tuple(out_shape),
        in_specs=in_specs,
        out_specs=tuple(vmem for _ in out_shape),
        scratch_shapes=[
            pltpu.VMEM((blocks, count, full), jnp.float32),
            pltpu.SemaphoreType.DMA((chunks,)),
            pltpu.VMEM((count + 4 * ghost, 3 * width), jnp.bfloat16),
            pltpu.VMEM((blocks, count, width), jnp.float32),
            pltpu.VMEM((VECS, count, full), jnp.float32),
            pltpu.VMEM((2 * VECS, count, full), jnp.bfloat16),
        ],
        cost_estimate=pl.CostEstimate(
            flops=2 * blocks * count * full * VECS + 2 * 2 * VECS * count * full * BLK,
            bytes_accessed=4 * (blocks * count * full + 6 * count * width),
            transcendentals=0,
        ),
    )(*args)


def lending_kernel(lend_ref, values_ref, *lent_refs):
    for q, lent_ref in enumerate(lent_refs):
        for j in range(lend_ref.shape[1]):
            lent_ref[j:j + 1, :] = values_ref[pl.ds(lend_ref[q, j], 1), :]


def lent_rows_of(values, lend_rows):
    shape = jax.ShapeDtypeStruct((lend_rows.shape[1], values.shape[1]), values.dtype)
    whole = pl.BlockSpec(memory_space=pltpu.VMEM)
    return pl.pallas_call(
        lending_kernel,
        out_shape=(shape,) * lend_rows.shape[0],
        in_specs=[pl.BlockSpec(memory_space=pltpu.SMEM), whole],
        out_specs=(whole,) * lend_rows.shape[0],
    )(lend_rows, values)


def mixing_kernel(mix_ref, anchor_ref, first_ref, second_ref, correction_ref, residual_ref):
    width = anchor_ref.shape[1]
    segment = lax.broadcasted_iota(jnp.int32, (1, width), 1) // BLK

    def weights(row_offset, shift):
        out = jnp.zeros((1, width), jnp.float32)
        for d in range(VECS):
            out = jnp.where(segment == d, mix_ref[row_offset + (d - shift) % VECS, d], out)
        return out

    def mixed(values, row_offset):
        total = None
        for shift in range(VECS):
            moved = values if shift == 0 else pltpu.roll(values, shift * BLK, 1)
            term = moved * weights(row_offset, shift)
            total = term if total is None else total + term
        return total

    anchor = anchor_ref[...]
    first = first_ref[...]
    second = second_ref[...]
    correction_ref[...] = mixed(anchor, 0) + mixed(first, VECS)
    residual_ref[...] = anchor - (mixed(first, 0) + mixed(second, VECS))


def mix_outputs(coefficients, anchor, first, second):
    count, width = anchor.shape
    rows = min(ROWS_PER_STEP, count)
    block = pl.BlockSpec((rows, width), lambda b: (b, 0))
    return pl.pallas_call(
        mixing_kernel,
        out_shape=(jax.ShapeDtypeStruct(anchor.shape, jnp.float32),) * 2,
        grid=(count // rows,),
        in_specs=[pl.BlockSpec(memory_space=pltpu.SMEM), block, block, block],
        out_specs=(block, block),
    )(coefficients, anchor, first, second)


def per_device(start_block, jacobian, counts, columns, send_list):
    lend_rows = send_list[0]
    jac_t = jnp.transpose(jacobian, (1, 0, 2))

    def ghosts(outgoing):
        wide, narrow = lax.axis_size("wide"), lax.axis_size("narrow")
        return (
            lax.ppermute(outgoing[0], "wide", [(i, i + 1) for i in range(wide - 1)]),
            lax.ppermute(outgoing[1], "wide", [(i + 1, i) for i in range(wide - 1)]),
            lax.ppermute(outgoing[2], "narrow", [(i, i + 1) for i in range(narrow - 1)]),
            lax.ppermute(outgoing[3], "narrow", [(i + 1, i) for i in range(narrow - 1)]),
        )

    cols_t = jnp.transpose(columns, (1, 0))
    first = apply_operator(jac_t, start_block, ghosts(lent_rows_of(start_block, lend_rows)), cols_t, counts, lend_rows)
    first_image, first_lent, anchor = first[0], jnp.stack(first[1:5]), first[5]
    peers = lax.axis_size("wide") * lax.axis_size("narrow")
    second = apply_operator(jac_t, first_image, ghosts(first_lent), cols_t, counts, lend_rows, anchor, peers)
    second_image, raw_gram = second[0], second[6]
    everyone = lax.all_to_all(raw_gram, ("wide", "narrow"), 0, 0, tiled=True)
    raw_gram = jnp.transpose(jnp.sum(everyone, axis=0), (1, 0)).reshape(5, VECS, VECS)
    shift = np.arange(VECS)[:, None, None]
    row_c = np.arange(VECS)[None, :, None]
    col_d = np.arange(VECS)[None, None, :]
    pick = jnp.asarray(((row_c - col_d) % VECS == shift).astype(np.float32))
    gram_parts = jnp.sum(raw_gram[:, :, :, None] * pick[None], axis=1)
    normal_matrix = jnp.concatenate(
        [
            jnp.concatenate([gram_parts[1], gram_parts[3].T], 1),
            jnp.concatenate([gram_parts[3], gram_parts[4]], 1),
        ],
        0,
    )
    right_terms = jnp.concatenate([gram_parts[0], gram_parts[2]], 0)
    factor = jnp.linalg.cholesky(normal_matrix)
    coefficients = jax.scipy.linalg.cho_solve((factor, True), right_terms)
    return mix_outputs(coefficients, anchor, first_image, second_image)


def solution(mesh):
    placed = (
        P(("wide", "narrow"), None),
        P(("wide", "narrow"), None, None),
        P(("wide", "narrow")),
        P(("wide", "narrow"), None),
        P(("wide", "narrow"), None, None),
    )
    return jax.shard_map(
        per_device,
        mesh=mesh,
        in_specs=placed,
        out_specs=(P(("wide", "narrow"), None), P(("wide", "narrow"), None)),
        check_vma=False,
    )
```

```python
import functools

import jax
import jax.numpy as jnp
import numpy as np
from jax import lax
from jax.experimental import pallas as pl
from jax.experimental.pallas import tpu as pltpu
from jax.sharding import PartitionSpec as P

BLK = 64
VECS = 4
NB = 5
E_DEV = 128
LANES = 128
SUBLANES = 8
UNROLL = 32
CHUNK_ROWS = 16
ROWS_PER_STEP = 32


DIAG_SHIFT = 1.5


def padded(cells, sides, width):
    for axis, dim in sides:
        count = lax.axis_size(axis)
        ends = count - 1
        head = lax.slice_in_dim(cells, 0, width, axis=dim)
        tail = lax.slice_in_dim(cells, cells.shape[dim] - width, cells.shape[dim], axis=dim)
        cells = jnp.concatenate(
            [
                lax.ppermute(tail, axis, [(i, (i + 1) % count) for i in range(ends)]),
                cells,
                lax.ppermute(head, axis, [((i + 1) % count, i) for i in range(ends)]),
            ],
            axis=dim,
        )
    return cells


def combine(values, mixing):
    shaped = values.reshape(values.shape[0], VECS, BLK)
    return jnp.einsum("eci,cd->edi", shaped, mixing, precision=lax.Precision.HIGHEST).reshape(
        values.shape[0], VECS * BLK
    )


def inner_block(left_side, right_side):
    left_shaped = left_side.reshape(left_side.shape[0], VECS, BLK)
    right_shaped = right_side.reshape(right_side.shape[0], VECS, BLK)
    return jnp.einsum("eci,edi->cd", left_shaped, right_shaped, precision=lax.Precision.HIGHEST)


def tree_sum(values, axes):
    for axis in axes:
        count = lax.axis_size(axis)
        if count & (count - 1):
            values = lax.psum(values, axis)
            continue
        stride = 1
        while stride < count:
            values = values + lax.ppermute(values, axis, [(i, i ^ stride) for i in range(count)])
            stride *= 2
    return values


def split_three(values):
    high = values.astype(jnp.bfloat16)
    rest = values - high.astype(jnp.float32)
    middle = rest.astype(jnp.bfloat16)
    low = (rest - middle.astype(jnp.float32)).astype(jnp.bfloat16)
    return jnp.concatenate([high, middle, low], axis=1)


def exchange_sum(values, axes):
    count = 1
    for axis in axes:
        count *= lax.axis_size(axis)
    flat = values.reshape(1, -1)
    everyone = lax.all_to_all(jnp.broadcast_to(flat, (count, flat.shape[1])), axes, 0, 0, tiled=True)
    return jnp.sum(everyone, axis=0).reshape(values.shape)


def segment_sums(values, segments):
    width = values.shape[1]
    seg = (
        lax.broadcasted_iota(jnp.int32, (width, segments), 0) // (width // segments)
        == lax.broadcasted_iota(jnp.int32, (width, segments), 1)
    ).astype(jnp.bfloat16)
    parts = split_three(values)
    return (
        jnp.dot(parts[:, 0:width], seg, preferred_element_type=jnp.float32)
        + jnp.dot(parts[:, width:2 * width], seg, preferred_element_type=jnp.float32)
        + jnp.dot(parts[:, 2 * width:3 * width], seg, preferred_element_type=jnp.float32)
    )


def gram_columns(pairs):
    rows = []
    for left, right in pairs:
        for shift in range(VECS):
            moved = right if shift == 0 else pltpu.roll(right, shift * BLK, 1)
            rows.append(jnp.sum(left * moved, axis=0, keepdims=True))
    stacked = jnp.concatenate(rows, axis=0)
    width = stacked.shape[1]
    seg = (
        lax.broadcasted_iota(jnp.int32, (VECS, width), 1) // BLK
        == lax.broadcasted_iota(jnp.int32, (VECS, width), 0)
    ).astype(jnp.bfloat16)
    parts = split_three(stacked)
    dims = (((1,), (1,)), ((), ()))
    return sum(
        lax.dot_general(seg, parts[:, p * width:(p + 1) * width], dims, preferred_element_type=jnp.float32)
        for p in range(3)
    )


def coupling_kernel(with_gram, count_ref, lend_ref, jac_hbm, own_ref, g0_ref, g1_ref, g2_ref, g3_ref, cols_ref, *rest):
    if with_gram:
        anchor_ref, rest = rest[0], rest[1:]
    out_ref, l0_ref, l1_ref, l2_ref, l3_ref, kept_ref = rest[:6]
    rest = rest[6:]
    if with_gram:
        gram_ref, rest = rest[0], rest[1:]
    jac_ref, sems, source_ref, picked_ref, z_ref, parts_ref = rest
    tiles = jac_ref.shape[2] // LANES
    count = own_ref.shape[0]
    width = own_ref.shape[1]
    ghost = g0_ref.shape[0]
    chunks = sems.shape[0]
    chunk_rows = count // chunks

    def chunk_copy(b):
        rows = pl.ds(pl.multiple_of(b * chunk_rows, chunk_rows), chunk_rows)
        return pltpu.make_async_copy(jac_hbm.at[:, rows, :], jac_ref.at[:, rows, :], sems.at[b])

    for b in range(chunks):
        chunk_copy(b).start()

    living = lax.broadcasted_iota(jnp.int32, (count, 1), 0) < count_ref[0]
    source_ref[0:count] = split_three(jnp.where(living, own_ref[...], jnp.float32(0.0)))
    for q, piece in enumerate((g0_ref, g1_ref, g2_ref, g3_ref)):
        source_ref[count + q * ghost:count + (q + 1) * ghost] = split_three(piece[...])
    slots = lax.broadcasted_iota(jnp.int32, (source_ref.shape[0], count), 0)
    for k in range(NB):
        chosen = (cols_ref[k:k + 1, :] == slots).astype(jnp.bfloat16)
        spread = lax.dot_general(
            chosen, source_ref[...], (((0,), (0,)), ((), ())), preferred_element_type=jnp.float32
        )
        picked_ref[k] = spread[:, 0:width] + spread[:, width:2 * width] + spread[:, 2 * width:3 * width]

    lane = lax.broadcasted_iota(jnp.int32, (SUBLANES, LANES), 1)

    def one_chunk(b, carry):
        chunk_copy(b).wait()
        for group in range(chunk_rows // SUBLANES):
            first_row = pl.multiple_of(b * chunk_rows + group * SUBLANES, SUBLANES)
            doubled = []
            for k in range(NB):
                per_vector = []
                for pair in range(VECS // 2):
                    tile = picked_ref[k, pl.ds(first_row, SUBLANES), pair * LANES:(pair + 1) * LANES]
                    swapped = pltpu.roll(tile, BLK, 1)
                    per_vector.append(jnp.where(lane < BLK, tile, swapped))
                    per_vector.append(jnp.where(lane >= BLK, tile, swapped))
                doubled.append(per_vector)

            def one_tile(t, inner):
                off = pl.multiple_of(t * LANES, LANES)
                blocks = [jac_ref[k, pl.ds(first_row, SUBLANES), pl.ds(off, LANES)] for k in range(NB)]
                for c in range(VECS):
                    terms = [blocks[k] * doubled[k][c] for k in range(NB)]
                    while len(terms) > 1:
                        terms = [terms[i] + terms[i + 1] for i in range(0, len(terms) - 1, 2)] + (
                            [terms[-1]] if len(terms) % 2 else []
                        )
                    z_ref[c, pl.ds(first_row, SUBLANES), pl.ds(off, LANES)] = terms[0]
                return inner

            lax.fori_loop(0, tiles, one_tile, 0, unroll=UNROLL)
        return carry

    lax.fori_loop(0, chunks, one_chunk, 0)

    full = tiles * LANES
    for c in range(VECS):
        total = z_ref[c]
        high = total.astype(jnp.bfloat16)
        parts_ref[2 * c] = high
        parts_ref[2 * c + 1] = (total - high.astype(jnp.float32)).astype(jnp.bfloat16)
    flat = parts_ref[...].reshape(2 * VECS * count, full)
    seg = (
        lax.broadcasted_iota(jnp.int32, (full, BLK), 0) // BLK
        == lax.broadcasted_iota(jnp.int32, (full, BLK), 1)
    ).astype(jnp.bfloat16)
    sums = jnp.dot(flat, seg, preferred_element_type=jnp.float32)
    coupled = jnp.concatenate(
        [sums[(2 * c) * count:(2 * c + 1) * count] + sums[(2 * c + 1) * count:(2 * c + 2) * count] for c in range(VECS)],
        axis=1,
    )
    own = own_ref[...]
    image = jnp.where(living, DIAG_SHIFT * own + coupled, jnp.float32(0.0))
    out_ref[...] = image
    kept = jnp.where(living, own, jnp.float32(0.0))
    kept_ref[...] = kept
    for q, lent_ref in enumerate((l0_ref, l1_ref, l2_ref, l3_ref)):
        for j in range(lend_ref.shape[1]):
            lent_ref[j:j + 1, :] = out_ref[pl.ds(lend_ref[q, j], 1), :]
    if with_gram:
        anchor = anchor_ref[...]
        partial = gram_columns(((kept, anchor), (kept, kept), (image, anchor), (image, kept), (image, image)))
        for target in range(gram_ref.shape[0]):
            gram_ref[target] = partial


def apply_operator(jac_t, own, ghost_rows, cols_t, counts, lend_rows, anchor=None, peers=1):
    blocks, count, full = jac_t.shape
    width = own.shape[1]
    ghost = ghost_rows[0].shape[0]
    chunks = max(count // CHUNK_ROWS, 1)
    with_gram = anchor is not None
    smem = pl.BlockSpec(memory_space=pltpu.SMEM)
    vmem = pl.BlockSpec(memory_space=pltpu.VMEM)
    lent = lend_rows.shape[1]
    in_specs = [smem, smem, pl.BlockSpec(memory_space=pl.ANY), vmem, vmem, vmem, vmem, vmem, vmem]
    out_shape = [jax.ShapeDtypeStruct((count, width), jnp.float32)]
    out_shape += [jax.ShapeDtypeStruct((lent, width), jnp.float32)] * lend_rows.shape[0]
    out_shape += [jax.ShapeDtypeStruct((count, width), jnp.float32)]
    args = [counts, lend_rows, jac_t, own, *ghost_rows, cols_t]
    if with_gram:
        in_specs.append(vmem)
        args.append(anchor)
        out_shape.append(jax.ShapeDtypeStruct((peers, VECS, 5 * VECS), jnp.float32))
    return pl.pallas_call(
        functools.partial(coupling_kernel, with_gram),
        out_shape=tuple(out_shape),
        in_specs=in_specs,
        out_specs=tuple(vmem for _ in out_shape),
        scratch_shapes=[
            pltpu.VMEM((blocks, count, full), jnp.float32),
            pltpu.SemaphoreType.DMA((chunks,)),
            pltpu.VMEM((count + 4 * ghost, 3 * width), jnp.bfloat16),
            pltpu.VMEM((blocks, count, width), jnp.float32),
            pltpu.VMEM((VECS, count, full), jnp.float32),
            pltpu.VMEM((2 * VECS, count, full), jnp.bfloat16),
        ],
        cost_estimate=pl.CostEstimate(
            flops=2 * blocks * count * full * VECS + 2 * 2 * VECS * count * full * BLK,
            bytes_accessed=4 * (blocks * count * full + 6 * count * width),
            transcendentals=0,
        ),
    )(*args)


def lending_kernel(lend_ref, values_ref, *lent_refs):
    for q, lent_ref in enumerate(lent_refs):
        for j in range(lend_ref.shape[1]):
            lent_ref[j:j + 1, :] = values_ref[pl.ds(lend_ref[q, j], 1), :]


def lent_rows_of(values, lend_rows):
    shape = jax.ShapeDtypeStruct((lend_rows.shape[1], values.shape[1]), values.dtype)
    whole = pl.BlockSpec(memory_space=pltpu.VMEM)
    return pl.pallas_call(
        lending_kernel,
        out_shape=(shape,) * lend_rows.shape[0],
        in_specs=[pl.BlockSpec(memory_space=pltpu.SMEM), whole],
        out_specs=(whole,) * lend_rows.shape[0],
    )(lend_rows, values)


def mixing_kernel(mix_ref, anchor_ref, first_ref, second_ref, correction_ref, residual_ref):
    width = anchor_ref.shape[1]
    segment = lax.broadcasted_iota(jnp.int32, (1, width), 1) // BLK

    def weights(row_offset, shift):
        out = jnp.zeros((1, width), jnp.float32)
        for d in range(VECS):
            out = jnp.where(segment == d, mix_ref[row_offset + (d - shift) % VECS, d], out)
        return out

    def mixed(values, row_offset):
        total = None
        for shift in range(VECS):
            moved = values if shift == 0 else pltpu.roll(values, shift * BLK, 1)
            term = moved * weights(row_offset, shift)
            total = term if total is None else total + term
        return total

    anchor = anchor_ref[...]
    first = first_ref[...]
    second = second_ref[...]
    correction_ref[...] = mixed(anchor, 0) + mixed(first, VECS)
    residual_ref[...] = anchor - (mixed(first, 0) + mixed(second, VECS))


def mix_outputs(coefficients, anchor, first, second):
    whole = pl.BlockSpec(memory_space=pltpu.VMEM)
    return pl.pallas_call(
        mixing_kernel,
        out_shape=(jax.ShapeDtypeStruct(anchor.shape, jnp.float32),) * 2,
        in_specs=[pl.BlockSpec(memory_space=pltpu.SMEM), whole, whole, whole],
        out_specs=(whole, whole),
    )(coefficients, anchor, first, second)


def per_device(start_block, jacobian, counts, columns, send_list):
    lend_rows = send_list[0]
    jac_t = jnp.transpose(jacobian, (1, 0, 2))

    def ghosts(outgoing):
        wide, narrow = lax.axis_size("wide"), lax.axis_size("narrow")
        return (
            lax.ppermute(outgoing[0], "wide", [(i, i + 1) for i in range(wide - 1)]),
            lax.ppermute(outgoing[1], "wide", [(i + 1, i) for i in range(wide - 1)]),
            lax.ppermute(outgoing[2], "narrow", [(i, i + 1) for i in range(narrow - 1)]),
            lax.ppermute(outgoing[3], "narrow", [(i + 1, i) for i in range(narrow - 1)]),
        )

    cols_t = jnp.transpose(columns, (1, 0))
    first = apply_operator(jac_t, start_block, ghosts(lent_rows_of(start_block, lend_rows)), cols_t, counts, lend_rows)
    first_image, first_lent, anchor = first[0], jnp.stack(first[1:5]), first[5]
    peers = lax.axis_size("wide") * lax.axis_size("narrow")
    second = apply_operator(jac_t, first_image, ghosts(first_lent), cols_t, counts, lend_rows, anchor, peers)
    second_image, raw_gram = second[0], second[6]
    everyone = lax.all_to_all(raw_gram, ("wide", "narrow"), 0, 0, tiled=True)
    raw_gram = jnp.transpose(jnp.sum(everyone, axis=0), (1, 0)).reshape(5, VECS, VECS)
    shift = np.arange(VECS)[:, None, None]
    row_c = np.arange(VECS)[None, :, None]
    col_d = np.arange(VECS)[None, None, :]
    pick = jnp.asarray(((row_c - col_d) % VECS == shift).astype(np.float32))
    gram_parts = jnp.sum(raw_gram[:, :, :, None] * pick[None], axis=1)
    normal_matrix = jnp.concatenate(
        [
            jnp.concatenate([gram_parts[1], gram_parts[3].T], 1),
            jnp.concatenate([gram_parts[3], gram_parts[4]], 1),
        ],
        0,
    )
    right_terms = jnp.concatenate([gram_parts[0], gram_parts[2]], 0)
    factor = jnp.linalg.cholesky(normal_matrix)
    coefficients = jax.scipy.linalg.cho_solve((factor, True), right_terms)
    return mix_outputs(coefficients, anchor, first_image, second_image)


def solution(mesh):
    placed = (
        P(("wide", "narrow"), None),
        P(("wide", "narrow"), None, None),
        P(("wide", "narrow")),
        P(("wide", "narrow"), None),
        P(("wide", "narrow"), None, None),
    )
    return jax.shard_map(
        per_device,
        mesh=mesh,
        in_specs=placed,
        out_specs=(P(("wide", "narrow"), None), P(("wide", "narrow"), None)),
        check_vma=False,
    )
```

```python
import functools

import jax
import jax.numpy as jnp
import numpy as np
from jax import lax
from jax.experimental import pallas as pl
from jax.experimental.pallas import tpu as pltpu
from jax.sharding import PartitionSpec as P

BLK = 64
VECS = 4
NB = 5
E_DEV = 128
LANES = 128
SUBLANES = 8
UNROLL = 32
CHUNK_ROWS = 16
ROWS_PER_STEP = 32


DIAG_SHIFT = 1.5


def padded(cells, sides, width):
    for axis, dim in sides:
        count = lax.axis_size(axis)
        ends = count - 1
        head = lax.slice_in_dim(cells, 0, width, axis=dim)
        tail = lax.slice_in_dim(cells, cells.shape[dim] - width, cells.shape[dim], axis=dim)
        cells = jnp.concatenate(
            [
                lax.ppermute(tail, axis, [(i, (i + 1) % count) for i in range(ends)]),
                cells,
                lax.ppermute(head, axis, [((i + 1) % count, i) for i in range(ends)]),
            ],
            axis=dim,
        )
    return cells


def combine(values, mixing):
    shaped = values.reshape(values.shape[0], VECS, BLK)
    return jnp.einsum("eci,cd->edi", shaped, mixing, precision=lax.Precision.HIGHEST).reshape(
        values.shape[0], VECS * BLK
    )


def inner_block(left_side, right_side):
    left_shaped = left_side.reshape(left_side.shape[0], VECS, BLK)
    right_shaped = right_side.reshape(right_side.shape[0], VECS, BLK)
    return jnp.einsum("eci,edi->cd", left_shaped, right_shaped, precision=lax.Precision.HIGHEST)


def tree_sum(values, axes):
    for axis in axes:
        count = lax.axis_size(axis)
        if count & (count - 1):
            values = lax.psum(values, axis)
            continue
        stride = 1
        while stride < count:
            values = values + lax.ppermute(values, axis, [(i, i ^ stride) for i in range(count)])
            stride *= 2
    return values


def split_three(values):
    high = values.astype(jnp.bfloat16)
    rest = values - high.astype(jnp.float32)
    middle = rest.astype(jnp.bfloat16)
    low = (rest - middle.astype(jnp.float32)).astype(jnp.bfloat16)
    return jnp.concatenate([high, middle, low], axis=1)


def exchange_sum(values, axes):
    count = 1
    for axis in axes:
        count *= lax.axis_size(axis)
    flat = values.reshape(1, -1)
    everyone = lax.all_to_all(jnp.broadcast_to(flat, (count, flat.shape[1])), axes, 0, 0, tiled=True)
    return jnp.sum(everyone, axis=0).reshape(values.shape)


def segment_sums(values, segments):
    width = values.shape[1]
    seg = (
        lax.broadcasted_iota(jnp.int32, (width, segments), 0) // (width // segments)
        == lax.broadcasted_iota(jnp.int32, (width, segments), 1)
    ).astype(jnp.bfloat16)
    parts = split_three(values)
    return (
        jnp.dot(parts[:, 0:width], seg, preferred_element_type=jnp.float32)
        + jnp.dot(parts[:, width:2 * width], seg, preferred_element_type=jnp.float32)
        + jnp.dot(parts[:, 2 * width:3 * width], seg, preferred_element_type=jnp.float32)
    )


def gram_columns(pairs):
    rows = []
    for left, right in pairs:
        for shift in range(VECS):
            moved = right if shift == 0 else pltpu.roll(right, shift * BLK, 1)
            rows.append(jnp.sum(left * moved, axis=0, keepdims=True))
    stacked = jnp.concatenate(rows, axis=0)
    width = stacked.shape[1]
    seg = (
        lax.broadcasted_iota(jnp.int32, (VECS, width), 1) // BLK
        == lax.broadcasted_iota(jnp.int32, (VECS, width), 0)
    ).astype(jnp.bfloat16)
    parts = split_three(stacked)
    dims = (((1,), (1,)), ((), ()))
    return sum(
        lax.dot_general(seg, parts[:, p * width:(p + 1) * width], dims, preferred_element_type=jnp.float32)
        for p in range(3)
    )


def coupling_kernel(with_gram, count_ref, lend_ref, jac_hbm, own_ref, g0_ref, g1_ref, g2_ref, g3_ref, cols_ref, *rest):
    if with_gram:
        anchor_ref, out_ref, gram_ref = rest[:3]
        rest = rest[3:]
    else:
        out_ref, l0_ref, l1_ref, l2_ref, l3_ref, kept_ref = rest[:6]
        rest = rest[6:]
    jac_ref, sems, source_ref, picked_ref, z_ref, parts_ref = rest
    tiles = jac_ref.shape[2] // LANES
    count = own_ref.shape[0]
    width = own_ref.shape[1]
    ghost = g0_ref.shape[0]
    chunks = sems.shape[0]
    chunk_rows = count // chunks

    def chunk_copy(b):
        rows = pl.ds(pl.multiple_of(b * chunk_rows, chunk_rows), chunk_rows)
        return pltpu.make_async_copy(jac_hbm.at[:, rows, :], jac_ref.at[:, rows, :], sems.at[b])

    for b in range(chunks):
        chunk_copy(b).start()

    living = lax.broadcasted_iota(jnp.int32, (count, 1), 0) < count_ref[0]
    source_ref[0:count] = split_three(jnp.where(living, own_ref[...], jnp.float32(0.0)))
    for q, piece in enumerate((g0_ref, g1_ref, g2_ref, g3_ref)):
        source_ref[count + q * ghost:count + (q + 1) * ghost] = split_three(piece[...])
    slots = lax.broadcasted_iota(jnp.int32, (source_ref.shape[0], count), 0)
    for k in range(NB):
        chosen = (cols_ref[k:k + 1, :] == slots).astype(jnp.bfloat16)
        spread = lax.dot_general(
            chosen, source_ref[...], (((0,), (0,)), ((), ())), preferred_element_type=jnp.float32
        )
        picked_ref[k] = spread[:, 0:width] + spread[:, width:2 * width] + spread[:, 2 * width:3 * width]

    lane = lax.broadcasted_iota(jnp.int32, (SUBLANES, LANES), 1)

    def one_chunk(b, carry):
        chunk_copy(b).wait()
        for group in range(chunk_rows // SUBLANES):
            first_row = pl.multiple_of(b * chunk_rows + group * SUBLANES, SUBLANES)
            doubled = []
            for k in range(NB):
                per_vector = []
                for pair in range(VECS // 2):
                    tile = picked_ref[k, pl.ds(first_row, SUBLANES), pair * LANES:(pair + 1) * LANES]
                    swapped = pltpu.roll(tile, BLK, 1)
                    per_vector.append(jnp.where(lane < BLK, tile, swapped))
                    per_vector.append(jnp.where(lane >= BLK, tile, swapped))
                doubled.append(per_vector)

            def one_tile(t, inner):
                off = pl.multiple_of(t * LANES, LANES)
                blocks = [jac_ref[k, pl.ds(first_row, SUBLANES), pl.ds(off, LANES)] for k in range(NB)]
                for c in range(VECS):
                    terms = [blocks[k] * doubled[k][c] for k in range(NB)]
                    while len(terms) > 1:
                        terms = [terms[i] + terms[i + 1] for i in range(0, len(terms) - 1, 2)] + (
                            [terms[-1]] if len(terms) % 2 else []
                        )
                    z_ref[c, pl.ds(first_row, SUBLANES), pl.ds(off, LANES)] = terms[0]
                return inner

            lax.fori_loop(0, tiles, one_tile, 0, unroll=UNROLL)
        return carry

    lax.fori_loop(0, chunks, one_chunk, 0)

    full = tiles * LANES
    for c in range(VECS):
        total = z_ref[c]
        high = total.astype(jnp.bfloat16)
        parts_ref[2 * c] = high
        parts_ref[2 * c + 1] = (total - high.astype(jnp.float32)).astype(jnp.bfloat16)
    flat = parts_ref[...].reshape(2 * VECS * count, full)
    seg = (
        lax.broadcasted_iota(jnp.int32, (full, BLK), 0) // BLK
        == lax.broadcasted_iota(jnp.int32, (full, BLK), 1)
    ).astype(jnp.bfloat16)
    sums = jnp.dot(flat, seg, preferred_element_type=jnp.float32)
    coupled = jnp.concatenate(
        [sums[(2 * c) * count:(2 * c + 1) * count] + sums[(2 * c + 1) * count:(2 * c + 2) * count] for c in range(VECS)],
        axis=1,
    )
    own = own_ref[...]
    image = jnp.where(living, DIAG_SHIFT * own + coupled, jnp.float32(0.0))
    out_ref[...] = image
    kept = jnp.where(living, own, jnp.float32(0.0))
    if not with_gram:
        kept_ref[...] = kept
        for q, lent_ref in enumerate((l0_ref, l1_ref, l2_ref, l3_ref)):
            for j in range(lend_ref.shape[1]):
                lent_ref[j:j + 1, :] = out_ref[pl.ds(lend_ref[q, j], 1), :]
    else:
        anchor = anchor_ref[...]
        partial = gram_columns(((kept, anchor), (kept, kept), (image, anchor), (image, kept), (image, image)))
        for target in range(gram_ref.shape[0]):
            gram_ref[target] = partial


def apply_operator(jac_t, own, ghost_rows, cols_t, counts, lend_rows, anchor=None, peers=1):
    blocks, count, full = jac_t.shape
    width = own.shape[1]
    ghost = ghost_rows[0].shape[0]
    chunks = max(count // CHUNK_ROWS, 1)
    with_gram = anchor is not None
    smem = pl.BlockSpec(memory_space=pltpu.SMEM)
    vmem = pl.BlockSpec(memory_space=pltpu.VMEM)
    lent = lend_rows.shape[1]
    in_specs = [smem, smem, pl.BlockSpec(memory_space=pl.ANY), vmem, vmem, vmem, vmem, vmem, vmem]
    out_shape = [jax.ShapeDtypeStruct((count, width), jnp.float32)]
    args = [counts, lend_rows, jac_t, own, *ghost_rows, cols_t]
    if with_gram:
        in_specs.append(vmem)
        args.append(anchor)
        out_shape.append(jax.ShapeDtypeStruct((peers, VECS, 5 * VECS), jnp.float32))
    else:
        out_shape += [jax.ShapeDtypeStruct((lent, width), jnp.float32)] * lend_rows.shape[0]
        out_shape += [jax.ShapeDtypeStruct((count, width), jnp.float32)]
    return pl.pallas_call(
        functools.partial(coupling_kernel, with_gram),
        out_shape=tuple(out_shape),
        in_specs=in_specs,
        out_specs=tuple(vmem for _ in out_shape),
        scratch_shapes=[
            pltpu.VMEM((blocks, count, full), jnp.float32),
            pltpu.SemaphoreType.DMA((chunks,)),
            pltpu.VMEM((count + 4 * ghost, 3 * width), jnp.bfloat16),
            pltpu.VMEM((blocks, count, width), jnp.float32),
            pltpu.VMEM((VECS, count, full), jnp.float32),
            pltpu.VMEM((2 * VECS, count, full), jnp.bfloat16),
        ],
        cost_estimate=pl.CostEstimate(
            flops=2 * blocks * count * full * VECS + 2 * 2 * VECS * count * full * BLK,
            bytes_accessed=4 * (blocks * count * full + 6 * count * width),
            transcendentals=0,
        ),
    )(*args)


def lending_kernel(lend_ref, values_ref, *lent_refs):
    for q, lent_ref in enumerate(lent_refs):
        for j in range(lend_ref.shape[1]):
            lent_ref[j:j + 1, :] = values_ref[pl.ds(lend_ref[q, j], 1), :]


def lent_rows_of(values, lend_rows):
    shape = jax.ShapeDtypeStruct((lend_rows.shape[1], values.shape[1]), values.dtype)
    whole = pl.BlockSpec(memory_space=pltpu.VMEM)
    return pl.pallas_call(
        lending_kernel,
        out_shape=(shape,) * lend_rows.shape[0],
        in_specs=[pl.BlockSpec(memory_space=pltpu.SMEM), whole],
        out_specs=(whole,) * lend_rows.shape[0],
    )(lend_rows, values)


def mixing_kernel(mix_ref, anchor_ref, first_ref, second_ref, correction_ref, residual_ref):
    width = anchor_ref.shape[1]
    segment = lax.broadcasted_iota(jnp.int32, (1, width), 1) // BLK

    def weights(row_offset, shift):
        out = jnp.zeros((1, width), jnp.float32)
        for d in range(VECS):
            out = jnp.where(segment == d, mix_ref[row_offset + (d - shift) % VECS, d], out)
        return out

    def mixed(values, row_offset):
        total = None
        for shift in range(VECS):
            moved = values if shift == 0 else pltpu.roll(values, shift * BLK, 1)
            term = moved * weights(row_offset, shift)
            total = term if total is None else total + term
        return total

    anchor = anchor_ref[...]
    first = first_ref[...]
    second = second_ref[...]
    correction_ref[...] = mixed(anchor, 0) + mixed(first, VECS)
    residual_ref[...] = anchor - (mixed(first, 0) + mixed(second, VECS))


def mix_outputs(coefficients, anchor, first, second):
    whole = pl.BlockSpec(memory_space=pltpu.VMEM)
    return pl.pallas_call(
        mixing_kernel,
        out_shape=(jax.ShapeDtypeStruct(anchor.shape, jnp.float32),) * 2,
        in_specs=[pl.BlockSpec(memory_space=pltpu.SMEM), whole, whole, whole],
        out_specs=(whole, whole),
    )(coefficients, anchor, first, second)


def per_device(start_block, jacobian, counts, columns, send_list):
    lend_rows = send_list[0]
    jac_t = jnp.transpose(jacobian, (1, 0, 2))

    def ghosts(outgoing):
        wide, narrow = lax.axis_size("wide"), lax.axis_size("narrow")
        return (
            lax.ppermute(outgoing[0], "wide", [(i, i + 1) for i in range(wide - 1)]),
            lax.ppermute(outgoing[1], "wide", [(i + 1, i) for i in range(wide - 1)]),
            lax.ppermute(outgoing[2], "narrow", [(i, i + 1) for i in range(narrow - 1)]),
            lax.ppermute(outgoing[3], "narrow", [(i + 1, i) for i in range(narrow - 1)]),
        )

    cols_t = jnp.transpose(columns, (1, 0))
    first = apply_operator(jac_t, start_block, ghosts(lent_rows_of(start_block, lend_rows)), cols_t, counts, lend_rows)
    first_image, first_lent, anchor = first[0], jnp.stack(first[1:5]), first[5]
    peers = lax.axis_size("wide") * lax.axis_size("narrow")
    second = apply_operator(jac_t, first_image, ghosts(first_lent), cols_t, counts, lend_rows, anchor, peers)
    second_image, raw_gram = second
    everyone = lax.all_to_all(raw_gram, ("wide", "narrow"), 0, 0, tiled=True)
    raw_gram = jnp.transpose(jnp.sum(everyone, axis=0), (1, 0)).reshape(5, VECS, VECS)
    shift = np.arange(VECS)[:, None, None]
    row_c = np.arange(VECS)[None, :, None]
    col_d = np.arange(VECS)[None, None, :]
    pick = jnp.asarray(((row_c - col_d) % VECS == shift).astype(np.float32))
    gram_parts = jnp.sum(raw_gram[:, :, :, None] * pick[None], axis=1)
    normal_matrix = jnp.concatenate(
        [
            jnp.concatenate([gram_parts[1], gram_parts[3].T], 1),
            jnp.concatenate([gram_parts[3], gram_parts[4]], 1),
        ],
        0,
    )
    right_terms = jnp.concatenate([gram_parts[0], gram_parts[2]], 0)
    factor = jnp.linalg.cholesky(normal_matrix)
    coefficients = jax.scipy.linalg.cho_solve((factor, True), right_terms)
    return mix_outputs(coefficients, anchor, first_image, second_image)


def solution(mesh):
    placed = (
        P(("wide", "narrow"), None),
        P(("wide", "narrow"), None, None),
        P(("wide", "narrow")),
        P(("wide", "narrow"), None),
        P(("wide", "narrow"), None, None),
    )
    return jax.shard_map(
        per_device,
        mesh=mesh,
        in_specs=placed,
        out_specs=(P(("wide", "narrow"), None), P(("wide", "narrow"), None)),
        check_vma=False,
    )
```

```python
import functools

import jax
import jax.numpy as jnp
import numpy as np
from jax import lax
from jax.experimental import pallas as pl
from jax.experimental.pallas import tpu as pltpu
from jax.sharding import PartitionSpec as P

BLK = 64
VECS = 4
NB = 5
E_DEV = 128
LANES = 128
SUBLANES = 8
UNROLL = 32
CHUNK_ROWS = 16
ROWS_PER_STEP = 32


DIAG_SHIFT = 1.5


def padded(cells, sides, width):
    for axis, dim in sides:
        count = lax.axis_size(axis)
        ends = count - 1
        head = lax.slice_in_dim(cells, 0, width, axis=dim)
        tail = lax.slice_in_dim(cells, cells.shape[dim] - width, cells.shape[dim], axis=dim)
        cells = jnp.concatenate(
            [
                lax.ppermute(tail, axis, [(i, (i + 1) % count) for i in range(ends)]),
                cells,
                lax.ppermute(head, axis, [((i + 1) % count, i) for i in range(ends)]),
            ],
            axis=dim,
        )
    return cells


def combine(values, mixing):
    shaped = values.reshape(values.shape[0], VECS, BLK)
    return jnp.einsum("eci,cd->edi", shaped, mixing, precision=lax.Precision.HIGHEST).reshape(
        values.shape[0], VECS * BLK
    )


def inner_block(left_side, right_side):
    left_shaped = left_side.reshape(left_side.shape[0], VECS, BLK)
    right_shaped = right_side.reshape(right_side.shape[0], VECS, BLK)
    return jnp.einsum("eci,edi->cd", left_shaped, right_shaped, precision=lax.Precision.HIGHEST)


def tree_sum(values, axes):
    for axis in axes:
        count = lax.axis_size(axis)
        if count & (count - 1):
            values = lax.psum(values, axis)
            continue
        stride = 1
        while stride < count:
            values = values + lax.ppermute(values, axis, [(i, i ^ stride) for i in range(count)])
            stride *= 2
    return values


def split_three(values):
    high = values.astype(jnp.bfloat16)
    rest = values - high.astype(jnp.float32)
    middle = rest.astype(jnp.bfloat16)
    low = (rest - middle.astype(jnp.float32)).astype(jnp.bfloat16)
    return jnp.concatenate([high, middle, low], axis=1)


def exchange_sum(values, axes):
    count = 1
    for axis in axes:
        count *= lax.axis_size(axis)
    flat = values.reshape(1, -1)
    everyone = lax.all_to_all(jnp.broadcast_to(flat, (count, flat.shape[1])), axes, 0, 0, tiled=True)
    return jnp.sum(everyone, axis=0).reshape(values.shape)


def segment_sums(values, segments):
    width = values.shape[1]
    seg = (
        lax.broadcasted_iota(jnp.int32, (width, segments), 0) // (width // segments)
        == lax.broadcasted_iota(jnp.int32, (width, segments), 1)
    ).astype(jnp.bfloat16)
    parts = split_three(values)
    return (
        jnp.dot(parts[:, 0:width], seg, preferred_element_type=jnp.float32)
        + jnp.dot(parts[:, width:2 * width], seg, preferred_element_type=jnp.float32)
        + jnp.dot(parts[:, 2 * width:3 * width], seg, preferred_element_type=jnp.float32)
    )


def gram_columns(pairs):
    rows = []
    for left, right in pairs:
        for shift in range(VECS):
            moved = right if shift == 0 else pltpu.roll(right, shift * BLK, 1)
            rows.append(jnp.sum(left * moved, axis=0, keepdims=True))
    stacked = jnp.concatenate(rows, axis=0)
    width = stacked.shape[1]
    seg = (
        lax.broadcasted_iota(jnp.int32, (VECS, width), 1) // BLK
        == lax.broadcasted_iota(jnp.int32, (VECS, width), 0)
    ).astype(jnp.bfloat16)
    parts = split_three(stacked)
    dims = (((1,), (1,)), ((), ()))
    return sum(
        lax.dot_general(seg, parts[:, p * width:(p + 1) * width], dims, preferred_element_type=jnp.float32)
        for p in range(3)
    )


def coupling_kernel(with_gram, count_ref, lend_ref, jac_hbm, own_ref, g0_ref, g1_ref, g2_ref, g3_ref, cols_ref, *rest):
    if with_gram:
        anchor_ref, out_ref, gram_ref = rest[:3]
        rest = rest[3:]
    else:
        out_ref, l0_ref, l1_ref, l2_ref, l3_ref, kept_ref = rest[:6]
        rest = rest[6:]
    jac_ref, sems, source_ref, picked_ref, z_ref, parts_ref = rest
    tiles = jac_ref.shape[2] // LANES
    count = own_ref.shape[0]
    width = own_ref.shape[1]
    ghost = g0_ref.shape[0]
    chunks = sems.shape[0]
    chunk_rows = count // chunks

    def chunk_copy(b):
        rows = pl.ds(pl.multiple_of(b * chunk_rows, chunk_rows), chunk_rows)
        return pltpu.make_async_copy(jac_hbm.at[:, rows, :], jac_ref.at[:, rows, :], sems.at[b])

    for b in range(chunks):
        chunk_copy(b).start()

    living = lax.broadcasted_iota(jnp.int32, (count, 1), 0) < count_ref[0]
    source_ref[0:count] = split_three(jnp.where(living, own_ref[...], jnp.float32(0.0)))
    for q, piece in enumerate((g0_ref, g1_ref, g2_ref, g3_ref)):
        source_ref[count + q * ghost:count + (q + 1) * ghost] = split_three(piece[...])
    slots = lax.broadcasted_iota(jnp.int32, (source_ref.shape[0], count), 0)
    for k in range(NB):
        chosen = (cols_ref[k:k + 1, :] == slots).astype(jnp.bfloat16)
        spread = lax.dot_general(
            chosen, source_ref[...], (((0,), (0,)), ((), ())), preferred_element_type=jnp.float32
        )
        picked_ref[k] = spread[:, 0:width] + spread[:, width:2 * width] + spread[:, 2 * width:3 * width]

    lane = lax.broadcasted_iota(jnp.int32, (SUBLANES, LANES), 1)

    def one_chunk(b, carry):
        chunk_copy(b).wait()
        for group in range(chunk_rows // SUBLANES):
            first_row = pl.multiple_of(b * chunk_rows + group * SUBLANES, SUBLANES)
            doubled = []
            for k in range(NB):
                per_vector = []
                for pair in range(VECS // 2):
                    tile = picked_ref[k, pl.ds(first_row, SUBLANES), pair * LANES:(pair + 1) * LANES]
                    swapped = pltpu.roll(tile, BLK, 1)
                    per_vector.append(jnp.where(lane < BLK, tile, swapped))
                    per_vector.append(jnp.where(lane >= BLK, tile, swapped))
                doubled.append(per_vector)

            def one_tile(t, inner):
                off = pl.multiple_of(t * LANES, LANES)
                blocks = [jac_ref[k, pl.ds(first_row, SUBLANES), pl.ds(off, LANES)] for k in range(NB)]
                for c in range(VECS):
                    terms = [blocks[k] * doubled[k][c] for k in range(NB)]
                    while len(terms) > 1:
                        terms = [terms[i] + terms[i + 1] for i in range(0, len(terms) - 1, 2)] + (
                            [terms[-1]] if len(terms) % 2 else []
                        )
                    z_ref[c, pl.ds(first_row, SUBLANES), pl.ds(off, LANES)] = terms[0]
                return inner

            lax.fori_loop(0, tiles, one_tile, 0, unroll=UNROLL)
        return carry

    lax.fori_loop(0, chunks, one_chunk, 0)

    full = tiles * LANES
    for c in range(VECS):
        total = z_ref[c]
        high = total.astype(jnp.bfloat16)
        parts_ref[2 * c] = high
        parts_ref[2 * c + 1] = (total - high.astype(jnp.float32)).astype(jnp.bfloat16)
    flat = parts_ref[...].reshape(2 * VECS * count, full)
    seg = (
        lax.broadcasted_iota(jnp.int32, (full, BLK), 0) // BLK
        == lax.broadcasted_iota(jnp.int32, (full, BLK), 1)
    ).astype(jnp.bfloat16)
    sums = jnp.dot(flat, seg, preferred_element_type=jnp.float32)
    coupled = jnp.concatenate(
        [sums[(2 * c) * count:(2 * c + 1) * count] + sums[(2 * c + 1) * count:(2 * c + 2) * count] for c in range(VECS)],
        axis=1,
    )
    own = own_ref[...]
    image = jnp.where(living, DIAG_SHIFT * own + coupled, jnp.float32(0.0))
    out_ref[...] = image
    kept = jnp.where(living, own, jnp.float32(0.0))
    if not with_gram:
        kept_ref[...] = kept
        for q, lent_ref in enumerate((l0_ref, l1_ref, l2_ref, l3_ref)):
            for j in range(lend_ref.shape[1]):
                lent_ref[j:j + 1, :] = out_ref[pl.ds(lend_ref[q, j], 1), :]
    else:
        anchor = anchor_ref[...]
        partial = gram_columns(((kept, anchor), (kept, kept), (image, anchor), (image, kept), (image, image)))
        for target in range(gram_ref.shape[0]):
            gram_ref[target] = partial


def apply_operator(jac_t, own, ghost_rows, cols_t, counts, lend_rows, anchor=None, peers=1):
    blocks, count, full = jac_t.shape
    width = own.shape[1]
    ghost = ghost_rows[0].shape[0]
    chunks = max(count // CHUNK_ROWS, 1)
    with_gram = anchor is not None
    smem = pl.BlockSpec(memory_space=pltpu.SMEM)
    vmem = pl.BlockSpec(memory_space=pltpu.VMEM)
    lent = lend_rows.shape[1]
    in_specs = [smem, smem, pl.BlockSpec(memory_space=pl.ANY), vmem, vmem, vmem, vmem, vmem, vmem]
    out_shape = [jax.ShapeDtypeStruct((count, width), jnp.float32)]
    args = [counts, lend_rows, jac_t, own, *ghost_rows, cols_t]
    if with_gram:
        in_specs.append(vmem)
        args.append(anchor)
        out_shape.append(jax.ShapeDtypeStruct((peers, VECS, 5 * VECS), jnp.float32))
    else:
        out_shape += [jax.ShapeDtypeStruct((lent, width), jnp.float32)] * lend_rows.shape[0]
        out_shape += [jax.ShapeDtypeStruct((count, width), jnp.float32)]
    return pl.pallas_call(
        functools.partial(coupling_kernel, with_gram),
        out_shape=tuple(out_shape),
        in_specs=in_specs,
        out_specs=tuple(vmem for _ in out_shape),
        scratch_shapes=[
            pltpu.VMEM((blocks, count, full), jnp.float32),
            pltpu.SemaphoreType.DMA((chunks,)),
            pltpu.VMEM((count + 4 * ghost, 3 * width), jnp.bfloat16),
            pltpu.VMEM((blocks, count, width), jnp.float32),
            pltpu.VMEM((VECS, count, full), jnp.float32),
            pltpu.VMEM((2 * VECS, count, full), jnp.bfloat16),
        ],
        cost_estimate=pl.CostEstimate(
            flops=2 * blocks * count * full * VECS + 2 * 2 * VECS * count * full * BLK,
            bytes_accessed=4 * (blocks * count * full + 6 * count * width),
            transcendentals=0,
        ),
    )(*args)


def lending_kernel(lend_ref, values_ref, *lent_refs):
    for q, lent_ref in enumerate(lent_refs):
        for j in range(lend_ref.shape[1]):
            lent_ref[j:j + 1, :] = values_ref[pl.ds(lend_ref[q, j], 1), :]


def lent_rows_of(values, lend_rows):
    shape = jax.ShapeDtypeStruct((lend_rows.shape[1], values.shape[1]), values.dtype)
    whole = pl.BlockSpec(memory_space=pltpu.VMEM)
    return pl.pallas_call(
        lending_kernel,
        out_shape=(shape,) * lend_rows.shape[0],
        in_specs=[pl.BlockSpec(memory_space=pltpu.SMEM), whole],
        out_specs=(whole,) * lend_rows.shape[0],
    )(lend_rows, values)


def mixing_kernel(mix_ref, anchor_ref, first_ref, second_ref, correction_ref, residual_ref):
    width = anchor_ref.shape[1]
    segment = lax.broadcasted_iota(jnp.int32, (1, width), 1) // BLK

    def weights(row_offset, shift):
        out = jnp.zeros((1, width), jnp.float32)
        for d in range(VECS):
            out = jnp.where(segment == d, mix_ref[row_offset + (d - shift) % VECS, d], out)
        return out

    def mixed(values, row_offset):
        total = None
        for shift in range(VECS):
            moved = values if shift == 0 else pltpu.roll(values, shift * BLK, 1)
            term = moved * weights(row_offset, shift)
            total = term if total is None else total + term
        return total

    anchor = anchor_ref[...]
    first = first_ref[...]
    second = second_ref[...]
    correction_ref[...] = mixed(anchor, 0) + mixed(first, VECS)
    residual_ref[...] = anchor - (mixed(first, 0) + mixed(second, VECS))


def mix_outputs(coefficients, anchor, first, second):
    whole = pl.BlockSpec(memory_space=pltpu.VMEM)
    return pl.pallas_call(
        mixing_kernel,
        out_shape=(jax.ShapeDtypeStruct(anchor.shape, jnp.float32),) * 2,
        in_specs=[pl.BlockSpec(memory_space=pltpu.SMEM), whole, whole, whole],
        out_specs=(whole, whole),
    )(coefficients, anchor, first, second)


def per_device(start_block, jacobian, counts, columns, send_list):
    lend_rows = send_list[0]
    jac_t = jnp.transpose(jacobian, (1, 0, 2))

    def ghosts(outgoing):
        wide, narrow = lax.axis_size("wide"), lax.axis_size("narrow")
        return (
            lax.ppermute(outgoing[0], "wide", [(i, i + 1) for i in range(wide - 1)]),
            lax.ppermute(outgoing[1], "wide", [(i + 1, i) for i in range(wide - 1)]),
            lax.ppermute(outgoing[2], "narrow", [(i, i + 1) for i in range(narrow - 1)]),
            lax.ppermute(outgoing[3], "narrow", [(i + 1, i) for i in range(narrow - 1)]),
        )

    cols_t = jnp.transpose(columns, (1, 0))
    first = apply_operator(jac_t, start_block, ghosts(lent_rows_of(start_block, lend_rows)), cols_t, counts, lend_rows)
    first_image, first_lent, anchor = first[0], jnp.stack(first[1:5]), first[5]
    peers = lax.axis_size("wide") * lax.axis_size("narrow")
    second = apply_operator(jac_t, first_image, ghosts(first_lent), cols_t, counts, lend_rows, anchor, peers)
    second_image, raw_gram = second
    everyone = lax.all_to_all(raw_gram, ("wide", "narrow"), 0, 0, tiled=True)
    raw_gram = jnp.transpose(jnp.sum(everyone, axis=0), (1, 0)).reshape(5, VECS, VECS)
    shift = np.arange(VECS)[:, None, None]
    row_c = np.arange(VECS)[None, :, None]
    col_d = np.arange(VECS)[None, None, :]
    pick = jnp.asarray(((row_c - col_d) % VECS == shift).astype(np.float32))
    gram_parts = jnp.sum(raw_gram[:, :, :, None] * pick[None], axis=1)
    normal_matrix = jnp.concatenate(
        [
            jnp.concatenate([gram_parts[1], gram_parts[3].T], 1),
            jnp.concatenate([gram_parts[3], gram_parts[4]], 1),
        ],
        0,
    )
    right_terms = jnp.concatenate([gram_parts[0], gram_parts[2]], 0)
    factor = lax.linalg.cholesky(normal_matrix, symmetrize_input=False)
    coefficients = jax.scipy.linalg.cho_solve((factor, True), right_terms)
    return mix_outputs(coefficients, anchor, first_image, second_image)


def solution(mesh):
    placed = (
        P(("wide", "narrow"), None),
        P(("wide", "narrow"), None, None),
        P(("wide", "narrow")),
        P(("wide", "narrow"), None),
        P(("wide", "narrow"), None, None),
    )
    return jax.shard_map(
        per_device,
        mesh=mesh,
        in_specs=placed,
        out_specs=(P(("wide", "narrow"), None), P(("wide", "narrow"), None)),
        check_vma=False,
    )
```

```python
import functools

import jax
import jax.numpy as jnp
import numpy as np
from jax import lax
from jax.experimental import pallas as pl
from jax.experimental.pallas import tpu as pltpu
from jax.sharding import PartitionSpec as P

BLK = 64
VECS = 4
NB = 5
E_DEV = 128
LANES = 128
SUBLANES = 8
UNROLL = 32
CHUNK_ROWS = 16
ROWS_PER_STEP = 32


DIAG_SHIFT = 1.5


def padded(cells, sides, width):
    for axis, dim in sides:
        count = lax.axis_size(axis)
        ends = count - 1
        head = lax.slice_in_dim(cells, 0, width, axis=dim)
        tail = lax.slice_in_dim(cells, cells.shape[dim] - width, cells.shape[dim], axis=dim)
        cells = jnp.concatenate(
            [
                lax.ppermute(tail, axis, [(i, (i + 1) % count) for i in range(ends)]),
                cells,
                lax.ppermute(head, axis, [((i + 1) % count, i) for i in range(ends)]),
            ],
            axis=dim,
        )
    return cells


def combine(values, mixing):
    shaped = values.reshape(values.shape[0], VECS, BLK)
    return jnp.einsum("eci,cd->edi", shaped, mixing, precision=lax.Precision.HIGHEST).reshape(
        values.shape[0], VECS * BLK
    )


def inner_block(left_side, right_side):
    left_shaped = left_side.reshape(left_side.shape[0], VECS, BLK)
    right_shaped = right_side.reshape(right_side.shape[0], VECS, BLK)
    return jnp.einsum("eci,edi->cd", left_shaped, right_shaped, precision=lax.Precision.HIGHEST)


def tree_sum(values, axes):
    for axis in axes:
        count = lax.axis_size(axis)
        if count & (count - 1):
            values = lax.psum(values, axis)
            continue
        stride = 1
        while stride < count:
            values = values + lax.ppermute(values, axis, [(i, i ^ stride) for i in range(count)])
            stride *= 2
    return values


def split_three(values):
    high = values.astype(jnp.bfloat16)
    rest = values - high.astype(jnp.float32)
    middle = rest.astype(jnp.bfloat16)
    low = (rest - middle.astype(jnp.float32)).astype(jnp.bfloat16)
    return jnp.concatenate([high, middle, low], axis=1)


def exchange_sum(values, axes):
    count = 1
    for axis in axes:
        count *= lax.axis_size(axis)
    flat = values.reshape(1, -1)
    everyone = lax.all_to_all(jnp.broadcast_to(flat, (count, flat.shape[1])), axes, 0, 0, tiled=True)
    return jnp.sum(everyone, axis=0).reshape(values.shape)


def segment_sums(values, segments):
    width = values.shape[1]
    seg = (
        lax.broadcasted_iota(jnp.int32, (width, segments), 0) // (width // segments)
        == lax.broadcasted_iota(jnp.int32, (width, segments), 1)
    ).astype(jnp.bfloat16)
    parts = split_three(values)
    return (
        jnp.dot(parts[:, 0:width], seg, preferred_element_type=jnp.float32)
        + jnp.dot(parts[:, width:2 * width], seg, preferred_element_type=jnp.float32)
        + jnp.dot(parts[:, 2 * width:3 * width], seg, preferred_element_type=jnp.float32)
    )


def gram_columns(pairs):
    rows = []
    for left, right in pairs:
        for shift in range(VECS):
            moved = right if shift == 0 else pltpu.roll(right, shift * BLK, 1)
            rows.append(jnp.sum(left * moved, axis=0, keepdims=True))
    stacked = jnp.concatenate(rows, axis=0)
    width = stacked.shape[1]
    seg = (
        lax.broadcasted_iota(jnp.int32, (VECS, width), 1) // BLK
        == lax.broadcasted_iota(jnp.int32, (VECS, width), 0)
    ).astype(jnp.bfloat16)
    parts = split_three(stacked)
    dims = (((1,), (1,)), ((), ()))
    return sum(
        lax.dot_general(seg, parts[:, p * width:(p + 1) * width], dims, preferred_element_type=jnp.float32)
        for p in range(3)
    )


def coupling_kernel(with_gram, count_ref, lend_ref, jac_hbm, own_ref, g0_ref, g1_ref, g2_ref, g3_ref, cols_ref, *rest):
    if with_gram:
        anchor_ref, out_ref, gram_ref = rest[:3]
        rest = rest[3:]
    else:
        out_ref, l0_ref, l1_ref, l2_ref, l3_ref, kept_ref = rest[:6]
        rest = rest[6:]
    jac_ref, sems, source_ref, picked_ref, z_ref, parts_ref = rest
    tiles = jac_ref.shape[2] // LANES
    count = own_ref.shape[0]
    width = own_ref.shape[1]
    ghost = g0_ref.shape[0]
    chunks = sems.shape[0]
    chunk_rows = count // chunks

    def chunk_copy(b):
        rows = pl.ds(pl.multiple_of(b * chunk_rows, chunk_rows), chunk_rows)
        return pltpu.make_async_copy(jac_hbm.at[:, rows, :], jac_ref.at[:, rows, :], sems.at[b])

    for b in range(chunks):
        chunk_copy(b).start()

    living = lax.broadcasted_iota(jnp.int32, (count, 1), 0) < count_ref[0]
    source_ref[0:count] = split_three(jnp.where(living, own_ref[...], jnp.float32(0.0)))
    for q, piece in enumerate((g0_ref, g1_ref, g2_ref, g3_ref)):
        source_ref[count + q * ghost:count + (q + 1) * ghost] = split_three(piece[...])
    slots = lax.broadcasted_iota(jnp.int32, (source_ref.shape[0], count), 0)
    for k in range(NB):
        chosen = (cols_ref[k:k + 1, :] == slots).astype(jnp.bfloat16)
        spread = lax.dot_general(
            chosen, source_ref[...], (((0,), (0,)), ((), ())), preferred_element_type=jnp.float32
        )
        picked_ref[k] = spread[:, 0:width] + spread[:, width:2 * width] + spread[:, 2 * width:3 * width]

    lane = lax.broadcasted_iota(jnp.int32, (SUBLANES, LANES), 1)

    def one_chunk(b, carry):
        chunk_copy(b).wait()
        for group in range(chunk_rows // SUBLANES):
            first_row = pl.multiple_of(b * chunk_rows + group * SUBLANES, SUBLANES)
            doubled = []
            for k in range(NB):
                per_vector = []
                for pair in range(VECS // 2):
                    tile = picked_ref[k, pl.ds(first_row, SUBLANES), pair * LANES:(pair + 1) * LANES]
                    swapped = pltpu.roll(tile, BLK, 1)
                    per_vector.append(jnp.where(lane < BLK, tile, swapped))
                    per_vector.append(jnp.where(lane >= BLK, tile, swapped))
                doubled.append(per_vector)

            def one_tile(t, inner):
                off = pl.multiple_of(t * LANES, LANES)
                blocks = [jac_ref[k, pl.ds(first_row, SUBLANES), pl.ds(off, LANES)] for k in range(NB)]
                for c in range(VECS):
                    terms = [blocks[k] * doubled[k][c] for k in range(NB)]
                    while len(terms) > 1:
                        terms = [terms[i] + terms[i + 1] for i in range(0, len(terms) - 1, 2)] + (
                            [terms[-1]] if len(terms) % 2 else []
                        )
                    z_ref[c, pl.ds(first_row, SUBLANES), pl.ds(off, LANES)] = terms[0]
                return inner

            lax.fori_loop(0, tiles, one_tile, 0, unroll=UNROLL)
        return carry

    lax.fori_loop(0, chunks, one_chunk, 0, unroll=True)

    full = tiles * LANES
    for c in range(VECS):
        total = z_ref[c]
        high = total.astype(jnp.bfloat16)
        parts_ref[2 * c] = high
        parts_ref[2 * c + 1] = (total - high.astype(jnp.float32)).astype(jnp.bfloat16)
    flat = parts_ref[...].reshape(2 * VECS * count, full)
    seg = (
        lax.broadcasted_iota(jnp.int32, (full, BLK), 0) // BLK
        == lax.broadcasted_iota(jnp.int32, (full, BLK), 1)
    ).astype(jnp.bfloat16)
    sums = jnp.dot(flat, seg, preferred_element_type=jnp.float32)
    coupled = jnp.concatenate(
        [sums[(2 * c) * count:(2 * c + 1) * count] + sums[(2 * c + 1) * count:(2 * c + 2) * count] for c in range(VECS)],
        axis=1,
    )
    own = own_ref[...]
    image = jnp.where(living, DIAG_SHIFT * own + coupled, jnp.float32(0.0))
    out_ref[...] = image
    kept = jnp.where(living, own, jnp.float32(0.0))
    if not with_gram:
        kept_ref[...] = kept
        for q, lent_ref in enumerate((l0_ref, l1_ref, l2_ref, l3_ref)):
            for j in range(lend_ref.shape[1]):
                lent_ref[j:j + 1, :] = out_ref[pl.ds(lend_ref[q, j], 1), :]
    else:
        anchor = anchor_ref[...]
        partial = gram_columns(((kept, anchor), (kept, kept), (image, anchor), (image, kept), (image, image)))
        for target in range(gram_ref.shape[0]):
            gram_ref[target] = partial


def apply_operator(jac_t, own, ghost_rows, cols_t, counts, lend_rows, anchor=None, peers=1):
    blocks, count, full = jac_t.shape
    width = own.shape[1]
    ghost = ghost_rows[0].shape[0]
    chunks = max(count // CHUNK_ROWS, 1)
    with_gram = anchor is not None
    smem = pl.BlockSpec(memory_space=pltpu.SMEM)
    vmem = pl.BlockSpec(memory_space=pltpu.VMEM)
    lent = lend_rows.shape[1]
    in_specs = [smem, smem, pl.BlockSpec(memory_space=pl.ANY), vmem, vmem, vmem, vmem, vmem, vmem]
    out_shape = [jax.ShapeDtypeStruct((count, width), jnp.float32)]
    args = [counts, lend_rows, jac_t, own, *ghost_rows, cols_t]
    if with_gram:
        in_specs.append(vmem)
        args.append(anchor)
        out_shape.append(jax.ShapeDtypeStruct((peers, VECS, 5 * VECS), jnp.float32))
    else:
        out_shape += [jax.ShapeDtypeStruct((lent, width), jnp.float32)] * lend_rows.shape[0]
        out_shape += [jax.ShapeDtypeStruct((count, width), jnp.float32)]
    return pl.pallas_call(
        functools.partial(coupling_kernel, with_gram),
        out_shape=tuple(out_shape),
        in_specs=in_specs,
        out_specs=tuple(vmem for _ in out_shape),
        scratch_shapes=[
            pltpu.VMEM((blocks, count, full), jnp.float32),
            pltpu.SemaphoreType.DMA((chunks,)),
            pltpu.VMEM((count + 4 * ghost, 3 * width), jnp.bfloat16),
            pltpu.VMEM((blocks, count, width), jnp.float32),
            pltpu.VMEM((VECS, count, full), jnp.float32),
            pltpu.VMEM((2 * VECS, count, full), jnp.bfloat16),
        ],
        cost_estimate=pl.CostEstimate(
            flops=2 * blocks * count * full * VECS + 2 * 2 * VECS * count * full * BLK,
            bytes_accessed=4 * (blocks * count * full + 6 * count * width),
            transcendentals=0,
        ),
    )(*args)


def lending_kernel(lend_ref, values_ref, *lent_refs):
    for q, lent_ref in enumerate(lent_refs):
        for j in range(lend_ref.shape[1]):
            lent_ref[j:j + 1, :] = values_ref[pl.ds(lend_ref[q, j], 1), :]


def lent_rows_of(values, lend_rows):
    shape = jax.ShapeDtypeStruct((lend_rows.shape[1], values.shape[1]), values.dtype)
    whole = pl.BlockSpec(memory_space=pltpu.VMEM)
    return pl.pallas_call(
        lending_kernel,
        out_shape=(shape,) * lend_rows.shape[0],
        in_specs=[pl.BlockSpec(memory_space=pltpu.SMEM), whole],
        out_specs=(whole,) * lend_rows.shape[0],
    )(lend_rows, values)


def mixing_kernel(mix_ref, anchor_ref, first_ref, second_ref, correction_ref, residual_ref):
    width = anchor_ref.shape[1]
    segment = lax.broadcasted_iota(jnp.int32, (1, width), 1) // BLK

    def weights(row_offset, shift):
        out = jnp.zeros((1, width), jnp.float32)
        for d in range(VECS):
            out = jnp.where(segment == d, mix_ref[row_offset + (d - shift) % VECS, d], out)
        return out

    def mixed(values, row_offset):
        total = None
        for shift in range(VECS):
            moved = values if shift == 0 else pltpu.roll(values, shift * BLK, 1)
            term = moved * weights(row_offset, shift)
            total = term if total is None else total + term
        return total

    anchor = anchor_ref[...]
    first = first_ref[...]
    second = second_ref[...]
    correction_ref[...] = mixed(anchor, 0) + mixed(first, VECS)
    residual_ref[...] = anchor - (mixed(first, 0) + mixed(second, VECS))


def mix_outputs(coefficients, anchor, first, second):
    whole = pl.BlockSpec(memory_space=pltpu.VMEM)
    return pl.pallas_call(
        mixing_kernel,
        out_shape=(jax.ShapeDtypeStruct(anchor.shape, jnp.float32),) * 2,
        in_specs=[pl.BlockSpec(memory_space=pltpu.SMEM), whole, whole, whole],
        out_specs=(whole, whole),
    )(coefficients, anchor, first, second)


def per_device(start_block, jacobian, counts, columns, send_list):
    lend_rows = send_list[0]
    jac_t = jnp.transpose(jacobian, (1, 0, 2))

    def ghosts(outgoing):
        wide, narrow = lax.axis_size("wide"), lax.axis_size("narrow")
        return (
            lax.ppermute(outgoing[0], "wide", [(i, i + 1) for i in range(wide - 1)]),
            lax.ppermute(outgoing[1], "wide", [(i + 1, i) for i in range(wide - 1)]),
            lax.ppermute(outgoing[2], "narrow", [(i, i + 1) for i in range(narrow - 1)]),
            lax.ppermute(outgoing[3], "narrow", [(i + 1, i) for i in range(narrow - 1)]),
        )

    cols_t = jnp.transpose(columns, (1, 0))
    first = apply_operator(jac_t, start_block, ghosts(lent_rows_of(start_block, lend_rows)), cols_t, counts, lend_rows)
    first_image, first_lent, anchor = first[0], jnp.stack(first[1:5]), first[5]
    peers = lax.axis_size("wide") * lax.axis_size("narrow")
    second = apply_operator(jac_t, first_image, ghosts(first_lent), cols_t, counts, lend_rows, anchor, peers)
    second_image, raw_gram = second
    everyone = lax.all_to_all(raw_gram, ("wide", "narrow"), 0, 0, tiled=True)
    raw_gram = jnp.transpose(jnp.sum(everyone, axis=0), (1, 0)).reshape(5, VECS, VECS)
    shift = np.arange(VECS)[:, None, None]
    row_c = np.arange(VECS)[None, :, None]
    col_d = np.arange(VECS)[None, None, :]
    pick = jnp.asarray(((row_c - col_d) % VECS == shift).astype(np.float32))
    gram_parts = jnp.sum(raw_gram[:, :, :, None] * pick[None], axis=1)
    normal_matrix = jnp.concatenate(
        [
            jnp.concatenate([gram_parts[1], gram_parts[3].T], 1),
            jnp.concatenate([gram_parts[3], gram_parts[4]], 1),
        ],
        0,
    )
    right_terms = jnp.concatenate([gram_parts[0], gram_parts[2]], 0)
    factor = jnp.linalg.cholesky(normal_matrix)
    coefficients = jax.scipy.linalg.cho_solve((factor, True), right_terms)
    return mix_outputs(coefficients, anchor, first_image, second_image)


def solution(mesh):
    placed = (
        P(("wide", "narrow"), None),
        P(("wide", "narrow"), None, None),
        P(("wide", "narrow")),
        P(("wide", "narrow"), None),
        P(("wide", "narrow"), None, None),
    )
    return jax.shard_map(
        per_device,
        mesh=mesh,
        in_specs=placed,
        out_specs=(P(("wide", "narrow"), None), P(("wide", "narrow"), None)),
        check_vma=False,
    )
```

```python
import functools

import jax
import jax.numpy as jnp
import numpy as np
from jax import lax
from jax.experimental import pallas as pl
from jax.experimental.pallas import tpu as pltpu
from jax.sharding import PartitionSpec as P

BLK = 64
VECS = 4
NB = 5
E_DEV = 128
LANES = 128
SUBLANES = 8
UNROLL = 32
CHUNK_ROWS = 8
ROWS_PER_STEP = 32


DIAG_SHIFT = 1.5


def padded(cells, sides, width):
    for axis, dim in sides:
        count = lax.axis_size(axis)
        ends = count - 1
        head = lax.slice_in_dim(cells, 0, width, axis=dim)
        tail = lax.slice_in_dim(cells, cells.shape[dim] - width, cells.shape[dim], axis=dim)
        cells = jnp.concatenate(
            [
                lax.ppermute(tail, axis, [(i, (i + 1) % count) for i in range(ends)]),
                cells,
                lax.ppermute(head, axis, [((i + 1) % count, i) for i in range(ends)]),
            ],
            axis=dim,
        )
    return cells


def combine(values, mixing):
    shaped = values.reshape(values.shape[0], VECS, BLK)
    return jnp.einsum("eci,cd->edi", shaped, mixing, precision=lax.Precision.HIGHEST).reshape(
        values.shape[0], VECS * BLK
    )


def inner_block(left_side, right_side):
    left_shaped = left_side.reshape(left_side.shape[0], VECS, BLK)
    right_shaped = right_side.reshape(right_side.shape[0], VECS, BLK)
    return jnp.einsum("eci,edi->cd", left_shaped, right_shaped, precision=lax.Precision.HIGHEST)


def tree_sum(values, axes):
    for axis in axes:
        count = lax.axis_size(axis)
        if count & (count - 1):
            values = lax.psum(values, axis)
            continue
        stride = 1
        while stride < count:
            values = values + lax.ppermute(values, axis, [(i, i ^ stride) for i in range(count)])
            stride *= 2
    return values


def split_three(values):
    high = values.astype(jnp.bfloat16)
    rest = values - high.astype(jnp.float32)
    middle = rest.astype(jnp.bfloat16)
    low = (rest - middle.astype(jnp.float32)).astype(jnp.bfloat16)
    return jnp.concatenate([high, middle, low], axis=1)


def exchange_sum(values, axes):
    count = 1
    for axis in axes:
        count *= lax.axis_size(axis)
    flat = values.reshape(1, -1)
    everyone = lax.all_to_all(jnp.broadcast_to(flat, (count, flat.shape[1])), axes, 0, 0, tiled=True)
    return jnp.sum(everyone, axis=0).reshape(values.shape)


def segment_sums(values, segments):
    width = values.shape[1]
    seg = (
        lax.broadcasted_iota(jnp.int32, (width, segments), 0) // (width // segments)
        == lax.broadcasted_iota(jnp.int32, (width, segments), 1)
    ).astype(jnp.bfloat16)
    parts = split_three(values)
    return (
        jnp.dot(parts[:, 0:width], seg, preferred_element_type=jnp.float32)
        + jnp.dot(parts[:, width:2 * width], seg, preferred_element_type=jnp.float32)
        + jnp.dot(parts[:, 2 * width:3 * width], seg, preferred_element_type=jnp.float32)
    )


def gram_columns(pairs):
    rows = []
    for left, right in pairs:
        for shift in range(VECS):
            moved = right if shift == 0 else pltpu.roll(right, shift * BLK, 1)
            rows.append(jnp.sum(left * moved, axis=0, keepdims=True))
    stacked = jnp.concatenate(rows, axis=0)
    width = stacked.shape[1]
    seg = (
        lax.broadcasted_iota(jnp.int32, (VECS, width), 1) // BLK
        == lax.broadcasted_iota(jnp.int32, (VECS, width), 0)
    ).astype(jnp.bfloat16)
    parts = split_three(stacked)
    dims = (((1,), (1,)), ((), ()))
    return sum(
        lax.dot_general(seg, parts[:, p * width:(p + 1) * width], dims, preferred_element_type=jnp.float32)
        for p in range(3)
    )


def coupling_kernel(with_gram, count_ref, lend_ref, jac_hbm, own_ref, g0_ref, g1_ref, g2_ref, g3_ref, cols_ref, *rest):
    if with_gram:
        anchor_ref, out_ref, gram_ref = rest[:3]
        rest = rest[3:]
    else:
        out_ref, l0_ref, l1_ref, l2_ref, l3_ref, kept_ref = rest[:6]
        rest = rest[6:]
    jac_ref, sems, source_ref, picked_ref, z_ref, parts_ref = rest
    tiles = jac_ref.shape[2] // LANES
    count = own_ref.shape[0]
    width = own_ref.shape[1]
    ghost = g0_ref.shape[0]
    chunks = sems.shape[0]
    chunk_rows = count // chunks

    def chunk_copy(b):
        rows = pl.ds(pl.multiple_of(b * chunk_rows, chunk_rows), chunk_rows)
        return pltpu.make_async_copy(jac_hbm.at[:, rows, :], jac_ref.at[:, rows, :], sems.at[b])

    for b in range(chunks):
        chunk_copy(b).start()

    living = lax.broadcasted_iota(jnp.int32, (count, 1), 0) < count_ref[0]
    source_ref[0:count] = split_three(jnp.where(living, own_ref[...], jnp.float32(0.0)))
    for q, piece in enumerate((g0_ref, g1_ref, g2_ref, g3_ref)):
        source_ref[count + q * ghost:count + (q + 1) * ghost] = split_three(piece[...])
    slots = lax.broadcasted_iota(jnp.int32, (source_ref.shape[0], count), 0)
    for k in range(NB):
        chosen = (cols_ref[k:k + 1, :] == slots).astype(jnp.bfloat16)
        spread = lax.dot_general(
            chosen, source_ref[...], (((0,), (0,)), ((), ())), preferred_element_type=jnp.float32
        )
        picked_ref[k] = spread[:, 0:width] + spread[:, width:2 * width] + spread[:, 2 * width:3 * width]

    lane = lax.broadcasted_iota(jnp.int32, (SUBLANES, LANES), 1)

    def one_chunk(b, carry):
        chunk_copy(b).wait()
        for group in range(chunk_rows // SUBLANES):
            first_row = pl.multiple_of(b * chunk_rows + group * SUBLANES, SUBLANES)
            doubled = []
            for k in range(NB):
                per_vector = []
                for pair in range(VECS // 2):
                    tile = picked_ref[k, pl.ds(first_row, SUBLANES), pair * LANES:(pair + 1) * LANES]
                    swapped = pltpu.roll(tile, BLK, 1)
                    per_vector.append(jnp.where(lane < BLK, tile, swapped))
                    per_vector.append(jnp.where(lane >= BLK, tile, swapped))
                doubled.append(per_vector)

            def one_tile(t, inner):
                off = pl.multiple_of(t * LANES, LANES)
                blocks = [jac_ref[k, pl.ds(first_row, SUBLANES), pl.ds(off, LANES)] for k in range(NB)]
                for c in range(VECS):
                    terms = [blocks[k] * doubled[k][c] for k in range(NB)]
                    while len(terms) > 1:
                        terms = [terms[i] + terms[i + 1] for i in range(0, len(terms) - 1, 2)] + (
                            [terms[-1]] if len(terms) % 2 else []
                        )
                    z_ref[c, pl.ds(first_row, SUBLANES), pl.ds(off, LANES)] = terms[0]
                return inner

            lax.fori_loop(0, tiles, one_tile, 0, unroll=UNROLL)
        return carry

    lax.fori_loop(0, chunks, one_chunk, 0, unroll=True)

    full = tiles * LANES
    for c in range(VECS):
        total = z_ref[c]
        high = total.astype(jnp.bfloat16)
        parts_ref[2 * c] = high
        parts_ref[2 * c + 1] = (total - high.astype(jnp.float32)).astype(jnp.bfloat16)
    flat = parts_ref[...].reshape(2 * VECS * count, full)
    seg = (
        lax.broadcasted_iota(jnp.int32, (full, BLK), 0) // BLK
        == lax.broadcasted_iota(jnp.int32, (full, BLK), 1)
    ).astype(jnp.bfloat16)
    sums = jnp.dot(flat, seg, preferred_element_type=jnp.float32)
    coupled = jnp.concatenate(
        [sums[(2 * c) * count:(2 * c + 1) * count] + sums[(2 * c + 1) * count:(2 * c + 2) * count] for c in range(VECS)],
        axis=1,
    )
    own = own_ref[...]
    image = jnp.where(living, DIAG_SHIFT * own + coupled, jnp.float32(0.0))
    out_ref[...] = image
    kept = jnp.where(living, own, jnp.float32(0.0))
    if not with_gram:
        kept_ref[...] = kept
        for q, lent_ref in enumerate((l0_ref, l1_ref, l2_ref, l3_ref)):
            for j in range(lend_ref.shape[1]):
                lent_ref[j:j + 1, :] = out_ref[pl.ds(lend_ref[q, j], 1), :]
    else:
        anchor = anchor_ref[...]
        partial = gram_columns(((kept, anchor), (kept, kept), (image, anchor), (image, kept), (image, image)))
        for target in range(gram_ref.shape[0]):
            gram_ref[target] = partial


def apply_operator(jac_t, own, ghost_rows, cols_t, counts, lend_rows, anchor=None, peers=1):
    blocks, count, full = jac_t.shape
    width = own.shape[1]
    ghost = ghost_rows[0].shape[0]
    chunks = max(count // CHUNK_ROWS, 1)
    with_gram = anchor is not None
    smem = pl.BlockSpec(memory_space=pltpu.SMEM)
    vmem = pl.BlockSpec(memory_space=pltpu.VMEM)
    lent = lend_rows.shape[1]
    in_specs = [smem, smem, pl.BlockSpec(memory_space=pl.ANY), vmem, vmem, vmem, vmem, vmem, vmem]
    out_shape = [jax.ShapeDtypeStruct((count, width), jnp.float32)]
    args = [counts, lend_rows, jac_t, own, *ghost_rows, cols_t]
    if with_gram:
        in_specs.append(vmem)
        args.append(anchor)
        out_shape.append(jax.ShapeDtypeStruct((peers, VECS, 5 * VECS), jnp.float32))
    else:
        out_shape += [jax.ShapeDtypeStruct((lent, width), jnp.float32)] * lend_rows.shape[0]
        out_shape += [jax.ShapeDtypeStruct((count, width), jnp.float32)]
    return pl.pallas_call(
        functools.partial(coupling_kernel, with_gram),
        out_shape=tuple(out_shape),
        in_specs=in_specs,
        out_specs=tuple(vmem for _ in out_shape),
        scratch_shapes=[
            pltpu.VMEM((blocks, count, full), jnp.float32),
            pltpu.SemaphoreType.DMA((chunks,)),
            pltpu.VMEM((count + 4 * ghost, 3 * width), jnp.bfloat16),
            pltpu.VMEM((blocks, count, width), jnp.float32),
            pltpu.VMEM((VECS, count, full), jnp.float32),
            pltpu.VMEM((2 * VECS, count, full), jnp.bfloat16),
        ],
        cost_estimate=pl.CostEstimate(
            flops=2 * blocks * count * full * VECS + 2 * 2 * VECS * count * full * BLK,
            bytes_accessed=4 * (blocks * count * full + 6 * count * width),
            transcendentals=0,
        ),
    )(*args)


def lending_kernel(lend_ref, values_ref, *lent_refs):
    for q, lent_ref in enumerate(lent_refs):
        for j in range(lend_ref.shape[1]):
            lent_ref[j:j + 1, :] = values_ref[pl.ds(lend_ref[q, j], 1), :]


def lent_rows_of(values, lend_rows):
    shape = jax.ShapeDtypeStruct((lend_rows.shape[1], values.shape[1]), values.dtype)
    whole = pl.BlockSpec(memory_space=pltpu.VMEM)
    return pl.pallas_call(
        lending_kernel,
        out_shape=(shape,) * lend_rows.shape[0],
        in_specs=[pl.BlockSpec(memory_space=pltpu.SMEM), whole],
        out_specs=(whole,) * lend_rows.shape[0],
    )(lend_rows, values)


def mixing_kernel(mix_ref, anchor_ref, first_ref, second_ref, correction_ref, residual_ref):
    width = anchor_ref.shape[1]
    segment = lax.broadcasted_iota(jnp.int32, (1, width), 1) // BLK

    def weights(row_offset, shift):
        out = jnp.zeros((1, width), jnp.float32)
        for d in range(VECS):
            out = jnp.where(segment == d, mix_ref[row_offset + (d - shift) % VECS, d], out)
        return out

    def mixed(values, row_offset):
        total = None
        for shift in range(VECS):
            moved = values if shift == 0 else pltpu.roll(values, shift * BLK, 1)
            term = moved * weights(row_offset, shift)
            total = term if total is None else total + term
        return total

    anchor = anchor_ref[...]
    first = first_ref[...]
    second = second_ref[...]
    correction_ref[...] = mixed(anchor, 0) + mixed(first, VECS)
    residual_ref[...] = anchor - (mixed(first, 0) + mixed(second, VECS))


def mix_outputs(coefficients, anchor, first, second):
    whole = pl.BlockSpec(memory_space=pltpu.VMEM)
    return pl.pallas_call(
        mixing_kernel,
        out_shape=(jax.ShapeDtypeStruct(anchor.shape, jnp.float32),) * 2,
        in_specs=[pl.BlockSpec(memory_space=pltpu.SMEM), whole, whole, whole],
        out_specs=(whole, whole),
    )(coefficients, anchor, first, second)


def per_device(start_block, jacobian, counts, columns, send_list):
    lend_rows = send_list[0]
    jac_t = jnp.transpose(jacobian, (1, 0, 2))

    def ghosts(outgoing):
        wide, narrow = lax.axis_size("wide"), lax.axis_size("narrow")
        return (
            lax.ppermute(outgoing[0], "wide", [(i, i + 1) for i in range(wide - 1)]),
            lax.ppermute(outgoing[1], "wide", [(i + 1, i) for i in range(wide - 1)]),
            lax.ppermute(outgoing[2], "narrow", [(i, i + 1) for i in range(narrow - 1)]),
            lax.ppermute(outgoing[3], "narrow", [(i + 1, i) for i in range(narrow - 1)]),
        )

    cols_t = jnp.transpose(columns, (1, 0))
    first = apply_operator(jac_t, start_block, ghosts(lent_rows_of(start_block, lend_rows)), cols_t, counts, lend_rows)
    first_image, first_lent, anchor = first[0], jnp.stack(first[1:5]), first[5]
    peers = lax.axis_size("wide") * lax.axis_size("narrow")
    second = apply_operator(jac_t, first_image, ghosts(first_lent), cols_t, counts, lend_rows, anchor, peers)
    second_image, raw_gram = second
    everyone = lax.all_to_all(raw_gram, ("wide", "narrow"), 0, 0, tiled=True)
    raw_gram = jnp.transpose(jnp.sum(everyone, axis=0), (1, 0)).reshape(5, VECS, VECS)
    shift = np.arange(VECS)[:, None, None]
    row_c = np.arange(VECS)[None, :, None]
    col_d = np.arange(VECS)[None, None, :]
    pick = jnp.asarray(((row_c - col_d) % VECS == shift).astype(np.float32))
    gram_parts = jnp.sum(raw_gram[:, :, :, None] * pick[None], axis=1)
    normal_matrix = jnp.concatenate(
        [
            jnp.concatenate([gram_parts[1], gram_parts[3].T], 1),
            jnp.concatenate([gram_parts[3], gram_parts[4]], 1),
        ],
        0,
    )
    right_terms = jnp.concatenate([gram_parts[0], gram_parts[2]], 0)
    factor = jnp.linalg.cholesky(normal_matrix)
    coefficients = jax.scipy.linalg.cho_solve((factor, True), right_terms)
    return mix_outputs(coefficients, anchor, first_image, second_image)


def solution(mesh):
    placed = (
        P(("wide", "narrow"), None),
        P(("wide", "narrow"), None, None),
        P(("wide", "narrow")),
        P(("wide", "narrow"), None),
        P(("wide", "narrow"), None, None),
    )
    return jax.shard_map(
        per_device,
        mesh=mesh,
        in_specs=placed,
        out_specs=(P(("wide", "narrow"), None), P(("wide", "narrow"), None)),
        check_vma=False,
    )
```

```python
import functools

import jax
import jax.numpy as jnp
import numpy as np
from jax import lax
from jax.experimental import pallas as pl
from jax.experimental.pallas import tpu as pltpu
from jax.sharding import PartitionSpec as P

BLK = 64
VECS = 4
NB = 5
E_DEV = 128
LANES = 128
SUBLANES = 8
UNROLL = 32
CHUNK_ROWS = 16
ROWS_PER_STEP = 32


DIAG_SHIFT = 1.5


def padded(cells, sides, width):
    for axis, dim in sides:
        count = lax.axis_size(axis)
        ends = count - 1
        head = lax.slice_in_dim(cells, 0, width, axis=dim)
        tail = lax.slice_in_dim(cells, cells.shape[dim] - width, cells.shape[dim], axis=dim)
        cells = jnp.concatenate(
            [
                lax.ppermute(tail, axis, [(i, (i + 1) % count) for i in range(ends)]),
                cells,
                lax.ppermute(head, axis, [((i + 1) % count, i) for i in range(ends)]),
            ],
            axis=dim,
        )
    return cells


def combine(values, mixing):
    shaped = values.reshape(values.shape[0], VECS, BLK)
    return jnp.einsum("eci,cd->edi", shaped, mixing, precision=lax.Precision.HIGHEST).reshape(
        values.shape[0], VECS * BLK
    )


def inner_block(left_side, right_side):
    left_shaped = left_side.reshape(left_side.shape[0], VECS, BLK)
    right_shaped = right_side.reshape(right_side.shape[0], VECS, BLK)
    return jnp.einsum("eci,edi->cd", left_shaped, right_shaped, precision=lax.Precision.HIGHEST)


def tree_sum(values, axes):
    for axis in axes:
        count = lax.axis_size(axis)
        if count & (count - 1):
            values = lax.psum(values, axis)
            continue
        stride = 1
        while stride < count:
            values = values + lax.ppermute(values, axis, [(i, i ^ stride) for i in range(count)])
            stride *= 2
    return values


def split_three(values):
    high = values.astype(jnp.bfloat16)
    rest = values - high.astype(jnp.float32)
    middle = rest.astype(jnp.bfloat16)
    low = (rest - middle.astype(jnp.float32)).astype(jnp.bfloat16)
    return jnp.concatenate([high, middle, low], axis=1)


def exchange_sum(values, axes):
    count = 1
    for axis in axes:
        count *= lax.axis_size(axis)
    flat = values.reshape(1, -1)
    everyone = lax.all_to_all(jnp.broadcast_to(flat, (count, flat.shape[1])), axes, 0, 0, tiled=True)
    return jnp.sum(everyone, axis=0).reshape(values.shape)


def segment_sums(values, segments):
    width = values.shape[1]
    seg = (
        lax.broadcasted_iota(jnp.int32, (width, segments), 0) // (width // segments)
        == lax.broadcasted_iota(jnp.int32, (width, segments), 1)
    ).astype(jnp.bfloat16)
    parts = split_three(values)
    return (
        jnp.dot(parts[:, 0:width], seg, preferred_element_type=jnp.float32)
        + jnp.dot(parts[:, width:2 * width], seg, preferred_element_type=jnp.float32)
        + jnp.dot(parts[:, 2 * width:3 * width], seg, preferred_element_type=jnp.float32)
    )


def gram_columns(pairs):
    rows = []
    for left, right in pairs:
        for shift in range(VECS):
            moved = right if shift == 0 else pltpu.roll(right, shift * BLK, 1)
            rows.append(jnp.sum(left * moved, axis=0, keepdims=True))
    stacked = jnp.concatenate(rows, axis=0)
    width = stacked.shape[1]
    seg = (
        lax.broadcasted_iota(jnp.int32, (VECS, width), 1) // BLK
        == lax.broadcasted_iota(jnp.int32, (VECS, width), 0)
    ).astype(jnp.bfloat16)
    parts = split_three(stacked)
    dims = (((1,), (1,)), ((), ()))
    return sum(
        lax.dot_general(seg, parts[:, p * width:(p + 1) * width], dims, preferred_element_type=jnp.float32)
        for p in range(3)
    )


def coupling_kernel(with_gram, count_ref, lend_ref, jac_hbm, own_ref, g0_ref, g1_ref, g2_ref, g3_ref, cols_ref, *rest):
    if with_gram:
        anchor_ref, out_ref, gram_ref = rest[:3]
        rest = rest[3:]
    else:
        out_ref, l0_ref, l1_ref, l2_ref, l3_ref, kept_ref = rest[:6]
        rest = rest[6:]
    jac_ref, sems, source_ref, picked_ref, z_ref, parts_ref = rest
    tiles = jac_ref.shape[2] // LANES
    count = own_ref.shape[0]
    width = own_ref.shape[1]
    ghost = g0_ref.shape[0]
    chunks = sems.shape[0]
    chunk_rows = count // chunks

    def chunk_copy(b):
        rows = pl.ds(pl.multiple_of(b * chunk_rows, chunk_rows), chunk_rows)
        return pltpu.make_async_copy(jac_hbm.at[:, rows, :], jac_ref.at[:, rows, :], sems.at[b])

    for b in range(chunks):
        chunk_copy(b).start()

    living = lax.broadcasted_iota(jnp.int32, (count, 1), 0) < count_ref[0]
    source_ref[0:count] = split_three(jnp.where(living, own_ref[...], jnp.float32(0.0)))
    for q, piece in enumerate((g0_ref, g1_ref, g2_ref, g3_ref)):
        source_ref[count + q * ghost:count + (q + 1) * ghost] = split_three(piece[...])
    slots = lax.broadcasted_iota(jnp.int32, (source_ref.shape[0], count), 0)
    for k in range(NB):
        chosen = (cols_ref[k:k + 1, :] == slots).astype(jnp.bfloat16)
        spread = lax.dot_general(
            chosen, source_ref[...], (((0,), (0,)), ((), ())), preferred_element_type=jnp.float32
        )
        picked_ref[k] = spread[:, 0:width] + spread[:, width:2 * width] + spread[:, 2 * width:3 * width]

    lane = lax.broadcasted_iota(jnp.int32, (SUBLANES, LANES), 1)

    def one_chunk(b, carry):
        chunk_copy(b).wait()
        for group in range(chunk_rows // SUBLANES):
            first_row = pl.multiple_of(b * chunk_rows + group * SUBLANES, SUBLANES)
            doubled = []
            for k in range(NB):
                per_vector = []
                for pair in range(VECS // 2):
                    tile = picked_ref[k, pl.ds(first_row, SUBLANES), pair * LANES:(pair + 1) * LANES]
                    swapped = pltpu.roll(tile, BLK, 1)
                    per_vector.append(jnp.where(lane < BLK, tile, swapped))
                    per_vector.append(jnp.where(lane >= BLK, tile, swapped))
                doubled.append(per_vector)

            def one_tile(t, inner):
                off = pl.multiple_of(t * LANES, LANES)
                blocks = [jac_ref[k, pl.ds(first_row, SUBLANES), pl.ds(off, LANES)] for k in range(NB)]
                for c in range(VECS):
                    terms = [blocks[k] * doubled[k][c] for k in range(NB)]
                    while len(terms) > 1:
                        terms = [terms[i] + terms[i + 1] for i in range(0, len(terms) - 1, 2)] + (
                            [terms[-1]] if len(terms) % 2 else []
                        )
                    z_ref[c, pl.ds(first_row, SUBLANES), pl.ds(off, LANES)] = terms[0]
                return inner

            lax.fori_loop(0, tiles, one_tile, 0, unroll=UNROLL)
        rows = pl.ds(pl.multiple_of(b * chunk_rows, chunk_rows), chunk_rows)
        for c in range(VECS):
            total = z_ref[c, rows, :]
            high = total.astype(jnp.bfloat16)
            parts_ref[2 * c, rows, :] = high
            parts_ref[2 * c + 1, rows, :] = (total - high.astype(jnp.float32)).astype(jnp.bfloat16)
        return carry

    lax.fori_loop(0, chunks, one_chunk, 0, unroll=True)

    full = tiles * LANES
    flat = parts_ref[...].reshape(2 * VECS * count, full)
    seg = (
        lax.broadcasted_iota(jnp.int32, (full, BLK), 0) // BLK
        == lax.broadcasted_iota(jnp.int32, (full, BLK), 1)
    ).astype(jnp.bfloat16)
    sums = jnp.dot(flat, seg, preferred_element_type=jnp.float32)
    coupled = jnp.concatenate(
        [sums[(2 * c) * count:(2 * c + 1) * count] + sums[(2 * c + 1) * count:(2 * c + 2) * count] for c in range(VECS)],
        axis=1,
    )
    own = own_ref[...]
    image = jnp.where(living, DIAG_SHIFT * own + coupled, jnp.float32(0.0))
    out_ref[...] = image
    kept = jnp.where(living, own, jnp.float32(0.0))
    if not with_gram:
        kept_ref[...] = kept
        for q, lent_ref in enumerate((l0_ref, l1_ref, l2_ref, l3_ref)):
            for j in range(lend_ref.shape[1]):
                lent_ref[j:j + 1, :] = out_ref[pl.ds(lend_ref[q, j], 1), :]
    else:
        anchor = anchor_ref[...]
        partial = gram_columns(((kept, anchor), (kept, kept), (image, anchor), (image, kept), (image, image)))
        for target in range(gram_ref.shape[0]):
            gram_ref[target] = partial


def apply_operator(jac_t, own, ghost_rows, cols_t, counts, lend_rows, anchor=None, peers=1):
    blocks, count, full = jac_t.shape
    width = own.shape[1]
    ghost = ghost_rows[0].shape[0]
    chunks = max(count // CHUNK_ROWS, 1)
    with_gram = anchor is not None
    smem = pl.BlockSpec(memory_space=pltpu.SMEM)
    vmem = pl.BlockSpec(memory_space=pltpu.VMEM)
    lent = lend_rows.shape[1]
    in_specs = [smem, smem, pl.BlockSpec(memory_space=pl.ANY), vmem, vmem, vmem, vmem, vmem, vmem]
    out_shape = [jax.ShapeDtypeStruct((count, width), jnp.float32)]
    args = [counts, lend_rows, jac_t, own, *ghost_rows, cols_t]
    if with_gram:
        in_specs.append(vmem)
        args.append(anchor)
        out_shape.append(jax.ShapeDtypeStruct((peers, VECS, 5 * VECS), jnp.float32))
    else:
        out_shape += [jax.ShapeDtypeStruct((lent, width), jnp.float32)] * lend_rows.shape[0]
        out_shape += [jax.ShapeDtypeStruct((count, width), jnp.float32)]
    return pl.pallas_call(
        functools.partial(coupling_kernel, with_gram),
        out_shape=tuple(out_shape),
        in_specs=in_specs,
        out_specs=tuple(vmem for _ in out_shape),
        scratch_shapes=[
            pltpu.VMEM((blocks, count, full), jnp.float32),
            pltpu.SemaphoreType.DMA((chunks,)),
            pltpu.VMEM((count + 4 * ghost, 3 * width), jnp.bfloat16),
            pltpu.VMEM((blocks, count, width), jnp.float32),
            pltpu.VMEM((VECS, count, full), jnp.float32),
            pltpu.VMEM((2 * VECS, count, full), jnp.bfloat16),
        ],
        cost_estimate=pl.CostEstimate(
            flops=2 * blocks * count * full * VECS + 2 * 2 * VECS * count * full * BLK,
            bytes_accessed=4 * (blocks * count * full + 6 * count * width),
            transcendentals=0,
        ),
    )(*args)


def lending_kernel(lend_ref, values_ref, *lent_refs):
    for q, lent_ref in enumerate(lent_refs):
        for j in range(lend_ref.shape[1]):
            lent_ref[j:j + 1, :] = values_ref[pl.ds(lend_ref[q, j], 1), :]


def lent_rows_of(values, lend_rows):
    shape = jax.ShapeDtypeStruct((lend_rows.shape[1], values.shape[1]), values.dtype)
    whole = pl.BlockSpec(memory_space=pltpu.VMEM)
    return pl.pallas_call(
        lending_kernel,
        out_shape=(shape,) * lend_rows.shape[0],
        in_specs=[pl.BlockSpec(memory_space=pltpu.SMEM), whole],
        out_specs=(whole,) * lend_rows.shape[0],
    )(lend_rows, values)


def mixing_kernel(mix_ref, anchor_ref, first_ref, second_ref, correction_ref, residual_ref):
    width = anchor_ref.shape[1]
    segment = lax.broadcasted_iota(jnp.int32, (1, width), 1) // BLK

    def weights(row_offset, shift):
        out = jnp.zeros((1, width), jnp.float32)
        for d in range(VECS):
            out = jnp.where(segment == d, mix_ref[row_offset + (d - shift) % VECS, d], out)
        return out

    def mixed(values, row_offset):
        total = None
        for shift in range(VECS):
            moved = values if shift == 0 else pltpu.roll(values, shift * BLK, 1)
            term = moved * weights(row_offset, shift)
            total = term if total is None else total + term
        return total

    anchor = anchor_ref[...]
    first = first_ref[...]
    second = second_ref[...]
    correction_ref[...] = mixed(anchor, 0) + mixed(first, VECS)
    residual_ref[...] = anchor - (mixed(first, 0) + mixed(second, VECS))


def mix_outputs(coefficients, anchor, first, second):
    whole = pl.BlockSpec(memory_space=pltpu.VMEM)
    return pl.pallas_call(
        mixing_kernel,
        out_shape=(jax.ShapeDtypeStruct(anchor.shape, jnp.float32),) * 2,
        in_specs=[pl.BlockSpec(memory_space=pltpu.SMEM), whole, whole, whole],
        out_specs=(whole, whole),
    )(coefficients, anchor, first, second)


def per_device(start_block, jacobian, counts, columns, send_list):
    lend_rows = send_list[0]
    jac_t = jnp.transpose(jacobian, (1, 0, 2))

    def ghosts(outgoing):
        wide, narrow = lax.axis_size("wide"), lax.axis_size("narrow")
        return (
            lax.ppermute(outgoing[0], "wide", [(i, i + 1) for i in range(wide - 1)]),
            lax.ppermute(outgoing[1], "wide", [(i + 1, i) for i in range(wide - 1)]),
            lax.ppermute(outgoing[2], "narrow", [(i, i + 1) for i in range(narrow - 1)]),
            lax.ppermute(outgoing[3], "narrow", [(i + 1, i) for i in range(narrow - 1)]),
        )

    cols_t = jnp.transpose(columns, (1, 0))
    first = apply_operator(jac_t, start_block, ghosts(lent_rows_of(start_block, lend_rows)), cols_t, counts, lend_rows)
    first_image, first_lent, anchor = first[0], jnp.stack(first[1:5]), first[5]
    peers = lax.axis_size("wide") * lax.axis_size("narrow")
    second = apply_operator(jac_t, first_image, ghosts(first_lent), cols_t, counts, lend_rows, anchor, peers)
    second_image, raw_gram = second
    everyone = lax.all_to_all(raw_gram, ("wide", "narrow"), 0, 0, tiled=True)
    raw_gram = jnp.transpose(jnp.sum(everyone, axis=0), (1, 0)).reshape(5, VECS, VECS)
    shift = np.arange(VECS)[:, None, None]
    row_c = np.arange(VECS)[None, :, None]
    col_d = np.arange(VECS)[None, None, :]
    pick = jnp.asarray(((row_c - col_d) % VECS == shift).astype(np.float32))
    gram_parts = jnp.sum(raw_gram[:, :, :, None] * pick[None], axis=1)
    normal_matrix = jnp.concatenate(
        [
            jnp.concatenate([gram_parts[1], gram_parts[3].T], 1),
            jnp.concatenate([gram_parts[3], gram_parts[4]], 1),
        ],
        0,
    )
    right_terms = jnp.concatenate([gram_parts[0], gram_parts[2]], 0)
    factor = jnp.linalg.cholesky(normal_matrix)
    coefficients = jax.scipy.linalg.cho_solve((factor, True), right_terms)
    return mix_outputs(coefficients, anchor, first_image, second_image)


def solution(mesh):
    placed = (
        P(("wide", "narrow"), None),
        P(("wide", "narrow"), None, None),
        P(("wide", "narrow")),
        P(("wide", "narrow"), None),
        P(("wide", "narrow"), None, None),
    )
    return jax.shard_map(
        per_device,
        mesh=mesh,
        in_specs=placed,
        out_specs=(P(("wide", "narrow"), None), P(("wide", "narrow"), None)),
        check_vma=False,
    )
```

```python
import functools

import jax
import jax.numpy as jnp
import numpy as np
from jax import lax
from jax.experimental import pallas as pl
from jax.experimental.pallas import tpu as pltpu
from jax.sharding import PartitionSpec as P

BLK = 64
VECS = 4
NB = 5
E_DEV = 128
LANES = 128
SUBLANES = 8
UNROLL = 32
CHUNK_ROWS = 16
ROWS_PER_STEP = 32


DIAG_SHIFT = 1.5


def padded(cells, sides, width):
    for axis, dim in sides:
        count = lax.axis_size(axis)
        ends = count - 1
        head = lax.slice_in_dim(cells, 0, width, axis=dim)
        tail = lax.slice_in_dim(cells, cells.shape[dim] - width, cells.shape[dim], axis=dim)
        cells = jnp.concatenate(
            [
                lax.ppermute(tail, axis, [(i, (i + 1) % count) for i in range(ends)]),
                cells,
                lax.ppermute(head, axis, [((i + 1) % count, i) for i in range(ends)]),
            ],
            axis=dim,
        )
    return cells


def combine(values, mixing):
    shaped = values.reshape(values.shape[0], VECS, BLK)
    return jnp.einsum("eci,cd->edi", shaped, mixing, precision=lax.Precision.HIGHEST).reshape(
        values.shape[0], VECS * BLK
    )


def inner_block(left_side, right_side):
    left_shaped = left_side.reshape(left_side.shape[0], VECS, BLK)
    right_shaped = right_side.reshape(right_side.shape[0], VECS, BLK)
    return jnp.einsum("eci,edi->cd", left_shaped, right_shaped, precision=lax.Precision.HIGHEST)


def tree_sum(values, axes):
    for axis in axes:
        count = lax.axis_size(axis)
        if count & (count - 1):
            values = lax.psum(values, axis)
            continue
        stride = 1
        while stride < count:
            values = values + lax.ppermute(values, axis, [(i, i ^ stride) for i in range(count)])
            stride *= 2
    return values


def split_three(values):
    high = values.astype(jnp.bfloat16)
    rest = values - high.astype(jnp.float32)
    middle = rest.astype(jnp.bfloat16)
    low = (rest - middle.astype(jnp.float32)).astype(jnp.bfloat16)
    return jnp.concatenate([high, middle, low], axis=1)


def exchange_sum(values, axes):
    count = 1
    for axis in axes:
        count *= lax.axis_size(axis)
    flat = values.reshape(1, -1)
    everyone = lax.all_to_all(jnp.broadcast_to(flat, (count, flat.shape[1])), axes, 0, 0, tiled=True)
    return jnp.sum(everyone, axis=0).reshape(values.shape)


def segment_sums(values, segments):
    width = values.shape[1]
    seg = (
        lax.broadcasted_iota(jnp.int32, (width, segments), 0) // (width // segments)
        == lax.broadcasted_iota(jnp.int32, (width, segments), 1)
    ).astype(jnp.bfloat16)
    parts = split_three(values)
    return (
        jnp.dot(parts[:, 0:width], seg, preferred_element_type=jnp.float32)
        + jnp.dot(parts[:, width:2 * width], seg, preferred_element_type=jnp.float32)
        + jnp.dot(parts[:, 2 * width:3 * width], seg, preferred_element_type=jnp.float32)
    )


def gram_columns(pairs):
    rows = []
    for left, right in pairs:
        for shift in range(VECS):
            moved = right if shift == 0 else pltpu.roll(right, shift * BLK, 1)
            rows.append(jnp.sum(left * moved, axis=0, keepdims=True))
    stacked = jnp.concatenate(rows, axis=0)
    width = stacked.shape[1]
    seg = (
        lax.broadcasted_iota(jnp.int32, (VECS, width), 1) // BLK
        == lax.broadcasted_iota(jnp.int32, (VECS, width), 0)
    ).astype(jnp.bfloat16)
    parts = split_three(stacked)
    dims = (((1,), (1,)), ((), ()))
    return sum(
        lax.dot_general(seg, parts[:, p * width:(p + 1) * width], dims, preferred_element_type=jnp.float32)
        for p in range(3)
    )


def coupling_kernel(with_gram, count_ref, lend_ref, jac_hbm, own_ref, g0_ref, g1_ref, g2_ref, g3_ref, cols_ref, *rest):
    if with_gram:
        anchor_ref, out_ref, gram_ref = rest[:3]
        rest = rest[3:]
    else:
        out_ref, l0_ref, l1_ref, l2_ref, l3_ref, kept_ref = rest[:6]
        rest = rest[6:]
    jac_ref, sems, source_ref, picked_ref, z_ref, parts_ref = rest
    tiles = jac_ref.shape[2] // LANES
    count = own_ref.shape[0]
    width = own_ref.shape[1]
    ghost = g0_ref.shape[0]
    chunks = sems.shape[0]
    chunk_rows = count // chunks

    def chunk_copy(b):
        rows = pl.ds(pl.multiple_of(b * chunk_rows, chunk_rows), chunk_rows)
        return pltpu.make_async_copy(jac_hbm.at[:, rows, :], jac_ref.at[:, rows, :], sems.at[b])

    for b in range(chunks):
        chunk_copy(b).start()

    living = lax.broadcasted_iota(jnp.int32, (count, 1), 0) < count_ref[0]
    source_ref[0:count] = split_three(jnp.where(living, own_ref[...], jnp.float32(0.0)))
    for q, piece in enumerate((g0_ref, g1_ref, g2_ref, g3_ref)):
        source_ref[count + q * ghost:count + (q + 1) * ghost] = split_three(piece[...])
    if with_gram:
        kept_early = jnp.where(living, own_ref[...], jnp.float32(0.0))
        early = gram_columns(((kept_early, anchor_ref[...]), (kept_early, kept_early)))
    slots = lax.broadcasted_iota(jnp.int32, (source_ref.shape[0], count), 0)
    for k in range(NB):
        chosen = (cols_ref[k:k + 1, :] == slots).astype(jnp.bfloat16)
        spread = lax.dot_general(
            chosen, source_ref[...], (((0,), (0,)), ((), ())), preferred_element_type=jnp.float32
        )
        picked_ref[k] = spread[:, 0:width] + spread[:, width:2 * width] + spread[:, 2 * width:3 * width]

    lane = lax.broadcasted_iota(jnp.int32, (SUBLANES, LANES), 1)

    def one_chunk(b, carry):
        chunk_copy(b).wait()
        for group in range(chunk_rows // SUBLANES):
            first_row = pl.multiple_of(b * chunk_rows + group * SUBLANES, SUBLANES)
            doubled = []
            for k in range(NB):
                per_vector = []
                for pair in range(VECS // 2):
                    tile = picked_ref[k, pl.ds(first_row, SUBLANES), pair * LANES:(pair + 1) * LANES]
                    swapped = pltpu.roll(tile, BLK, 1)
                    per_vector.append(jnp.where(lane < BLK, tile, swapped))
                    per_vector.append(jnp.where(lane >= BLK, tile, swapped))
                doubled.append(per_vector)

            def one_tile(t, inner):
                off = pl.multiple_of(t * LANES, LANES)
                blocks = [jac_ref[k, pl.ds(first_row, SUBLANES), pl.ds(off, LANES)] for k in range(NB)]
                for c in range(VECS):
                    terms = [blocks[k] * doubled[k][c] for k in range(NB)]
                    while len(terms) > 1:
                        terms = [terms[i] + terms[i + 1] for i in range(0, len(terms) - 1, 2)] + (
                            [terms[-1]] if len(terms) % 2 else []
                        )
                    z_ref[c, pl.ds(first_row, SUBLANES), pl.ds(off, LANES)] = terms[0]
                return inner

            lax.fori_loop(0, tiles, one_tile, 0, unroll=UNROLL)
        return carry

    lax.fori_loop(0, chunks, one_chunk, 0, unroll=True)

    full = tiles * LANES
    for c in range(VECS):
        total = z_ref[c]
        high = total.astype(jnp.bfloat16)
        parts_ref[2 * c] = high
        parts_ref[2 * c + 1] = (total - high.astype(jnp.float32)).astype(jnp.bfloat16)
    flat = parts_ref[...].reshape(2 * VECS * count, full)
    seg = (
        lax.broadcasted_iota(jnp.int32, (full, BLK), 0) // BLK
        == lax.broadcasted_iota(jnp.int32, (full, BLK), 1)
    ).astype(jnp.bfloat16)
    sums = jnp.dot(flat, seg, preferred_element_type=jnp.float32)
    coupled = jnp.concatenate(
        [sums[(2 * c) * count:(2 * c + 1) * count] + sums[(2 * c + 1) * count:(2 * c + 2) * count] for c in range(VECS)],
        axis=1,
    )
    own = own_ref[...]
    image = jnp.where(living, DIAG_SHIFT * own + coupled, jnp.float32(0.0))
    out_ref[...] = image
    kept = jnp.where(living, own, jnp.float32(0.0))
    if not with_gram:
        kept_ref[...] = kept
        for q, lent_ref in enumerate((l0_ref, l1_ref, l2_ref, l3_ref)):
            for j in range(lend_ref.shape[1]):
                lent_ref[j:j + 1, :] = out_ref[pl.ds(lend_ref[q, j], 1), :]
    else:
        anchor = anchor_ref[...]
        late = gram_columns(((image, anchor), (image, kept), (image, image)))
        partial = jnp.concatenate([early, late], axis=1)
        for target in range(gram_ref.shape[0]):
            gram_ref[target] = partial


def apply_operator(jac_t, own, ghost_rows, cols_t, counts, lend_rows, anchor=None, peers=1):
    blocks, count, full = jac_t.shape
    width = own.shape[1]
    ghost = ghost_rows[0].shape[0]
    chunks = max(count // CHUNK_ROWS, 1)
    with_gram = anchor is not None
    smem = pl.BlockSpec(memory_space=pltpu.SMEM)
    vmem = pl.BlockSpec(memory_space=pltpu.VMEM)
    lent = lend_rows.shape[1]
    in_specs = [smem, smem, pl.BlockSpec(memory_space=pl.ANY), vmem, vmem, vmem, vmem, vmem, vmem]
    out_shape = [jax.ShapeDtypeStruct((count, width), jnp.float32)]
    args = [counts, lend_rows, jac_t, own, *ghost_rows, cols_t]
    if with_gram:
        in_specs.append(vmem)
        args.append(anchor)
        out_shape.append(jax.ShapeDtypeStruct((peers, VECS, 5 * VECS), jnp.float32))
    else:
        out_shape += [jax.ShapeDtypeStruct((lent, width), jnp.float32)] * lend_rows.shape[0]
        out_shape += [jax.ShapeDtypeStruct((count, width), jnp.float32)]
    return pl.pallas_call(
        functools.partial(coupling_kernel, with_gram),
        out_shape=tuple(out_shape),
        in_specs=in_specs,
        out_specs=tuple(vmem for _ in out_shape),
        scratch_shapes=[
            pltpu.VMEM((blocks, count, full), jnp.float32),
            pltpu.SemaphoreType.DMA((chunks,)),
            pltpu.VMEM((count + 4 * ghost, 3 * width), jnp.bfloat16),
            pltpu.VMEM((blocks, count, width), jnp.float32),
            pltpu.VMEM((VECS, count, full), jnp.float32),
            pltpu.VMEM((2 * VECS, count, full), jnp.bfloat16),
        ],
        cost_estimate=pl.CostEstimate(
            flops=2 * blocks * count * full * VECS + 2 * 2 * VECS * count * full * BLK,
            bytes_accessed=4 * (blocks * count * full + 6 * count * width),
            transcendentals=0,
        ),
    )(*args)


def lending_kernel(lend_ref, values_ref, *lent_refs):
    for q, lent_ref in enumerate(lent_refs):
        for j in range(lend_ref.shape[1]):
            lent_ref[j:j + 1, :] = values_ref[pl.ds(lend_ref[q, j], 1), :]


def lent_rows_of(values, lend_rows):
    shape = jax.ShapeDtypeStruct((lend_rows.shape[1], values.shape[1]), values.dtype)
    whole = pl.BlockSpec(memory_space=pltpu.VMEM)
    return pl.pallas_call(
        lending_kernel,
        out_shape=(shape,) * lend_rows.shape[0],
        in_specs=[pl.BlockSpec(memory_space=pltpu.SMEM), whole],
        out_specs=(whole,) * lend_rows.shape[0],
    )(lend_rows, values)


def mixing_kernel(mix_ref, anchor_ref, first_ref, second_ref, correction_ref, residual_ref):
    width = anchor_ref.shape[1]
    segment = lax.broadcasted_iota(jnp.int32, (1, width), 1) // BLK

    def weights(row_offset, shift):
        out = jnp.zeros((1, width), jnp.float32)
        for d in range(VECS):
            out = jnp.where(segment == d, mix_ref[row_offset + (d - shift) % VECS, d], out)
        return out

    def mixed(values, row_offset):
        total = None
        for shift in range(VECS):
            moved = values if shift == 0 else pltpu.roll(values, shift * BLK, 1)
            term = moved * weights(row_offset, shift)
            total = term if total is None else total + term
        return total

    anchor = anchor_ref[...]
    first = first_ref[...]
    second = second_ref[...]
    correction_ref[...] = mixed(anchor, 0) + mixed(first, VECS)
    residual_ref[...] = anchor - (mixed(first, 0) + mixed(second, VECS))


def mix_outputs(coefficients, anchor, first, second):
    whole = pl.BlockSpec(memory_space=pltpu.VMEM)
    return pl.pallas_call(
        mixing_kernel,
        out_shape=(jax.ShapeDtypeStruct(anchor.shape, jnp.float32),) * 2,
        in_specs=[pl.BlockSpec(memory_space=pltpu.SMEM), whole, whole, whole],
        out_specs=(whole, whole),
    )(coefficients, anchor, first, second)


def per_device(start_block, jacobian, counts, columns, send_list):
    lend_rows = send_list[0]
    jac_t = jnp.transpose(jacobian, (1, 0, 2))

    def ghosts(outgoing):
        wide, narrow = lax.axis_size("wide"), lax.axis_size("narrow")
        return (
            lax.ppermute(outgoing[0], "wide", [(i, i + 1) for i in range(wide - 1)]),
            lax.ppermute(outgoing[1], "wide", [(i + 1, i) for i in range(wide - 1)]),
            lax.ppermute(outgoing[2], "narrow", [(i, i + 1) for i in range(narrow - 1)]),
            lax.ppermute(outgoing[3], "narrow", [(i + 1, i) for i in range(narrow - 1)]),
        )

    cols_t = jnp.transpose(columns, (1, 0))
    first = apply_operator(jac_t, start_block, ghosts(lent_rows_of(start_block, lend_rows)), cols_t, counts, lend_rows)
    first_image, first_lent, anchor = first[0], jnp.stack(first[1:5]), first[5]
    peers = lax.axis_size("wide") * lax.axis_size("narrow")
    second = apply_operator(jac_t, first_image, ghosts(first_lent), cols_t, counts, lend_rows, anchor, peers)
    second_image, raw_gram = second
    everyone = lax.all_to_all(raw_gram, ("wide", "narrow"), 0, 0, tiled=True)
    raw_gram = jnp.transpose(jnp.sum(everyone, axis=0), (1, 0)).reshape(5, VECS, VECS)
    shift = np.arange(VECS)[:, None, None]
    row_c = np.arange(VECS)[None, :, None]
    col_d = np.arange(VECS)[None, None, :]
    pick = jnp.asarray(((row_c - col_d) % VECS == shift).astype(np.float32))
    gram_parts = jnp.sum(raw_gram[:, :, :, None] * pick[None], axis=1)
    normal_matrix = jnp.concatenate(
        [
            jnp.concatenate([gram_parts[1], gram_parts[3].T], 1),
            jnp.concatenate([gram_parts[3], gram_parts[4]], 1),
        ],
        0,
    )
    right_terms = jnp.concatenate([gram_parts[0], gram_parts[2]], 0)
    factor = jnp.linalg.cholesky(normal_matrix)
    coefficients = jax.scipy.linalg.cho_solve((factor, True), right_terms)
    return mix_outputs(coefficients, anchor, first_image, second_image)


def solution(mesh):
    placed = (
        P(("wide", "narrow"), None),
        P(("wide", "narrow"), None, None),
        P(("wide", "narrow")),
        P(("wide", "narrow"), None),
        P(("wide", "narrow"), None, None),
    )
    return jax.shard_map(
        per_device,
        mesh=mesh,
        in_specs=placed,
        out_specs=(P(("wide", "narrow"), None), P(("wide", "narrow"), None)),
        check_vma=False,
    )
```

```python
import functools

import jax
import jax.numpy as jnp
import numpy as np
from jax import lax
from jax.experimental import pallas as pl
from jax.experimental.pallas import tpu as pltpu
from jax.sharding import PartitionSpec as P

BLK = 64
VECS = 4
NB = 5
E_DEV = 128
LANES = 128
SUBLANES = 8
UNROLL = 32
CHUNK_ROWS = 32
ROWS_PER_STEP = 32


DIAG_SHIFT = 1.5


def padded(cells, sides, width):
    for axis, dim in sides:
        count = lax.axis_size(axis)
        ends = count - 1
        head = lax.slice_in_dim(cells, 0, width, axis=dim)
        tail = lax.slice_in_dim(cells, cells.shape[dim] - width, cells.shape[dim], axis=dim)
        cells = jnp.concatenate(
            [
                lax.ppermute(tail, axis, [(i, (i + 1) % count) for i in range(ends)]),
                cells,
                lax.ppermute(head, axis, [((i + 1) % count, i) for i in range(ends)]),
            ],
            axis=dim,
        )
    return cells


def combine(values, mixing):
    shaped = values.reshape(values.shape[0], VECS, BLK)
    return jnp.einsum("eci,cd->edi", shaped, mixing, precision=lax.Precision.HIGHEST).reshape(
        values.shape[0], VECS * BLK
    )


def inner_block(left_side, right_side):
    left_shaped = left_side.reshape(left_side.shape[0], VECS, BLK)
    right_shaped = right_side.reshape(right_side.shape[0], VECS, BLK)
    return jnp.einsum("eci,edi->cd", left_shaped, right_shaped, precision=lax.Precision.HIGHEST)


def tree_sum(values, axes):
    for axis in axes:
        count = lax.axis_size(axis)
        if count & (count - 1):
            values = lax.psum(values, axis)
            continue
        stride = 1
        while stride < count:
            values = values + lax.ppermute(values, axis, [(i, i ^ stride) for i in range(count)])
            stride *= 2
    return values


def split_three(values):
    high = values.astype(jnp.bfloat16)
    rest = values - high.astype(jnp.float32)
    middle = rest.astype(jnp.bfloat16)
    low = (rest - middle.astype(jnp.float32)).astype(jnp.bfloat16)
    return jnp.concatenate([high, middle, low], axis=1)


def exchange_sum(values, axes):
    count = 1
    for axis in axes:
        count *= lax.axis_size(axis)
    flat = values.reshape(1, -1)
    everyone = lax.all_to_all(jnp.broadcast_to(flat, (count, flat.shape[1])), axes, 0, 0, tiled=True)
    return jnp.sum(everyone, axis=0).reshape(values.shape)


def segment_sums(values, segments):
    width = values.shape[1]
    seg = (
        lax.broadcasted_iota(jnp.int32, (width, segments), 0) // (width // segments)
        == lax.broadcasted_iota(jnp.int32, (width, segments), 1)
    ).astype(jnp.bfloat16)
    parts = split_three(values)
    return (
        jnp.dot(parts[:, 0:width], seg, preferred_element_type=jnp.float32)
        + jnp.dot(parts[:, width:2 * width], seg, preferred_element_type=jnp.float32)
        + jnp.dot(parts[:, 2 * width:3 * width], seg, preferred_element_type=jnp.float32)
    )


def gram_columns(pairs):
    rows = []
    for left, right in pairs:
        for shift in range(VECS):
            moved = right if shift == 0 else pltpu.roll(right, shift * BLK, 1)
            rows.append(jnp.sum(left * moved, axis=0, keepdims=True))
    stacked = jnp.concatenate(rows, axis=0)
    width = stacked.shape[1]
    seg = (
        lax.broadcasted_iota(jnp.int32, (VECS, width), 1) // BLK
        == lax.broadcasted_iota(jnp.int32, (VECS, width), 0)
    ).astype(jnp.bfloat16)
    parts = split_three(stacked)
    dims = (((1,), (1,)), ((), ()))
    return sum(
        lax.dot_general(seg, parts[:, p * width:(p + 1) * width], dims, preferred_element_type=jnp.float32)
        for p in range(3)
    )


def coupling_kernel(with_gram, count_ref, lend_ref, jac_hbm, own_ref, g0_ref, g1_ref, g2_ref, g3_ref, cols_ref, *rest):
    if with_gram:
        anchor_ref, out_ref, gram_ref = rest[:3]
        rest = rest[3:]
    else:
        out_ref, l0_ref, l1_ref, l2_ref, l3_ref, kept_ref = rest[:6]
        rest = rest[6:]
    jac_ref, sems, source_ref, picked_ref, z_ref, parts_ref = rest
    tiles = jac_ref.shape[2] // LANES
    count = own_ref.shape[0]
    width = own_ref.shape[1]
    ghost = g0_ref.shape[0]
    chunks = sems.shape[0]
    chunk_rows = count // chunks

    def chunk_copy(b):
        rows = pl.ds(pl.multiple_of(b * chunk_rows, chunk_rows), chunk_rows)
        return pltpu.make_async_copy(jac_hbm.at[:, rows, :], jac_ref.at[:, rows, :], sems.at[b])

    for b in range(chunks):
        chunk_copy(b).start()

    living = lax.broadcasted_iota(jnp.int32, (count, 1), 0) < count_ref[0]
    source_ref[0:count] = split_three(jnp.where(living, own_ref[...], jnp.float32(0.0)))
    for q, piece in enumerate((g0_ref, g1_ref, g2_ref, g3_ref)):
        source_ref[count + q * ghost:count + (q + 1) * ghost] = split_three(piece[...])
    slots = lax.broadcasted_iota(jnp.int32, (source_ref.shape[0], count), 0)
    for k in range(NB):
        chosen = (cols_ref[k:k + 1, :] == slots).astype(jnp.bfloat16)
        spread = lax.dot_general(
            chosen, source_ref[...], (((0,), (0,)), ((), ())), preferred_element_type=jnp.float32
        )
        picked_ref[k] = spread[:, 0:width] + spread[:, width:2 * width] + spread[:, 2 * width:3 * width]

    lane = lax.broadcasted_iota(jnp.int32, (SUBLANES, LANES), 1)

    def one_chunk(b, carry):
        chunk_copy(b).wait()
        for group in range(chunk_rows // SUBLANES):
            first_row = pl.multiple_of(b * chunk_rows + group * SUBLANES, SUBLANES)
            doubled = []
            for k in range(NB):
                per_vector = []
                for pair in range(VECS // 2):
                    tile = picked_ref[k, pl.ds(first_row, SUBLANES), pair * LANES:(pair + 1) * LANES]
                    swapped = pltpu.roll(tile, BLK, 1)
                    per_vector.append(jnp.where(lane < BLK, tile, swapped))
                    per_vector.append(jnp.where(lane >= BLK, tile, swapped))
                doubled.append(per_vector)

            def one_tile(t, inner):
                off = pl.multiple_of(t * LANES, LANES)
                blocks = [jac_ref[k, pl.ds(first_row, SUBLANES), pl.ds(off, LANES)] for k in range(NB)]
                for c in range(VECS):
                    terms = [blocks[k] * doubled[k][c] for k in range(NB)]
                    while len(terms) > 1:
                        terms = [terms[i] + terms[i + 1] for i in range(0, len(terms) - 1, 2)] + (
                            [terms[-1]] if len(terms) % 2 else []
                        )
                    z_ref[c, pl.ds(first_row, SUBLANES), pl.ds(off, LANES)] = terms[0]
                return inner

            lax.fori_loop(0, tiles, one_tile, 0, unroll=UNROLL)
        return carry

    lax.fori_loop(0, chunks, one_chunk, 0, unroll=True)

    full = tiles * LANES
    for c in range(VECS):
        total = z_ref[c]
        high = total.astype(jnp.bfloat16)
        parts_ref[2 * c] = high
        parts_ref[2 * c + 1] = (total - high.astype(jnp.float32)).astype(jnp.bfloat16)
    flat = parts_ref[...].reshape(2 * VECS * count, full)
    seg = (
        lax.broadcasted_iota(jnp.int32, (full, BLK), 0) // BLK
        == lax.broadcasted_iota(jnp.int32, (full, BLK), 1)
    ).astype(jnp.bfloat16)
    sums = jnp.dot(flat, seg, preferred_element_type=jnp.float32)
    coupled = jnp.concatenate(
        [sums[(2 * c) * count:(2 * c + 1) * count] + sums[(2 * c + 1) * count:(2 * c + 2) * count] for c in range(VECS)],
        axis=1,
    )
    own = own_ref[...]
    image = jnp.where(living, DIAG_SHIFT * own + coupled, jnp.float32(0.0))
    out_ref[...] = image
    kept = jnp.where(living, own, jnp.float32(0.0))
    if not with_gram:
        kept_ref[...] = kept
        for q, lent_ref in enumerate((l0_ref, l1_ref, l2_ref, l3_ref)):
            for j in range(lend_ref.shape[1]):
                lent_ref[j:j + 1, :] = out_ref[pl.ds(lend_ref[q, j], 1), :]
    else:
        anchor = anchor_ref[...]
        partial = gram_columns(((kept, anchor), (kept, kept), (image, anchor), (image, kept), (image, image)))
        for target in range(gram_ref.shape[0]):
            gram_ref[target] = partial


def apply_operator(jac_t, own, ghost_rows, cols_t, counts, lend_rows, anchor=None, peers=1):
    blocks, count, full = jac_t.shape
    width = own.shape[1]
    ghost = ghost_rows[0].shape[0]
    chunks = max(count // CHUNK_ROWS, 1)
    with_gram = anchor is not None
    smem = pl.BlockSpec(memory_space=pltpu.SMEM)
    vmem = pl.BlockSpec(memory_space=pltpu.VMEM)
    lent = lend_rows.shape[1]
    in_specs = [smem, smem, pl.BlockSpec(memory_space=pl.ANY), vmem, vmem, vmem, vmem, vmem, vmem]
    out_shape = [jax.ShapeDtypeStruct((count, width), jnp.float32)]
    args = [counts, lend_rows, jac_t, own, *ghost_rows, cols_t]
    if with_gram:
        in_specs.append(vmem)
        args.append(anchor)
        out_shape.append(jax.ShapeDtypeStruct((peers, VECS, 5 * VECS), jnp.float32))
    else:
        out_shape += [jax.ShapeDtypeStruct((lent, width), jnp.float32)] * lend_rows.shape[0]
        out_shape += [jax.ShapeDtypeStruct((count, width), jnp.float32)]
    return pl.pallas_call(
        functools.partial(coupling_kernel, with_gram),
        out_shape=tuple(out_shape),
        in_specs=in_specs,
        out_specs=tuple(vmem for _ in out_shape),
        scratch_shapes=[
            pltpu.VMEM((blocks, count, full), jnp.float32),
            pltpu.SemaphoreType.DMA((chunks,)),
            pltpu.VMEM((count + 4 * ghost, 3 * width), jnp.bfloat16),
            pltpu.VMEM((blocks, count, width), jnp.float32),
            pltpu.VMEM((VECS, count, full), jnp.float32),
            pltpu.VMEM((2 * VECS, count, full), jnp.bfloat16),
        ],
        cost_estimate=pl.CostEstimate(
            flops=2 * blocks * count * full * VECS + 2 * 2 * VECS * count * full * BLK,
            bytes_accessed=4 * (blocks * count * full + 6 * count * width),
            transcendentals=0,
        ),
    )(*args)


def lending_kernel(lend_ref, values_ref, *lent_refs):
    for q, lent_ref in enumerate(lent_refs):
        for j in range(lend_ref.shape[1]):
            lent_ref[j:j + 1, :] = values_ref[pl.ds(lend_ref[q, j], 1), :]


def lent_rows_of(values, lend_rows):
    shape = jax.ShapeDtypeStruct((lend_rows.shape[1], values.shape[1]), values.dtype)
    whole = pl.BlockSpec(memory_space=pltpu.VMEM)
    return pl.pallas_call(
        lending_kernel,
        out_shape=(shape,) * lend_rows.shape[0],
        in_specs=[pl.BlockSpec(memory_space=pltpu.SMEM), whole],
        out_specs=(whole,) * lend_rows.shape[0],
    )(lend_rows, values)


def mixing_kernel(mix_ref, anchor_ref, first_ref, second_ref, correction_ref, residual_ref):
    width = anchor_ref.shape[1]
    segment = lax.broadcasted_iota(jnp.int32, (1, width), 1) // BLK

    def weights(row_offset, shift):
        out = jnp.zeros((1, width), jnp.float32)
        for d in range(VECS):
            out = jnp.where(segment == d, mix_ref[row_offset + (d - shift) % VECS, d], out)
        return out

    def mixed(values, row_offset):
        total = None
        for shift in range(VECS):
            moved = values if shift == 0 else pltpu.roll(values, shift * BLK, 1)
            term = moved * weights(row_offset, shift)
            total = term if total is None else total + term
        return total

    anchor = anchor_ref[...]
    first = first_ref[...]
    second = second_ref[...]
    correction_ref[...] = mixed(anchor, 0) + mixed(first, VECS)
    residual_ref[...] = anchor - (mixed(first, 0) + mixed(second, VECS))


def mix_outputs(coefficients, anchor, first, second):
    whole = pl.BlockSpec(memory_space=pltpu.VMEM)
    return pl.pallas_call(
        mixing_kernel,
        out_shape=(jax.ShapeDtypeStruct(anchor.shape, jnp.float32),) * 2,
        in_specs=[pl.BlockSpec(memory_space=pltpu.SMEM), whole, whole, whole],
        out_specs=(whole, whole),
    )(coefficients, anchor, first, second)


def per_device(start_block, jacobian, counts, columns, send_list):
    lend_rows = send_list[0]
    jac_t = jnp.transpose(jacobian, (1, 0, 2))

    def ghosts(outgoing):
        wide, narrow = lax.axis_size("wide"), lax.axis_size("narrow")
        return (
            lax.ppermute(outgoing[0], "wide", [(i, i + 1) for i in range(wide - 1)]),
            lax.ppermute(outgoing[1], "wide", [(i + 1, i) for i in range(wide - 1)]),
            lax.ppermute(outgoing[2], "narrow", [(i, i + 1) for i in range(narrow - 1)]),
            lax.ppermute(outgoing[3], "narrow", [(i + 1, i) for i in range(narrow - 1)]),
        )

    cols_t = jnp.transpose(columns, (1, 0))
    first = apply_operator(jac_t, start_block, ghosts(lent_rows_of(start_block, lend_rows)), cols_t, counts, lend_rows)
    first_image, first_lent, anchor = first[0], jnp.stack(first[1:5]), first[5]
    peers = lax.axis_size("wide") * lax.axis_size("narrow")
    second = apply_operator(jac_t, first_image, ghosts(first_lent), cols_t, counts, lend_rows, anchor, peers)
    second_image, raw_gram = second
    everyone = lax.all_to_all(raw_gram, ("wide", "narrow"), 0, 0, tiled=True)
    raw_gram = jnp.transpose(jnp.sum(everyone, axis=0), (1, 0)).reshape(5, VECS, VECS)
    shift = np.arange(VECS)[:, None, None]
    row_c = np.arange(VECS)[None, :, None]
    col_d = np.arange(VECS)[None, None, :]
    pick = jnp.asarray(((row_c - col_d) % VECS == shift).astype(np.float32))
    gram_parts = jnp.sum(raw_gram[:, :, :, None] * pick[None], axis=1)
    normal_matrix = jnp.concatenate(
        [
            jnp.concatenate([gram_parts[1], gram_parts[3].T], 1),
            jnp.concatenate([gram_parts[3], gram_parts[4]], 1),
        ],
        0,
    )
    right_terms = jnp.concatenate([gram_parts[0], gram_parts[2]], 0)
    factor = jnp.linalg.cholesky(normal_matrix)
    coefficients = jax.scipy.linalg.cho_solve((factor, True), right_terms)
    return mix_outputs(coefficients, anchor, first_image, second_image)


def solution(mesh):
    placed = (
        P(("wide", "narrow"), None),
        P(("wide", "narrow"), None, None),
        P(("wide", "narrow")),
        P(("wide", "narrow"), None),
        P(("wide", "narrow"), None, None),
    )
    return jax.shard_map(
        per_device,
        mesh=mesh,
        in_specs=placed,
        out_specs=(P(("wide", "narrow"), None), P(("wide", "narrow"), None)),
        check_vma=False,
    )
```
